128 devices in a mesh: band: 32 (over z, x, core), seg: 4 (over y).
Axes of the slice: x: 4, y: 4, z: 4, core: 2. Of those that a mesh axis runs over, the one named last changes fastest.
Arguments:
- voltages: float32 [4, 1, 2, 2, 1024, 3072], P('seg', None, None, None, 'band'), may hold values from -6 to 6
- chirp_phase: float32 [1, 1024, 4096], P(None, 'seg', 'band'), may hold values from -3.140625 to 3.140625
Outputs:
- dedispersed: float32 [4, 1, 2, 2, 1024, 3072], P('seg', None, None, None, 'band')
The draws below stay inside these ranges and needn't reach their ends.
All inputs are finite; a program needn't handle non-finite values.
Results may differ from the reference program's by a relative error of at most 0.00015.
Values sent between devices are 32-bit elements; how exact they have to be, the bound alone decides.
No kernel may reach another device: no remote copies, remote signals or barrier semaphores. Data moves between devices by JAX's collectives and lax.ppermute only.
A program may use at most 64 MiB of HBM per device.

```python
import jax
import jax.numpy as jnp
from jax import lax

SUB = 1
COLS = 4096
ROWS = 1024
VALID_COLS = 3072
LENGTH = 4194304
SEGS = 4


def steps_of(rng, extent, pieces, least, largest):
    gain = 1.0
    for position, blocks in pieces:
        steps = jax.random.uniform(jax.random.fold_in(jax.random.fold_in(rng, 6), position), (blocks,), jnp.float32, least / len(pieces), largest / len(pieces))
        gain = gain * jnp.repeat(jnp.exp(steps), extent[position] // blocks).reshape((-1,) + (1,) * (len(extent) - 1 - position))
    return gain


def scatter_about(rng, shape, width, bound, split=(), held_as=jnp.bfloat16):
    entries = jax.random.normal(rng, shape, jnp.float32) * width
    if len(split) > 0:
        entries = steps_of(rng, shape, split, -0.22, 0.18) * entries
    return jnp.clip(entries, min=-bound, max=bound).astype(held_as)


def setup_inputs(seed: int = 0) -> dict:
    splits = jax.random.split(jax.random.key(seed), 3)
    return {
        "voltages": scatter_about(splits[0], (SEGS, SUB, 2, 2, ROWS, VALID_COLS), 1.0, 6.0, ((0, 4), (4, 32)), jnp.float32),
        "chirp_phase": jnp.clip(jax.random.uniform(splits[1], (SUB, ROWS, COLS), jnp.float32, -3.140625, 3.140625), -3.140625, 3.140625),
    }


def reference(voltages, chirp_phase):
    lead_in = ROWS * COLS // 4
    valid = ROWS * VALID_COLS
    series = lax.complex(voltages[:, :, :, 0], voltages[:, :, :, 1])
    series = jnp.swapaxes(series, -1, -2).reshape(SEGS, SUB, 2, valid)
    series = jnp.moveaxis(series, 0, 2).reshape(SUB, 2, SEGS * valid)
    padded = jnp.concatenate([jnp.zeros((SUB, 2, lead_in), dtype=series.dtype), series], axis=-1)
    chirp = lax.complex(jnp.cos(chirp_phase), jnp.sin(chirp_phase)).reshape(SUB, 1, LENGTH)
    results = []
    for segment in range(SEGS):
        buffer = padded[:, :, segment * valid: segment * valid + LENGTH]
        spectrum = jnp.fft.fft(buffer, axis=-1) * chirp
        restored = jnp.fft.ifft(spectrum, axis=-1)[:, :, lead_in:]
        restored = jnp.swapaxes(restored.reshape(SUB, 2, VALID_COLS, ROWS), -1, -2)
        results.append(jnp.stack([jnp.real(restored), jnp.imag(restored)], axis=2))
    return jnp.stack(results, axis=0).astype(jnp.float32)
```

```python
import math

import jax
import jax.numpy as jnp
from jax import lax
from jax.sharding import PartitionSpec as P


def passed_along(block, axis, distance):
    devices = range(lax.axis_size(axis))
    route = [(i - distance, i) for i in devices if i - distance in devices]
    return lax.ppermute(block, axis, route)


def gathered(block, axis, dim):
    size = lax.axis_size(axis)
    pieces = [block]
    for shift in range(1, size):
        route = [((i + shift) % size, i) for i in range(size)]
        pieces.append(lax.ppermute(block, axis, route))
    ahead = jnp.stack(pieces, axis=0)
    ordered = jnp.roll(ahead, lax.axis_index(axis), axis=0)
    ordered = jnp.moveaxis(ordered, 0, dim)
    shape = list(block.shape)
    shape[dim] *= size
    return ordered.reshape(shape)


def split_factor(length):
    factor = int(math.isqrt(length))
    while length % factor:
        factor -= 1
    return factor


def tables(length, direction):
    places = jnp.arange(length, dtype=jnp.int32)
    product = places[:, None] * places[None, :] % length
    angles = direction * 2.0 * math.pi / length * product.astype(jnp.float32)
    return (jnp.cos(angles), jnp.sin(angles))


def rotate(real_part, imag_part, product, scale):
    angles = scale * product.astype(jnp.float32)
    cosine = jnp.cos(angles)
    sine = jnp.sin(angles)
    return (real_part * cosine - imag_part * sine, real_part * sine + imag_part * cosine)


def transform_last(real_part, imag_part, direction):
    length = real_part.shape[-1]
    inner = split_factor(length)
    outer = length // inner
    leading = real_part.shape[:-1]
    real_part = real_part.reshape(leading + (outer, inner))
    imag_part = imag_part.reshape(leading + (outer, inner))
    cos_outer, sin_outer = tables(outer, direction)
    highest = lax.Precision.HIGHEST
    first_real = jnp.einsum(
        "...nj,nk->...kj", real_part, cos_outer, precision=highest
    ) - jnp.einsum("...nj,nk->...kj", imag_part, sin_outer, precision=highest)
    first_imag = jnp.einsum(
        "...nj,nk->...kj", real_part, sin_outer, precision=highest
    ) + jnp.einsum("...nj,nk->...kj", imag_part, cos_outer, precision=highest)
    outer_index = jnp.arange(outer, dtype=jnp.int32)[:, None]
    inner_index = jnp.arange(inner, dtype=jnp.int32)[None, :]
    first_real, first_imag = rotate(
        first_real,
        first_imag,
        outer_index * inner_index % length,
        direction * 2.0 * math.pi / length,
    )
    cos_inner, sin_inner = tables(inner, direction)
    last_real = jnp.matmul(first_real, cos_inner, precision=highest) - jnp.matmul(
        first_imag, sin_inner, precision=highest
    )
    last_imag = jnp.matmul(first_real, sin_inner, precision=highest) + jnp.matmul(
        first_imag, cos_inner, precision=highest
    )
    last_real = jnp.swapaxes(last_real, -1, -2).reshape(leading + (length,))
    last_imag = jnp.swapaxes(last_imag, -1, -2).reshape(leading + (length,))
    return (last_real, last_imag)


def transform_rows(real_part, imag_part, direction):
    result_real, result_imag = transform_last(
        jnp.swapaxes(real_part, -1, -2), jnp.swapaxes(imag_part, -1, -2), direction
    )
    return (jnp.swapaxes(result_real, -1, -2), jnp.swapaxes(result_imag, -1, -2))


def row_pass(spread):
    result_real, result_imag = transform_rows(spread[:, :, 0], spread[:, :, 1], -1.0)
    return jnp.stack([result_real, result_imag], axis=2)


def column_pass(gathered):
    cols = gathered.shape[-1]
    length_scale = 1.0 / (gathered.shape[-2] * lax.axis_size("band") * cols)
    result_real, result_imag = transform_last(gathered[:, :, 0], gathered[:, :, 1], 1.0)
    result = jnp.stack([result_real * length_scale, result_imag * length_scale], axis=2)
    return result[..., cols // 4 :]


def per_device(voltages, chirp_phase):
    block = voltages[0]
    rows_dev = block.shape[3]
    valid_cols = block.shape[4]
    cols = valid_cols * 4 // 3
    bands = lax.axis_size("band")
    rows = rows_dev * bands
    length = rows * cols
    width = cols // bands
    tail = block[..., valid_cols - cols // 4 :]
    history = passed_along(tail, "seg", 1)
    buffer = jnp.concatenate([history, block], axis=-1)
    real_part, imag_part = transform_last(buffer[:, :, 0], buffer[:, :, 1], -1.0)
    row_index = lax.axis_index("band") * rows_dev + jnp.arange(rows_dev, dtype=jnp.int32)
    col_index = jnp.arange(cols, dtype=jnp.int32)
    real_part, imag_part = rotate(
        real_part,
        imag_part,
        row_index[:, None] * col_index[None, :] % length,
        -2.0 * math.pi / length,
    )
    stacked = jnp.stack([real_part, imag_part], axis=2)
    spectra = row_pass(lax.all_to_all(stacked, "band", split_axis=4, concat_axis=3, tiled=True))
    real_part, imag_part = (spectra[:, :, 0], spectra[:, :, 1])
    phases = gathered(chirp_phase, "seg", 1)
    cosine = jnp.cos(phases)[:, None]
    sine = jnp.sin(phases)[:, None]
    real_part, imag_part = (
        real_part * cosine - imag_part * sine,
        real_part * sine + imag_part * cosine,
    )
    real_part, imag_part = transform_rows(real_part, imag_part, 1.0)
    full_rows = jnp.arange(rows, dtype=jnp.int32)
    own_cols = lax.axis_index("band") * width + jnp.arange(width, dtype=jnp.int32)
    real_part, imag_part = rotate(
        real_part,
        imag_part,
        full_rows[:, None] * own_cols[None, :] % length,
        2.0 * math.pi / length,
    )
    columns = jnp.stack([real_part, imag_part], axis=2)
    result = column_pass(lax.all_to_all(columns, "band", split_axis=3, concat_axis=4, tiled=True))
    return result[None]


def solution(mesh):
    in_specs = (P("seg", None, None, None, "band", None), P(None, "seg", "band"))
    out_specs = P("seg", None, None, None, "band", None)
    return jax.shard_map(
        per_device, mesh=mesh, in_specs=in_specs, out_specs=out_specs, check_vma=False
    )
```

```python
import math

import numpy as np
import jax
import jax.numpy as jnp
from jax import lax
from jax.experimental import pallas as pl
from jax.experimental.pallas import tpu as pltpu
from jax.sharding import PartitionSpec as P

INTERPRET = False
HIGHEST = lax.Precision.HIGHEST
F32 = jnp.float32
ROWS_DEV = 32
COLS = 4096
HIST = 1024
LENGTH = 1024 * 4096


def passed_along(block, axis, distance):
    devices = range(lax.axis_size(axis))
    route = [(i - distance, i) for i in devices if i - distance in devices]
    return lax.ppermute(block, axis, route)


def gathered(block, axis, dim):
    size = lax.axis_size(axis)
    pieces = [block]
    for shift in range(1, size):
        route = [((i + shift) % size, i) for i in range(size)]
        pieces.append(lax.ppermute(block, axis, route))
    ahead = jnp.stack(pieces, axis=0)
    ordered = jnp.roll(ahead, lax.axis_index(axis), axis=0)
    ordered = jnp.moveaxis(ordered, 0, dim)
    shape = list(block.shape)
    shape[dim] *= size
    return ordered.reshape(shape)


def fft_list(xr, xi, sign):
    n = len(xr)
    if n == 1:
        return list(xr), list(xi)
    er, ei = fft_list(xr[0::2], xi[0::2], sign)
    odd_r, odd_i = fft_list(xr[1::2], xi[1::2], sign)
    half = n // 2
    outr = [None] * n
    outi = [None] * n
    for k in range(half):
        a, b = odd_r[k], odd_i[k]
        if k == 0:
            tr, ti = a, b
        elif 4 * k == n:
            tr, ti = (-b, a) if sign > 0 else (b, -a)
        else:
            angle = sign * 2.0 * math.pi * k / n
            c, s = math.cos(angle), math.sin(angle)
            tr = a * c - b * s
            ti = a * s + b * c
        outr[k] = er[k] + tr
        outi[k] = ei[k] + ti
        outr[k + half] = er[k] - tr
        outi[k + half] = ei[k] - ti
    return outr, outi


def unit(m, n, sign):
    angle = (m % n).astype(F32) * F32(sign * 2.0 * math.pi / n)
    return jnp.cos(angle), jnp.sin(angle)


def send_matrices():
    row = np.arange(256)
    dd, pp, ks = row // 8, (row // 4) % 2, row % 4
    k2 = 4 * dd + ks
    col = np.arange(512)
    pin, riin, lane = col // 256, (col // 128) % 2, col % 128
    ang = -2.0 * np.pi * np.outer(k2, lane) / 128.0
    c, s = np.cos(ang), np.sin(ang)
    same = (pp[:, None] == pin[None, :])
    real = np.where(riin[None, :] == 0, c, -s) * same
    imag = np.where(riin[None, :] == 0, s, c) * same
    return real.astype(np.float32), imag.astype(np.float32)


def row_block(sign):
    idx = np.arange(128)
    q, r = idx // 32, idx % 32
    ang = sign * 2.0 * np.pi * np.outer(r, r) / 32.0
    same = q[:, None] == q[None, :]
    wr = np.cos(ang) * same
    wi = np.sin(ang) * same
    top = np.concatenate([wr, wi], axis=1)
    bottom = np.concatenate([-wi, wr], axis=1)
    return np.concatenate([top, bottom], axis=0).astype(np.float32)


def row_twiddle(sign):
    g = np.arange(32)[:, None]
    r = (np.arange(1024) % 32)[None, :]
    ang = sign * 2.0 * np.pi * (g * r) / 1024.0
    return np.cos(ang).astype(np.float32), np.sin(ang).astype(np.float32)


def receive_matrix():
    row = np.arange(512)
    riin, dd, pp, ks = row // 256, (row // 8) % 32, (row // 4) % 2, row % 4
    k2 = 4 * dd + ks
    col = np.arange(512)
    pout, riout, lc = col // 256, (col // 128) % 2, col % 128
    ang = 2.0 * np.pi * np.outer(k2, lc) / 128.0
    c, s = np.cos(ang), np.sin(ang)
    same = pp[:, None] == pout[None, :]
    val = np.where(riin[:, None] == 0,
                   np.where(riout[None, :] == 0, c, s),
                   np.where(riout[None, :] == 0, -s, c))
    return (val * same / LENGTH).astype(np.float32)


def column_twiddle():
    ka = np.arange(32)[:, None]
    lc = (np.arange(256) % 128)[None, :]
    ang = 2.0 * np.pi * (ka * lc) / 4096.0
    return np.cos(ang).astype(np.float32), np.sin(ang).astype(np.float32)


def column_forward_kernel(blk_ref, hist_ref, pre_c, pre_s, lr_ref, li_ref, post_c, post_s, out_ref, xs_ref):
    for p in range(2):
        xr, xi = [], []
        for t in range(32):
            if t < 8:
                xr.append(hist_ref[p, 0, :, t * 128:(t + 1) * 128])
                xi.append(hist_ref[p, 1, :, t * 128:(t + 1) * 128])
            else:
                xr.append(blk_ref[p, 0, :, (t - 8) * 128:(t - 7) * 128])
                xi.append(blk_ref[p, 1, :, (t - 8) * 128:(t - 7) * 128])
        ar, ai = fft_list(xr, xi, -1)
        for k in range(32):
            c = pre_c[k * 32:(k + 1) * 32, :]
            s = pre_s[k * 32:(k + 1) * 32, :]
            xs_ref[k * 32:(k + 1) * 32, p * 256:p * 256 + 128] = ar[k] * c - ai[k] * s
            xs_ref[k * 32:(k + 1) * 32, p * 256 + 128:p * 256 + 256] = ar[k] * s + ai[k] * c
    x = xs_ref[...]
    dims = (((1,), (1,)), ((), ()))
    ore = lax.dot_general(lr_ref[...], x, dims, precision=HIGHEST, preferred_element_type=F32)
    oim = lax.dot_general(li_ref[...], x, dims, precision=HIGHEST, preferred_element_type=F32)
    c = post_c[...]
    s = post_s[...]
    out_ref[:, 0:1024] = ore * c - oim * s
    out_ref[:, 1024:2048] = ore * s + oim * c


def row_kernel(x_ref, twc_ref, tws_ref, bf_ref, bb_ref, chc_ref, chs_ref, post_c, post_s, out_ref, y_ref, w_ref):
    er = [x_ref[8 * d:8 * d + 8, 0:1024] for d in range(32)]
    ei = [x_ref[8 * d:8 * d + 8, 1024:2048] for d in range(32)]
    fr, fi = fft_list(er, ei, -1)
    for g in range(32):
        c = twc_ref[g:g + 1, :]
        s = tws_ref[g:g + 1, :]
        a = fr[g] * c - fi[g] * s
        b = fr[g] * s + fi[g] * c
        for j in range(8):
            y_ref[256 * j + 8 * g:256 * j + 8 * g + 8, 0:128] = a[:, 128 * j:128 * (j + 1)]
            y_ref[256 * j + 8 * g:256 * j + 8 * g + 8, 128:256] = b[:, 128 * j:128 * (j + 1)]
    z = jnp.dot(y_ref[...], bf_ref[...], precision=HIGHEST, preferred_element_type=F32)
    zr = z[:, 0:128]
    zi = z[:, 128:256]
    c = chc_ref[...]
    s = chs_ref[...]
    y_ref[:, 0:128] = zr * c - zi * s
    y_ref[:, 128:256] = zr * s + zi * c
    w_ref[...] = jnp.dot(y_ref[...], bb_ref[...], precision=HIGHEST, preferred_element_type=F32)
    gr, gi = [], []
    for g in range(32):
        a = jnp.concatenate([w_ref[256 * j + 8 * g:256 * j + 8 * g + 8, 0:128] for j in range(8)], axis=1)
        b = jnp.concatenate([w_ref[256 * j + 8 * g:256 * j + 8 * g + 8, 128:256] for j in range(8)], axis=1)
        c = twc_ref[g:g + 1, :]
        s = -tws_ref[g:g + 1, :]
        gr.append(a * c - b * s)
        gi.append(a * s + b * c)
    ur, ui = fft_list(gr, gi, 1)
    for d in range(32):
        c = post_c[8 * d:8 * d + 8, :]
        s = post_s[8 * d:8 * d + 8, :]
        out_ref[8 * d:8 * d + 8, 0:1024] = ur[d] * c - ui[d] * s
        out_ref[8 * d:8 * d + 8, 1024:2048] = ur[d] * s + ui[d] * c


def column_inverse_kernel(x_ref, m_ref, twc_ref, tws_ref, out_ref, s_ref):
    lhs = jnp.concatenate([x_ref[:, 0:1024].T, x_ref[:, 1024:2048].T], axis=1)
    s_ref[...] = jnp.dot(lhs, m_ref[...], precision=HIGHEST, preferred_element_type=F32)
    er, ei = [], []
    for k in range(32):
        rows = slice(32 * k, 32 * (k + 1))
        a = jnp.concatenate([s_ref[rows, 0:128], s_ref[rows, 256:384]], axis=1)
        b = jnp.concatenate([s_ref[rows, 128:256], s_ref[rows, 384:512]], axis=1)
        c = twc_ref[k:k + 1, :]
        s = tws_ref[k:k + 1, :]
        er.append(a * c - b * s)
        ei.append(a * s + b * c)
    tr, ti = fft_list(er, ei, 1)
    for t in range(8, 32):
        for p in range(2):
            out_ref[p, 0, :, (t - 8) * 128:(t - 7) * 128] = tr[t][:, 128 * p:128 * (p + 1)]
            out_ref[p, 1, :, (t - 8) * 128:(t - 7) * 128] = ti[t][:, 128 * p:128 * (p + 1)]


def call(kernel, out_shape, scratch, *args):
    return pl.pallas_call(
        kernel,
        out_shape=jax.ShapeDtypeStruct(out_shape, F32),
        scratch_shapes=[pltpu.VMEM(s, F32) for s in scratch],
        interpret=INTERPRET,
    )(*args)


def per_device(voltages, chirp_phase):
    block = voltages[0, 0]
    band = lax.axis_index("band")
    history = passed_along(block[..., 3072 - HIST:], "seg", 1)
    phases = gathered(chirp_phase, "seg", 1)[0]

    ka = jnp.arange(1024, dtype=jnp.int32)[:, None] // 32
    rl = jnp.arange(1024, dtype=jnp.int32)[:, None] % 32
    lane = jnp.arange(128, dtype=jnp.int32)[None, :]
    pre_c, pre_s = unit(ka * (1024 * lane + 32 * band + rl), LENGTH, -1)
    row = jnp.arange(256, dtype=jnp.int32)[:, None]
    k2 = 4 * (row // 8) + row % 4
    r_lane = jnp.arange(1024, dtype=jnp.int32)[None, :] % 32
    ka_lane = jnp.arange(1024, dtype=jnp.int32)[None, :] // 32
    post_c, post_s = unit(32 * (32 * band + r_lane) * k2, LENGTH, -1)
    back_c, back_s = unit((32 * (row // 8) + r_lane) * (128 * band + ka_lane + 32 * (row % 4)), LENGTH, 1)

    chirp = phases.reshape(32, 32, 4, 8, 4).transpose(3, 1, 2, 4, 0)
    chirp = jnp.broadcast_to(chirp[:, :, None], (8, 32, 2, 4, 4, 32)).reshape(2048, 128)
    ch_c, ch_s = jnp.cos(chirp), jnp.sin(chirp)

    lr, li = send_matrices()
    send = call(column_forward_kernel, (256, 2048), [(1024, 512)],
                block, history, pre_c, pre_s, jnp.asarray(lr), jnp.asarray(li), post_c, post_s)
    received = lax.all_to_all(send.reshape(32, 8, 2048), "band", 0, 0, tiled=True).reshape(256, 2048)

    twc, tws = row_twiddle(-1)
    sent = call(row_kernel, (256, 2048), [(2048, 256), (2048, 256)],
                received, jnp.asarray(twc), jnp.asarray(tws), jnp.asarray(row_block(-1)),
                jnp.asarray(row_block(1)), ch_c, ch_s, back_c, back_s)
    returned = lax.all_to_all(sent.reshape(32, 8, 2048), "band", 0, 0, tiled=True).reshape(256, 2048)

    cc, cs = column_twiddle()
    out = call(column_inverse_kernel, (2, 2, ROWS_DEV, 3072), [(1024, 512)],
               returned, jnp.asarray(receive_matrix()), jnp.asarray(cc), jnp.asarray(cs))
    return out[None, None]


def solution(mesh):
    in_specs = (P("seg", None, None, None, "band", None), P(None, "seg", "band"))
    out_specs = P("seg", None, None, None, "band", None)
    return jax.shard_map(
        per_device, mesh=mesh, in_specs=in_specs, out_specs=out_specs, check_vma=False
    )
```

```python
import math

import numpy as np
import jax
import jax.numpy as jnp
from jax import lax
from jax.experimental import pallas as pl
from jax.experimental.pallas import tpu as pltpu
from jax.sharding import PartitionSpec as P

INTERPRET = False
HIGHEST = lax.Precision.HIGHEST
F32 = jnp.float32
ROWS_DEV = 32
COLS = 4096
HIST = 1024
LENGTH = 1024 * 4096


def passed_along(block, axis, distance):
    devices = range(lax.axis_size(axis))
    route = [(i - distance, i) for i in devices if i - distance in devices]
    return lax.ppermute(block, axis, route)


def gathered(block, axis, dim):
    size = lax.axis_size(axis)
    pieces = [block]
    for shift in range(1, size):
        route = [((i + shift) % size, i) for i in range(size)]
        pieces.append(lax.ppermute(block, axis, route))
    ahead = jnp.stack(pieces, axis=0)
    ordered = jnp.roll(ahead, lax.axis_index(axis), axis=0)
    ordered = jnp.moveaxis(ordered, 0, dim)
    shape = list(block.shape)
    shape[dim] *= size
    return ordered.reshape(shape)


def fft_list(xr, xi, sign):
    n = len(xr)
    if n == 1:
        return list(xr), list(xi)
    er, ei = fft_list(xr[0::2], xi[0::2], sign)
    odd_r, odd_i = fft_list(xr[1::2], xi[1::2], sign)
    half = n // 2
    outr = [None] * n
    outi = [None] * n
    for k in range(half):
        a, b = odd_r[k], odd_i[k]
        if k == 0:
            tr, ti = a, b
        elif 4 * k == n:
            tr, ti = (-b, a) if sign > 0 else (b, -a)
        else:
            angle = sign * 2.0 * math.pi * k / n
            c, s = math.cos(angle), math.sin(angle)
            tr = a * c - b * s
            ti = a * s + b * c
        outr[k] = er[k] + tr
        outi[k] = ei[k] + ti
        outr[k + half] = er[k] - tr
        outi[k + half] = ei[k] - ti
    return outr, outi


def unit(m, n, sign):
    angle = (m % n).astype(F32) * F32(sign * 2.0 * math.pi / n)
    return jnp.cos(angle), jnp.sin(angle)


def send_matrices():
    row = np.arange(256)
    dd, pp, ks = row // 8, (row // 4) % 2, row % 4
    k2 = 4 * dd + ks
    col = np.arange(512)
    pin, riin, lane = col // 256, (col // 128) % 2, col % 128
    ang = -2.0 * np.pi * np.outer(k2, lane) / 128.0
    c, s = np.cos(ang), np.sin(ang)
    same = (pp[:, None] == pin[None, :])
    real = np.where(riin[None, :] == 0, c, -s) * same
    imag = np.where(riin[None, :] == 0, s, c) * same
    return real.astype(np.float32), imag.astype(np.float32)


def row_block(sign):
    idx = np.arange(128)
    q, r = idx // 32, idx % 32
    ang = sign * 2.0 * np.pi * np.outer(r, r) / 32.0
    same = q[:, None] == q[None, :]
    wr = np.cos(ang) * same
    wi = np.sin(ang) * same
    top = np.concatenate([wr, wi], axis=1)
    bottom = np.concatenate([-wi, wr], axis=1)
    return np.concatenate([top, bottom], axis=0).astype(np.float32)


def row_twiddle(sign):
    g = np.arange(32)[:, None]
    r = (np.arange(512) % 32)[None, :]
    ang = sign * 2.0 * np.pi * (g * r) / 1024.0
    return np.cos(ang).astype(np.float32), np.sin(ang).astype(np.float32)


def receive_matrix():
    row = np.arange(512)
    riin, dd, pp, ks = row // 256, (row // 8) % 32, (row // 4) % 2, row % 4
    k2 = 4 * dd + ks
    col = np.arange(512)
    pout, riout, lc = col // 256, (col // 128) % 2, col % 128
    ang = 2.0 * np.pi * np.outer(k2, lc) / 128.0
    c, s = np.cos(ang), np.sin(ang)
    same = pp[:, None] == pout[None, :]
    val = np.where(riin[:, None] == 0,
                   np.where(riout[None, :] == 0, c, s),
                   np.where(riout[None, :] == 0, -s, c))
    return (val * same / LENGTH).astype(np.float32)


def lane_twiddle(sign, width):
    ka = np.arange(32)[:, None]
    lc = (np.arange(width) % 128)[None, :]
    ang = sign * 2.0 * np.pi * (ka * lc) / 4096.0
    return np.cos(ang).astype(np.float32), np.sin(ang).astype(np.float32)


def cmul(ar, ai, br, bi):
    return ar * br - ai * bi, ar * bi + ai * br


def column_forward_kernel(blk_ref, hist_ref, t1c, t1s, t2c, t2s, lr_ref, li_ref, pac, pas, pbc, pbs,
                          out0_ref, out1_ref, xs_ref):
    for p in range(2):
        xr, xi = [], []
        for t in range(32):
            if t < 8:
                xr.append(hist_ref[p, 0, :, t * 128:(t + 1) * 128])
                xi.append(hist_ref[p, 1, :, t * 128:(t + 1) * 128])
            else:
                xr.append(blk_ref[p, 0, :, (t - 8) * 128:(t - 7) * 128])
                xi.append(blk_ref[p, 1, :, (t - 8) * 128:(t - 7) * 128])
        ar, ai = fft_list(xr, xi, -1)
        for k in range(32):
            wc, ws = cmul(t1c[k:k + 1, :], t1s[k:k + 1, :], t2c[:, k:k + 1], t2s[:, k:k + 1])
            re, im = cmul(ar[k], ai[k], wc, ws)
            xs_ref[k * 32:(k + 1) * 32, p * 256:p * 256 + 128] = re
            xs_ref[k * 32:(k + 1) * 32, p * 256 + 128:p * 256 + 256] = im
    dims = (((1,), (1,)), ((), ()))
    for h, out_ref in enumerate((out0_ref, out1_ref)):
        x = xs_ref[512 * h:512 * (h + 1), :]
        ore = lax.dot_general(lr_ref[...], x, dims, precision=HIGHEST, preferred_element_type=F32)
        oim = lax.dot_general(li_ref[...], x, dims, precision=HIGHEST, preferred_element_type=F32)
        ac = pac[:, 512 * h:512 * (h + 1)]
        as_ = pas[:, 512 * h:512 * (h + 1)]
        for d in range(32):
            bc = pbc[d:d + 1, 512 * h:512 * (h + 1)]
            bs = pbs[d:d + 1, 512 * h:512 * (h + 1)]
            wc, ws = cmul(ac, as_, bc, bs)
            re, im = cmul(ore[8 * d:8 * d + 8], oim[8 * d:8 * d + 8], wc, ws)
            out_ref[8 * d:8 * d + 8, 0:512] = re
            out_ref[8 * d:8 * d + 8, 512:1024] = im


def row_kernel(x_ref, twc_ref, tws_ref, bf_ref, bb_ref, ph_ref, ac_ref, as_ref, bc_ref, bs_ref, cc_ref, cs_ref,
               out_ref, y_ref, w_ref):
    er = [x_ref[8 * d:8 * d + 8, 0:512] for d in range(32)]
    ei = [x_ref[8 * d:8 * d + 8, 512:1024] for d in range(32)]
    fr, fi = fft_list(er, ei, -1)
    for g in range(32):
        a, b = cmul(fr[g], fi[g], twc_ref[g:g + 1, :], tws_ref[g:g + 1, :])
        for j in range(4):
            y_ref[256 * j + 8 * g:256 * j + 8 * g + 8, 0:128] = a[:, 128 * j:128 * (j + 1)]
            y_ref[256 * j + 8 * g:256 * j + 8 * g + 8, 128:256] = b[:, 128 * j:128 * (j + 1)]
    z = jnp.dot(y_ref[...], bf_ref[...], precision=HIGHEST, preferred_element_type=F32)
    phase = ph_ref[...]
    re, im = cmul(z[:, 0:128], z[:, 128:256], jnp.cos(phase), jnp.sin(phase))
    y_ref[:, 0:128] = re
    y_ref[:, 128:256] = im
    w_ref[...] = jnp.dot(y_ref[...], bb_ref[...], precision=HIGHEST, preferred_element_type=F32)
    gr, gi = [], []
    for g in range(32):
        a = jnp.concatenate([w_ref[256 * j + 8 * g:256 * j + 8 * g + 8, 0:128] for j in range(4)], axis=1)
        b = jnp.concatenate([w_ref[256 * j + 8 * g:256 * j + 8 * g + 8, 128:256] for j in range(4)], axis=1)
        a, b = cmul(a, b, twc_ref[g:g + 1, :], -tws_ref[g:g + 1, :])
        gr.append(a)
        gi.append(b)
    ur, ui = fft_list(gr, gi, 1)
    ac = ac_ref[...]
    as_ = as_ref[...]
    for d in range(32):
        wc, ws = cmul(bc_ref[d:d + 1, :], bs_ref[d:d + 1, :], cc_ref[8 * d:8 * d + 8, 0:1], cs_ref[8 * d:8 * d + 8, 0:1])
        wc, ws = cmul(wc, ws, ac, as_)
        re, im = cmul(ur[d], ui[d], wc, ws)
        out_ref[8 * d:8 * d + 8, 0:512] = re
        out_ref[8 * d:8 * d + 8, 512:1024] = im


def column_inverse_kernel(x0_ref, x1_ref, m_ref, twc_ref, tws_ref, out_ref, s_ref):
    lhs_re = jnp.concatenate([x0_ref[:, 0:512].T, x1_ref[:, 0:512].T], axis=0)
    lhs_im = jnp.concatenate([x0_ref[:, 512:1024].T, x1_ref[:, 512:1024].T], axis=0)
    lhs = jnp.concatenate([lhs_re, lhs_im], axis=1)
    s_ref[...] = jnp.dot(lhs, m_ref[...], precision=HIGHEST, preferred_element_type=F32)
    er, ei = [], []
    for k in range(32):
        rows = slice(32 * k, 32 * (k + 1))
        a = jnp.concatenate([s_ref[rows, 0:128], s_ref[rows, 256:384]], axis=1)
        b = jnp.concatenate([s_ref[rows, 128:256], s_ref[rows, 384:512]], axis=1)
        a, b = cmul(a, b, twc_ref[k:k + 1, :], tws_ref[k:k + 1, :])
        er.append(a)
        ei.append(b)
    tr, ti = fft_list(er, ei, 1)
    for t in range(8, 32):
        for p in range(2):
            out_ref[p, 0, :, (t - 8) * 128:(t - 7) * 128] = tr[t][:, 128 * p:128 * (p + 1)]
            out_ref[p, 1, :, (t - 8) * 128:(t - 7) * 128] = ti[t][:, 128 * p:128 * (p + 1)]


def call(kernel, out_shapes, scratch, *args):
    return pl.pallas_call(
        kernel,
        out_shape=[jax.ShapeDtypeStruct(s, F32) for s in out_shapes],
        scratch_shapes=[pltpu.VMEM(s, F32) for s in scratch],
        interpret=INTERPRET,
    )(*args)


def exchanged(block):
    rows, width = block.shape
    out = lax.all_to_all(block.reshape(32, rows // 32, width), "band", 0, 0, tiled=True)
    return out.reshape(rows, width)


def per_device(voltages, chirp_phase):
    block = voltages[0, 0]
    band = lax.axis_index("band")
    history = passed_along(block[..., 3072 - HIST:], "seg", 1)
    phases = gathered(chirp_phase, "seg", 1)[0]
    chirp = phases.reshape(32, 32, 4, 8, 4).transpose(3, 1, 2, 4, 0)
    chirp = jnp.broadcast_to(chirp[:, :, None], (8, 32, 2, 4, 4, 32)).reshape(2048, 128)

    i32 = jnp.int32
    lane = jnp.arange(1024, dtype=i32)[None, :]
    r_lane = 32 * band + lane % 32
    ka_lane = lane // 32
    t2c, t2s = unit(jnp.arange(32, dtype=i32)[None, :] * (32 * band + jnp.arange(32, dtype=i32)[:, None]), LENGTH, -1)
    q = jnp.arange(8, dtype=i32)[:, None]
    dd = jnp.arange(32, dtype=i32)[:, None]
    pac, pas = unit(32 * r_lane * (q % 4), LENGTH, -1)
    pbc, pbs = unit(128 * r_lane * dd, LENGTH, -1)
    kc_lane = 128 * band + ka_lane
    rl_lane = lane % 32
    bac, bas = unit(rl_lane * (kc_lane + 32 * (q % 4)), LENGTH, 1)
    bbc, bbs = unit(32 * dd * kc_lane, LENGTH, 1)
    rows = jnp.arange(256, dtype=i32)[:, None]
    bcc, bcs = unit(jnp.broadcast_to(1024 * (rows // 8) * (rows % 4), (256, 128)), LENGTH, 1)

    t1c, t1s = lane_twiddle(-1, 128)
    lr, li = send_matrices()
    send0, send1 = call(column_forward_kernel, [(256, 1024), (256, 1024)], [(1024, 512)],
                        block, history, jnp.asarray(t1c), jnp.asarray(t1s), t2c, t2s,
                        jnp.asarray(lr), jnp.asarray(li), pac, pas, pbc, pbs)

    twc, tws = row_twiddle(-1)
    fwd, bwd = jnp.asarray(row_block(-1)), jnp.asarray(row_block(1))
    back = []
    for h, send in enumerate((send0, send1)):
        received = exchanged(send)
        lanes = slice(512 * h, 512 * (h + 1))
        (sent,) = call(row_kernel, [(256, 1024)], [(1024, 256), (1024, 256)],
                       received, jnp.asarray(twc), jnp.asarray(tws), fwd, bwd,
                       chirp[1024 * h:1024 * (h + 1)], bac[:, lanes], bas[:, lanes],
                       bbc[:, lanes], bbs[:, lanes], bcc, bcs)
        back.append(exchanged(sent))

    cc, cs = lane_twiddle(1, 256)
    (out,) = call(column_inverse_kernel, [(2, 2, ROWS_DEV, 3072)], [(1024, 512)],
                  back[0], back[1], jnp.asarray(receive_matrix()), jnp.asarray(cc), jnp.asarray(cs))
    return out[None, None]


def solution(mesh):
    in_specs = (P("seg", None, None, None, "band", None), P(None, "seg", "band"))
    out_specs = P("seg", None, None, None, "band", None)
    return jax.shard_map(
        per_device, mesh=mesh, in_specs=in_specs, out_specs=out_specs, check_vma=False
    )
```

```python
import math

import numpy as np
import jax
import jax.numpy as jnp
from jax import lax
from jax.experimental import pallas as pl
from jax.experimental.pallas import tpu as pltpu
from jax.sharding import PartitionSpec as P

INTERPRET = False
HIGHEST = lax.Precision.HIGHEST
F32 = jnp.float32
ROWS_DEV = 32
COLS = 4096
HIST = 1024
LENGTH = 1024 * 4096


def passed_along(block, axis, distance):
    devices = range(lax.axis_size(axis))
    route = [(i - distance, i) for i in devices if i - distance in devices]
    return lax.ppermute(block, axis, route)


def gathered(block, axis, dim):
    size = lax.axis_size(axis)
    pieces = [block]
    for shift in range(1, size):
        route = [((i + shift) % size, i) for i in range(size)]
        pieces.append(lax.ppermute(block, axis, route))
    ahead = jnp.stack(pieces, axis=0)
    ordered = jnp.roll(ahead, lax.axis_index(axis), axis=0)
    ordered = jnp.moveaxis(ordered, 0, dim)
    shape = list(block.shape)
    shape[dim] *= size
    return ordered.reshape(shape)


def fft_list(xr, xi, sign):
    n = len(xr)
    if n == 1:
        return list(xr), list(xi)
    er, ei = fft_list(xr[0::2], xi[0::2], sign)
    odd_r, odd_i = fft_list(xr[1::2], xi[1::2], sign)
    half = n // 2
    outr = [None] * n
    outi = [None] * n
    for k in range(half):
        a, b = odd_r[k], odd_i[k]
        if k == 0:
            tr, ti = a, b
        elif 4 * k == n:
            tr, ti = (-b, a) if sign > 0 else (b, -a)
        else:
            angle = sign * 2.0 * math.pi * k / n
            c, s = math.cos(angle), math.sin(angle)
            tr = a * c - b * s
            ti = a * s + b * c
        outr[k] = er[k] + tr
        outi[k] = ei[k] + ti
        outr[k + half] = er[k] - tr
        outi[k + half] = ei[k] - ti
    return outr, outi


def unit(m, n, sign):
    angle = (m % n).astype(F32) * F32(sign * 2.0 * math.pi / n)
    return jnp.cos(angle), jnp.sin(angle)


def send_matrices():
    row = np.arange(256)
    dd, pp, ks = row // 8, (row // 4) % 2, row % 4
    k2 = 4 * dd + ks
    col = np.arange(512)
    pin, riin, lane = col // 256, (col // 128) % 2, col % 128
    ang = -2.0 * np.pi * np.outer(k2, lane) / 128.0
    c, s = np.cos(ang), np.sin(ang)
    same = (pp[:, None] == pin[None, :])
    real = np.where(riin[None, :] == 0, c, -s) * same
    imag = np.where(riin[None, :] == 0, s, c) * same
    return real.astype(np.float32), imag.astype(np.float32)


def row_block(sign):
    idx = np.arange(128)
    q, r = idx // 32, idx % 32
    ang = sign * 2.0 * np.pi * np.outer(r, r) / 32.0
    same = q[:, None] == q[None, :]
    wr = np.cos(ang) * same
    wi = np.sin(ang) * same
    top = np.concatenate([wr, wi], axis=1)
    bottom = np.concatenate([-wi, wr], axis=1)
    return np.concatenate([top, bottom], axis=0).astype(np.float32)


def row_twiddle(sign):
    g = np.arange(32)[:, None]
    r = (np.arange(512) % 32)[None, :]
    ang = sign * 2.0 * np.pi * (g * r) / 1024.0
    return np.cos(ang).astype(np.float32), np.sin(ang).astype(np.float32)


def receive_matrix():
    row = np.arange(512)
    riin, dd, pp, ks = row // 256, (row // 8) % 32, (row // 4) % 2, row % 4
    k2 = 4 * dd + ks
    col = np.arange(512)
    pout, riout, lc = col // 256, (col // 128) % 2, col % 128
    ang = 2.0 * np.pi * np.outer(k2, lc) / 128.0
    c, s = np.cos(ang), np.sin(ang)
    same = pp[:, None] == pout[None, :]
    val = np.where(riin[:, None] == 0,
                   np.where(riout[None, :] == 0, c, s),
                   np.where(riout[None, :] == 0, -s, c))
    return (val * same / LENGTH).astype(np.float32)


def lane_twiddle(sign, width):
    ka = np.arange(32)[:, None]
    lc = (np.arange(width) % 128)[None, :]
    ang = sign * 2.0 * np.pi * (ka * lc) / 4096.0
    return np.cos(ang).astype(np.float32), np.sin(ang).astype(np.float32)


def cmul(ar, ai, br, bi):
    return ar * br - ai * bi, ar * bi + ai * br


def column_forward_kernel(blk_ref, hist_ref, t1c, t1s, t2c, t2s, lr_ref, li_ref, pac, pas, pbc, pbs,
                          out_ref, xs_ref):
    for p in range(2):
        xr, xi = [], []
        for t in range(32):
            if t < 8:
                xr.append(hist_ref[p, 0, :, t * 128:(t + 1) * 128])
                xi.append(hist_ref[p, 1, :, t * 128:(t + 1) * 128])
            else:
                xr.append(blk_ref[p, 0, :, (t - 8) * 128:(t - 7) * 128])
                xi.append(blk_ref[p, 1, :, (t - 8) * 128:(t - 7) * 128])
        ar, ai = fft_list(xr, xi, -1)
        for k in range(32):
            wc, ws = cmul(t1c[k:k + 1, :], t1s[k:k + 1, :], t2c[:, k:k + 1], t2s[:, k:k + 1])
            re, im = cmul(ar[k], ai[k], wc, ws)
            xs_ref[k * 32:(k + 1) * 32, p * 256:p * 256 + 128] = re
            xs_ref[k * 32:(k + 1) * 32, p * 256 + 128:p * 256 + 256] = im
    dims = (((1,), (1,)), ((), ()))
    for h in range(2):
        x = xs_ref[512 * h:512 * (h + 1), :]
        ore = lax.dot_general(lr_ref[...], x, dims, precision=HIGHEST, preferred_element_type=F32)
        oim = lax.dot_general(li_ref[...], x, dims, precision=HIGHEST, preferred_element_type=F32)
        ac = pac[:, 512 * h:512 * (h + 1)]
        as_ = pas[:, 512 * h:512 * (h + 1)]
        for d in range(32):
            bc = pbc[d:d + 1, 512 * h:512 * (h + 1)]
            bs = pbs[d:d + 1, 512 * h:512 * (h + 1)]
            wc, ws = cmul(ac, as_, bc, bs)
            re, im = cmul(ore[8 * d:8 * d + 8], oim[8 * d:8 * d + 8], wc, ws)
            out_ref[8 * d:8 * d + 8, 1024 * h:1024 * h + 512] = re
            out_ref[8 * d:8 * d + 8, 1024 * h + 512:1024 * h + 1024] = im


def row_kernel(x_ref, twc_ref, tws_ref, bf_ref, bb_ref, ph_ref, ac_ref, as_ref, bc_ref, bs_ref, cc_ref, cs_ref,
               out_ref, y_ref, w_ref):
    for h in range(2):
        row_half(h, x_ref, twc_ref, tws_ref, bf_ref, bb_ref, ph_ref, ac_ref, as_ref, bc_ref, bs_ref, cc_ref, cs_ref,
                 out_ref, y_ref, w_ref)


def row_half(h, x_ref, twc_ref, tws_ref, bf_ref, bb_ref, ph_ref, ac_ref, as_ref, bc_ref, bs_ref, cc_ref, cs_ref,
             out_ref, y_ref, w_ref):
    base = 1024 * h
    lanes = slice(512 * h, 512 * (h + 1))
    er = [x_ref[8 * d:8 * d + 8, base:base + 512] for d in range(32)]
    ei = [x_ref[8 * d:8 * d + 8, base + 512:base + 1024] for d in range(32)]
    fr, fi = fft_list(er, ei, -1)
    for g in range(32):
        a, b = cmul(fr[g], fi[g], twc_ref[g:g + 1, :], tws_ref[g:g + 1, :])
        for j in range(4):
            y_ref[256 * j + 8 * g:256 * j + 8 * g + 8, 0:128] = a[:, 128 * j:128 * (j + 1)]
            y_ref[256 * j + 8 * g:256 * j + 8 * g + 8, 128:256] = b[:, 128 * j:128 * (j + 1)]
    z = jnp.dot(y_ref[...], bf_ref[...], precision=HIGHEST, preferred_element_type=F32)
    phase = ph_ref[1024 * h:1024 * (h + 1), :]
    re, im = cmul(z[:, 0:128], z[:, 128:256], jnp.cos(phase), jnp.sin(phase))
    y_ref[:, 0:128] = re
    y_ref[:, 128:256] = im
    w_ref[...] = jnp.dot(y_ref[...], bb_ref[...], precision=HIGHEST, preferred_element_type=F32)
    gr, gi = [], []
    for g in range(32):
        a = jnp.concatenate([w_ref[256 * j + 8 * g:256 * j + 8 * g + 8, 0:128] for j in range(4)], axis=1)
        b = jnp.concatenate([w_ref[256 * j + 8 * g:256 * j + 8 * g + 8, 128:256] for j in range(4)], axis=1)
        a, b = cmul(a, b, twc_ref[g:g + 1, :], -tws_ref[g:g + 1, :])
        gr.append(a)
        gi.append(b)
    ur, ui = fft_list(gr, gi, 1)
    ac = ac_ref[:, lanes]
    as_ = as_ref[:, lanes]
    for d in range(32):
        wc, ws = cmul(bc_ref[d:d + 1, lanes], bs_ref[d:d + 1, lanes], cc_ref[8 * d:8 * d + 8, 0:1], cs_ref[8 * d:8 * d + 8, 0:1])
        wc, ws = cmul(wc, ws, ac, as_)
        re, im = cmul(ur[d], ui[d], wc, ws)
        out_ref[8 * d:8 * d + 8, base:base + 512] = re
        out_ref[8 * d:8 * d + 8, base + 512:base + 1024] = im


def column_inverse_kernel(x_ref, m_ref, twc_ref, tws_ref, out_ref, s_ref):
    lhs_re = jnp.concatenate([x_ref[:, 0:512].T, x_ref[:, 1024:1536].T], axis=0)
    lhs_im = jnp.concatenate([x_ref[:, 512:1024].T, x_ref[:, 1536:2048].T], axis=0)
    lhs = jnp.concatenate([lhs_re, lhs_im], axis=1)
    s_ref[...] = jnp.dot(lhs, m_ref[...], precision=HIGHEST, preferred_element_type=F32)
    er, ei = [], []
    for k in range(32):
        rows = slice(32 * k, 32 * (k + 1))
        a = jnp.concatenate([s_ref[rows, 0:128], s_ref[rows, 256:384]], axis=1)
        b = jnp.concatenate([s_ref[rows, 128:256], s_ref[rows, 384:512]], axis=1)
        a, b = cmul(a, b, twc_ref[k:k + 1, :], tws_ref[k:k + 1, :])
        er.append(a)
        ei.append(b)
    tr, ti = fft_list(er, ei, 1)
    for t in range(8, 32):
        for p in range(2):
            out_ref[p, 0, :, (t - 8) * 128:(t - 7) * 128] = tr[t][:, 128 * p:128 * (p + 1)]
            out_ref[p, 1, :, (t - 8) * 128:(t - 7) * 128] = ti[t][:, 128 * p:128 * (p + 1)]


def call(kernel, out_shapes, scratch, *args):
    return pl.pallas_call(
        kernel,
        out_shape=[jax.ShapeDtypeStruct(s, F32) for s in out_shapes],
        scratch_shapes=[pltpu.VMEM(s, F32) for s in scratch],
        interpret=INTERPRET,
    )(*args)


def exchanged(block):
    rows, width = block.shape
    out = lax.all_to_all(block.reshape(32, rows // 32, width), "band", 0, 0, tiled=True)
    return out.reshape(rows, width)


def per_device(voltages, chirp_phase):
    block = voltages[0, 0]
    band = lax.axis_index("band")
    history = passed_along(block[..., 3072 - HIST:], "seg", 1)
    phases = gathered(chirp_phase, "seg", 1)[0]
    chirp = phases.reshape(32, 32, 4, 8, 4).transpose(3, 1, 2, 4, 0)
    chirp = jnp.broadcast_to(chirp[:, :, None], (8, 32, 2, 4, 4, 32)).reshape(2048, 128)

    i32 = jnp.int32
    lane = jnp.arange(1024, dtype=i32)[None, :]
    r_lane = 32 * band + lane % 32
    ka_lane = lane // 32
    t2c, t2s = unit(jnp.arange(32, dtype=i32)[None, :] * (32 * band + jnp.arange(32, dtype=i32)[:, None]), LENGTH, -1)
    q = jnp.arange(8, dtype=i32)[:, None]
    dd = jnp.arange(32, dtype=i32)[:, None]
    pac, pas = unit(32 * r_lane * (q % 4), LENGTH, -1)
    pbc, pbs = unit(128 * r_lane * dd, LENGTH, -1)
    kc_lane = 128 * band + ka_lane
    rl_lane = lane % 32
    bac, bas = unit(rl_lane * (kc_lane + 32 * (q % 4)), LENGTH, 1)
    bbc, bbs = unit(32 * dd * kc_lane, LENGTH, 1)
    rows = jnp.arange(256, dtype=i32)[:, None]
    bcc, bcs = unit(jnp.broadcast_to(1024 * (rows // 8) * (rows % 4), (256, 128)), LENGTH, 1)

    t1c, t1s = lane_twiddle(-1, 128)
    lr, li = send_matrices()
    (send,) = call(column_forward_kernel, [(256, 2048)], [(1024, 512)],
                   block, history, jnp.asarray(t1c), jnp.asarray(t1s), t2c, t2s,
                   jnp.asarray(lr), jnp.asarray(li), pac, pas, pbc, pbs)
    received = exchanged(send)

    twc, tws = row_twiddle(-1)
    (sent,) = call(row_kernel, [(256, 2048)], [(1024, 256), (1024, 256)],
                   received, jnp.asarray(twc), jnp.asarray(tws), jnp.asarray(row_block(-1)),
                   jnp.asarray(row_block(1)), chirp, bac, bas, bbc, bbs, bcc, bcs)
    returned = exchanged(sent)

    cc, cs = lane_twiddle(1, 256)
    (out,) = call(column_inverse_kernel, [(2, 2, ROWS_DEV, 3072)], [(1024, 512)],
                  returned, jnp.asarray(receive_matrix()), jnp.asarray(cc), jnp.asarray(cs))
    return out[None, None]


def solution(mesh):
    in_specs = (P("seg", None, None, None, "band", None), P(None, "seg", "band"))
    out_specs = P("seg", None, None, None, "band", None)
    return jax.shard_map(
        per_device, mesh=mesh, in_specs=in_specs, out_specs=out_specs, check_vma=False
    )
```

```python
import math

import numpy as np
import jax
import jax.numpy as jnp
from jax import lax
from jax.experimental import pallas as pl
from jax.experimental.pallas import tpu as pltpu
from jax.sharding import PartitionSpec as P

INTERPRET = False
HIGHEST = lax.Precision.HIGHEST
F32 = jnp.float32
ROWS_DEV = 32
COLS = 4096
HIST = 1024
LENGTH = 1024 * 4096


def passed_along(block, axis, distance):
    devices = range(lax.axis_size(axis))
    route = [(i - distance, i) for i in devices if i - distance in devices]
    return lax.ppermute(block, axis, route)


def gathered(block, axis, dim):
    size = lax.axis_size(axis)
    pieces = [block]
    for shift in range(1, size):
        route = [((i + shift) % size, i) for i in range(size)]
        pieces.append(lax.ppermute(block, axis, route))
    ahead = jnp.stack(pieces, axis=0)
    ordered = jnp.roll(ahead, lax.axis_index(axis), axis=0)
    ordered = jnp.moveaxis(ordered, 0, dim)
    shape = list(block.shape)
    shape[dim] *= size
    return ordered.reshape(shape)


def fft_list(xr, xi, sign):
    n = len(xr)
    if n == 1:
        return list(xr), list(xi)
    er, ei = fft_list(xr[0::2], xi[0::2], sign)
    odd_r, odd_i = fft_list(xr[1::2], xi[1::2], sign)
    half = n // 2
    outr = [None] * n
    outi = [None] * n
    for k in range(half):
        a, b = odd_r[k], odd_i[k]
        if k == 0:
            tr, ti = a, b
        elif 4 * k == n:
            tr, ti = (-b, a) if sign > 0 else (b, -a)
        else:
            angle = sign * 2.0 * math.pi * k / n
            c, s = math.cos(angle), math.sin(angle)
            tr = a * c - b * s
            ti = a * s + b * c
        outr[k] = er[k] + tr
        outi[k] = ei[k] + ti
        outr[k + half] = er[k] - tr
        outi[k + half] = ei[k] - ti
    return outr, outi


def unit(m, n, sign):
    angle = (m % n).astype(F32) * F32(sign * 2.0 * math.pi / n)
    return jnp.cos(angle), jnp.sin(angle)


def send_matrices():
    row = np.arange(256)
    dd, pp, ks = row // 8, (row // 4) % 2, row % 4
    k2 = 4 * dd + ks
    col = np.arange(512)
    pin, riin, lane = col // 256, (col // 128) % 2, col % 128
    ang = -2.0 * np.pi * np.outer(k2, lane) / 128.0
    c, s = np.cos(ang), np.sin(ang)
    same = (pp[:, None] == pin[None, :])
    real = np.where(riin[None, :] == 0, c, -s) * same
    imag = np.where(riin[None, :] == 0, s, c) * same
    return real.astype(np.float32), imag.astype(np.float32)


def row_block(sign):
    idx = np.arange(128)
    q, r = idx // 32, idx % 32
    ang = sign * 2.0 * np.pi * np.outer(r, r) / 32.0
    same = q[:, None] == q[None, :]
    wr = np.cos(ang) * same
    wi = np.sin(ang) * same
    top = np.concatenate([wr, wi], axis=1)
    bottom = np.concatenate([-wi, wr], axis=1)
    return np.concatenate([top, bottom], axis=0).astype(np.float32)


def row_twiddle(sign):
    g = np.arange(32)[:, None]
    r = (np.arange(512) % 32)[None, :]
    ang = sign * 2.0 * np.pi * (g * r) / 1024.0
    return np.cos(ang).astype(np.float32), np.sin(ang).astype(np.float32)


def receive_matrix():
    row = np.arange(512)
    riin, dd, pp, ks = row // 256, (row // 8) % 32, (row // 4) % 2, row % 4
    k2 = 4 * dd + ks
    col = np.arange(512)
    pout, riout, lc = col // 256, (col // 128) % 2, col % 128
    ang = 2.0 * np.pi * np.outer(k2, lc) / 128.0
    c, s = np.cos(ang), np.sin(ang)
    same = pp[:, None] == pout[None, :]
    val = np.where(riin[:, None] == 0,
                   np.where(riout[None, :] == 0, c, s),
                   np.where(riout[None, :] == 0, -s, c))
    return (val * same / LENGTH).astype(np.float32)


def lane_twiddle(sign, width):
    ka = np.arange(32)[:, None]
    lc = (np.arange(width) % 128)[None, :]
    ang = sign * 2.0 * np.pi * (ka * lc) / 4096.0
    return np.cos(ang).astype(np.float32), np.sin(ang).astype(np.float32)


def cmul(ar, ai, br, bi):
    return ar * br - ai * bi, ar * bi + ai * br


def column_forward_kernel(blk_ref, hist_ref, t1c, t1s, t2c, t2s, lr_ref, li_ref, pac, pas, pbc, pbs,
                          out_ref, xs_ref):
    for p in range(2):
        xr, xi = [], []
        for t in range(32):
            if t < 8:
                xr.append(hist_ref[p, 0, :, t * 128:(t + 1) * 128])
                xi.append(hist_ref[p, 1, :, t * 128:(t + 1) * 128])
            else:
                xr.append(blk_ref[p, 0, :, (t - 8) * 128:(t - 7) * 128])
                xi.append(blk_ref[p, 1, :, (t - 8) * 128:(t - 7) * 128])
        ar, ai = fft_list(xr, xi, -1)
        for k in range(32):
            wc, ws = cmul(t1c[k:k + 1, :], t1s[k:k + 1, :], t2c[:, k:k + 1], t2s[:, k:k + 1])
            re, im = cmul(ar[k], ai[k], wc, ws)
            xs_ref[k * 32:(k + 1) * 32, p * 256:p * 256 + 128] = re
            xs_ref[k * 32:(k + 1) * 32, p * 256 + 128:p * 256 + 256] = im
    dims = (((1,), (1,)), ((), ()))
    for h in range(2):
        x = xs_ref[512 * h:512 * (h + 1), :]
        ore = lax.dot_general(lr_ref[...], x, dims, precision=HIGHEST, preferred_element_type=F32)
        oim = lax.dot_general(li_ref[...], x, dims, precision=HIGHEST, preferred_element_type=F32)
        ac = pac[:, 512 * h:512 * (h + 1)]
        as_ = pas[:, 512 * h:512 * (h + 1)]
        for d in range(32):
            bc = pbc[d:d + 1, 512 * h:512 * (h + 1)]
            bs = pbs[d:d + 1, 512 * h:512 * (h + 1)]
            wc, ws = cmul(ac, as_, bc, bs)
            re, im = cmul(ore[8 * d:8 * d + 8], oim[8 * d:8 * d + 8], wc, ws)
            out_ref[8 * d:8 * d + 8, 1024 * h:1024 * h + 512] = re
            out_ref[8 * d:8 * d + 8, 1024 * h + 512:1024 * h + 1024] = im


def row_kernel(x_ref, twc_ref, tws_ref, bf_ref, bb_ref, chc_ref, chs_ref, pc_ref, ps_ref, out_ref, y_ref, w_ref):
    for h in range(2):
        row_half(h, x_ref, twc_ref, tws_ref, bf_ref, bb_ref, chc_ref, chs_ref, pc_ref, ps_ref, out_ref, y_ref, w_ref)


def row_half(h, x_ref, twc_ref, tws_ref, bf_ref, bb_ref, chc_ref, chs_ref, pc_ref, ps_ref, out_ref, y_ref, w_ref):
    base = 1024 * h
    lanes = slice(512 * h, 512 * (h + 1))
    er = [x_ref[8 * d:8 * d + 8, base:base + 512] for d in range(32)]
    ei = [x_ref[8 * d:8 * d + 8, base + 512:base + 1024] for d in range(32)]
    fr, fi = fft_list(er, ei, -1)
    for g in range(32):
        a, b = cmul(fr[g], fi[g], twc_ref[g:g + 1, :], tws_ref[g:g + 1, :])
        for j in range(4):
            y_ref[256 * j + 8 * g:256 * j + 8 * g + 8, 0:128] = a[:, 128 * j:128 * (j + 1)]
            y_ref[256 * j + 8 * g:256 * j + 8 * g + 8, 128:256] = b[:, 128 * j:128 * (j + 1)]
    z = jnp.dot(y_ref[...], bf_ref[...], precision=HIGHEST, preferred_element_type=F32)
    re, im = cmul(z[:, 0:128], z[:, 128:256], chc_ref[1024 * h:1024 * (h + 1), :], chs_ref[1024 * h:1024 * (h + 1), :])
    y_ref[:, 0:128] = re
    y_ref[:, 128:256] = im
    w_ref[...] = jnp.dot(y_ref[...], bb_ref[...], precision=HIGHEST, preferred_element_type=F32)
    gr, gi = [], []
    for g in range(32):
        a = jnp.concatenate([w_ref[256 * j + 8 * g:256 * j + 8 * g + 8, 0:128] for j in range(4)], axis=1)
        b = jnp.concatenate([w_ref[256 * j + 8 * g:256 * j + 8 * g + 8, 128:256] for j in range(4)], axis=1)
        a, b = cmul(a, b, twc_ref[g:g + 1, :], -tws_ref[g:g + 1, :])
        gr.append(a)
        gi.append(b)
    ur, ui = fft_list(gr, gi, 1)
    for d in range(32):
        re, im = cmul(ur[d], ui[d], pc_ref[8 * d:8 * d + 8, lanes], ps_ref[8 * d:8 * d + 8, lanes])
        out_ref[8 * d:8 * d + 8, base:base + 512] = re
        out_ref[8 * d:8 * d + 8, base + 512:base + 1024] = im


def column_inverse_kernel(x_ref, m_ref, twc_ref, tws_ref, out_ref, s_ref):
    lhs_re = jnp.concatenate([x_ref[:, 0:512].T, x_ref[:, 1024:1536].T], axis=0)
    lhs_im = jnp.concatenate([x_ref[:, 512:1024].T, x_ref[:, 1536:2048].T], axis=0)
    lhs = jnp.concatenate([lhs_re, lhs_im], axis=1)
    s_ref[...] = jnp.dot(lhs, m_ref[...], precision=HIGHEST, preferred_element_type=F32)
    er, ei = [], []
    for k in range(32):
        rows = slice(32 * k, 32 * (k + 1))
        a = jnp.concatenate([s_ref[rows, 0:128], s_ref[rows, 256:384]], axis=1)
        b = jnp.concatenate([s_ref[rows, 128:256], s_ref[rows, 384:512]], axis=1)
        a, b = cmul(a, b, twc_ref[k:k + 1, :], tws_ref[k:k + 1, :])
        er.append(a)
        ei.append(b)
    tr, ti = fft_list(er, ei, 1)
    for t in range(8, 32):
        for p in range(2):
            out_ref[p, 0, :, (t - 8) * 128:(t - 7) * 128] = tr[t][:, 128 * p:128 * (p + 1)]
            out_ref[p, 1, :, (t - 8) * 128:(t - 7) * 128] = ti[t][:, 128 * p:128 * (p + 1)]


def call(kernel, out_shapes, scratch, *args):
    return pl.pallas_call(
        kernel,
        out_shape=[jax.ShapeDtypeStruct(s, F32) for s in out_shapes],
        scratch_shapes=[pltpu.VMEM(s, F32) for s in scratch],
        interpret=INTERPRET,
    )(*args)


def exchanged(block):
    rows, width = block.shape
    out = lax.all_to_all(block.reshape(32, rows // 32, width), "band", 0, 0, tiled=True)
    return out.reshape(rows, width)


def per_device(voltages, chirp_phase):
    block = voltages[0, 0]
    band = lax.axis_index("band")
    history = passed_along(block[..., 3072 - HIST:], "seg", 1)

    i32 = jnp.int32
    lane = jnp.arange(1024, dtype=i32)[None, :]
    r_lane = 32 * band + lane % 32
    ka_lane = lane // 32
    t2c, t2s = unit(jnp.arange(32, dtype=i32)[None, :] * (32 * band + jnp.arange(32, dtype=i32)[:, None]), LENGTH, -1)
    q = jnp.arange(8, dtype=i32)[:, None]
    dd = jnp.arange(32, dtype=i32)[:, None]
    pac, pas = unit(32 * r_lane * (q % 4), LENGTH, -1)
    pbc, pbs = unit(128 * r_lane * dd, LENGTH, -1)
    kc_lane = 128 * band + ka_lane
    rl_lane = lane % 32
    rows = jnp.arange(256, dtype=i32)[:, None]

    t1c, t1s = lane_twiddle(-1, 128)
    lr, li = send_matrices()
    (send,) = call(column_forward_kernel, [(256, 2048)], [(1024, 512)],
                   block, history, jnp.asarray(t1c), jnp.asarray(t1s), t2c, t2s,
                   jnp.asarray(lr), jnp.asarray(li), pac, pas, pbc, pbs)
    received = exchanged(send)

    chirp_phase, send = lax.optimization_barrier((chirp_phase, send))
    phases = gathered(chirp_phase, "seg", 1)[0]
    chirp = phases.reshape(32, 32, 4, 8, 4).transpose(3, 1, 2, 4, 0)
    chirp = jnp.broadcast_to(chirp[:, :, None], (8, 32, 2, 4, 4, 32)).reshape(2048, 128)
    ch_c, ch_s = jnp.cos(chirp), jnp.sin(chirp)
    back_c, back_s = unit((32 * (rows // 8) + lane % 32) * (kc_lane + 32 * (rows % 4)), LENGTH, 1)

    twc, tws = row_twiddle(-1)
    (sent,) = call(row_kernel, [(256, 2048)], [(1024, 256), (1024, 256)],
                   received, jnp.asarray(twc), jnp.asarray(tws), jnp.asarray(row_block(-1)),
                   jnp.asarray(row_block(1)), ch_c, ch_s, back_c, back_s)
    returned = exchanged(sent)

    cc, cs = lane_twiddle(1, 256)
    (out,) = call(column_inverse_kernel, [(2, 2, ROWS_DEV, 3072)], [(1024, 512)],
                  returned, jnp.asarray(receive_matrix()), jnp.asarray(cc), jnp.asarray(cs))
    return out[None, None]


def solution(mesh):
    in_specs = (P("seg", None, None, None, "band", None), P(None, "seg", "band"))
    out_specs = P("seg", None, None, None, "band", None)
    return jax.shard_map(
        per_device, mesh=mesh, in_specs=in_specs, out_specs=out_specs, check_vma=False
    )
```

```python
import math

import numpy as np
import jax
import jax.numpy as jnp
from jax import lax
from jax.experimental import pallas as pl
from jax.experimental.pallas import tpu as pltpu
from jax.sharding import PartitionSpec as P

INTERPRET = False
HIGHEST = lax.Precision.HIGHEST
F32 = jnp.float32
ROWS_DEV = 32
COLS = 4096
HIST = 1024
LENGTH = 1024 * 4096


def passed_along(block, axis, distance):
    devices = range(lax.axis_size(axis))
    route = [(i - distance, i) for i in devices if i - distance in devices]
    return lax.ppermute(block, axis, route)


def gathered(block, axis, dim):
    size = lax.axis_size(axis)
    pieces = [block]
    for shift in range(1, size):
        route = [((i + shift) % size, i) for i in range(size)]
        pieces.append(lax.ppermute(block, axis, route))
    ahead = jnp.stack(pieces, axis=0)
    ordered = jnp.roll(ahead, lax.axis_index(axis), axis=0)
    ordered = jnp.moveaxis(ordered, 0, dim)
    shape = list(block.shape)
    shape[dim] *= size
    return ordered.reshape(shape)


def fft_list(xr, xi, sign):
    n = len(xr)
    if n == 1:
        return list(xr), list(xi)
    er, ei = fft_list(xr[0::2], xi[0::2], sign)
    odd_r, odd_i = fft_list(xr[1::2], xi[1::2], sign)
    half = n // 2
    outr = [None] * n
    outi = [None] * n
    for k in range(half):
        a, b = odd_r[k], odd_i[k]
        if k == 0:
            tr, ti = a, b
        elif 4 * k == n:
            tr, ti = (-b, a) if sign > 0 else (b, -a)
        else:
            angle = sign * 2.0 * math.pi * k / n
            c, s = math.cos(angle), math.sin(angle)
            tr = a * c - b * s
            ti = a * s + b * c
        outr[k] = er[k] + tr
        outi[k] = ei[k] + ti
        outr[k + half] = er[k] - tr
        outi[k + half] = ei[k] - ti
    return outr, outi


def unit(m, n, sign):
    angle = (m % n).astype(F32) * F32(sign * 2.0 * math.pi / n)
    return jnp.cos(angle), jnp.sin(angle)


def send_matrices():
    row = np.arange(256)
    dd, pp, ks = row // 8, (row // 4) % 2, row % 4
    k2 = 4 * dd + ks
    col = np.arange(512)
    pin, riin, lane = col // 256, (col // 128) % 2, col % 128
    ang = -2.0 * np.pi * np.outer(k2, lane) / 128.0
    c, s = np.cos(ang), np.sin(ang)
    same = (pp[:, None] == pin[None, :])
    real = np.where(riin[None, :] == 0, c, -s) * same
    imag = np.where(riin[None, :] == 0, s, c) * same
    return real.astype(np.float32), imag.astype(np.float32)


def row_block(sign):
    idx = np.arange(128)
    q, r = idx // 32, idx % 32
    ang = sign * 2.0 * np.pi * np.outer(r, r) / 32.0
    same = q[:, None] == q[None, :]
    wr = np.cos(ang) * same
    wi = np.sin(ang) * same
    top = np.concatenate([wr, wi], axis=1)
    bottom = np.concatenate([-wi, wr], axis=1)
    return np.concatenate([top, bottom], axis=0).astype(np.float32)


def row_twiddle(sign):
    g = np.arange(32)[:, None]
    r = (np.arange(512) % 32)[None, :]
    ang = sign * 2.0 * np.pi * (g * r) / 1024.0
    return np.cos(ang).astype(np.float32), np.sin(ang).astype(np.float32)


def receive_matrix():
    row = np.arange(512)
    riin, dd, pp, ks = row // 256, (row // 8) % 32, (row // 4) % 2, row % 4
    k2 = 4 * dd + ks
    col = np.arange(512)
    pout, riout, lc = col // 256, (col // 128) % 2, col % 128
    ang = 2.0 * np.pi * np.outer(k2, lc) / 128.0
    c, s = np.cos(ang), np.sin(ang)
    same = pp[:, None] == pout[None, :]
    val = np.where(riin[:, None] == 0,
                   np.where(riout[None, :] == 0, c, s),
                   np.where(riout[None, :] == 0, -s, c))
    return (val * same / LENGTH).astype(np.float32)


def lane_twiddle(sign, width):
    ka = np.arange(32)[:, None]
    lc = (np.arange(width) % 128)[None, :]
    ang = sign * 2.0 * np.pi * (ka * lc) / 4096.0
    return np.cos(ang).astype(np.float32), np.sin(ang).astype(np.float32)


def cmul(ar, ai, br, bi):
    return ar * br - ai * bi, ar * bi + ai * br


def column_forward_kernel(blk_ref, hist_ref, t1c, t1s, t2c, t2s, lr_ref, li_ref, pac, pas, pbc, pbs,
                          out_ref, xs_ref):
    for p in range(2):
        xr, xi = [], []
        for t in range(32):
            if t < 8:
                xr.append(hist_ref[p, 0, :, t * 128:(t + 1) * 128])
                xi.append(hist_ref[p, 1, :, t * 128:(t + 1) * 128])
            else:
                xr.append(blk_ref[p, 0, :, (t - 8) * 128:(t - 7) * 128])
                xi.append(blk_ref[p, 1, :, (t - 8) * 128:(t - 7) * 128])
        ar, ai = fft_list(xr, xi, -1)
        for k in range(32):
            wc, ws = cmul(t1c[k:k + 1, :], t1s[k:k + 1, :], t2c[:, k:k + 1], t2s[:, k:k + 1])
            re, im = cmul(ar[k], ai[k], wc, ws)
            xs_ref[k * 32:(k + 1) * 32, p * 256:p * 256 + 128] = re
            xs_ref[k * 32:(k + 1) * 32, p * 256 + 128:p * 256 + 256] = im
    dims = (((1,), (1,)), ((), ()))
    for h in range(2):
        x = xs_ref[512 * h:512 * (h + 1), :]
        ore = lax.dot_general(lr_ref[...], x, dims, precision=HIGHEST, preferred_element_type=F32)
        oim = lax.dot_general(li_ref[...], x, dims, precision=HIGHEST, preferred_element_type=F32)
        ac = pac[:, 512 * h:512 * (h + 1)]
        as_ = pas[:, 512 * h:512 * (h + 1)]
        for d in range(32):
            bc = pbc[d:d + 1, 512 * h:512 * (h + 1)]
            bs = pbs[d:d + 1, 512 * h:512 * (h + 1)]
            wc, ws = cmul(ac, as_, bc, bs)
            re, im = cmul(ore[8 * d:8 * d + 8], oim[8 * d:8 * d + 8], wc, ws)
            out_ref[8 * d:8 * d + 8, 1024 * h:1024 * h + 512] = re
            out_ref[8 * d:8 * d + 8, 1024 * h + 512:1024 * h + 1024] = im


def row_kernel(x_ref, twc_ref, tws_ref, bf_ref, bb_ref, chc_ref, chs_ref, pc_ref, ps_ref, out_ref, y_ref, w_ref):
    for h in range(2):
        row_half(h, x_ref, twc_ref, tws_ref, bf_ref, bb_ref, chc_ref, chs_ref, pc_ref, ps_ref, out_ref, y_ref, w_ref)


def row_half(h, x_ref, twc_ref, tws_ref, bf_ref, bb_ref, chc_ref, chs_ref, pc_ref, ps_ref, out_ref, y_ref, w_ref):
    base = 1024 * h
    lanes = slice(512 * h, 512 * (h + 1))
    er = [x_ref[8 * d:8 * d + 8, base:base + 512] for d in range(32)]
    ei = [x_ref[8 * d:8 * d + 8, base + 512:base + 1024] for d in range(32)]
    fr, fi = fft_list(er, ei, -1)
    for g in range(32):
        a, b = cmul(fr[g], fi[g], twc_ref[g:g + 1, :], tws_ref[g:g + 1, :])
        for j in range(4):
            y_ref[256 * j + 8 * g:256 * j + 8 * g + 8, 0:128] = a[:, 128 * j:128 * (j + 1)]
            y_ref[256 * j + 8 * g:256 * j + 8 * g + 8, 128:256] = b[:, 128 * j:128 * (j + 1)]
    z = jnp.dot(y_ref[...], bf_ref[...], precision=HIGHEST, preferred_element_type=F32)
    re, im = cmul(z[:, 0:128], z[:, 128:256], chc_ref[1024 * h:1024 * (h + 1), :], chs_ref[1024 * h:1024 * (h + 1), :])
    y_ref[:, 0:128] = re
    y_ref[:, 128:256] = im
    w_ref[...] = jnp.dot(y_ref[...], bb_ref[...], precision=HIGHEST, preferred_element_type=F32)
    gr, gi = [], []
    for g in range(32):
        a = jnp.concatenate([w_ref[256 * j + 8 * g:256 * j + 8 * g + 8, 0:128] for j in range(4)], axis=1)
        b = jnp.concatenate([w_ref[256 * j + 8 * g:256 * j + 8 * g + 8, 128:256] for j in range(4)], axis=1)
        a, b = cmul(a, b, twc_ref[g:g + 1, :], -tws_ref[g:g + 1, :])
        gr.append(a)
        gi.append(b)
    ur, ui = fft_list(gr, gi, 1)
    for d in range(32):
        re, im = cmul(ur[d], ui[d], pc_ref[8 * d:8 * d + 8, lanes], ps_ref[8 * d:8 * d + 8, lanes])
        out_ref[8 * d:8 * d + 8, base:base + 512] = re
        out_ref[8 * d:8 * d + 8, base + 512:base + 1024] = im


def column_inverse_kernel(x_ref, m_ref, twc_ref, tws_ref, out_ref, s_ref):
    lhs_re = jnp.concatenate([x_ref[:, 0:512].T, x_ref[:, 1024:1536].T], axis=0)
    lhs_im = jnp.concatenate([x_ref[:, 512:1024].T, x_ref[:, 1536:2048].T], axis=0)
    lhs = jnp.concatenate([lhs_re, lhs_im], axis=1)
    s_ref[...] = jnp.dot(lhs, m_ref[...], precision=HIGHEST, preferred_element_type=F32)
    er, ei = [], []
    for k in range(32):
        rows = slice(32 * k, 32 * (k + 1))
        a = jnp.concatenate([s_ref[rows, 0:128], s_ref[rows, 256:384]], axis=1)
        b = jnp.concatenate([s_ref[rows, 128:256], s_ref[rows, 384:512]], axis=1)
        a, b = cmul(a, b, twc_ref[k:k + 1, :], tws_ref[k:k + 1, :])
        er.append(a)
        ei.append(b)
    tr, ti = fft_list(er, ei, 1)
    for t in range(8, 32):
        for p in range(2):
            out_ref[p, 0, :, (t - 8) * 128:(t - 7) * 128] = tr[t][:, 128 * p:128 * (p + 1)]
            out_ref[p, 1, :, (t - 8) * 128:(t - 7) * 128] = ti[t][:, 128 * p:128 * (p + 1)]


def call(kernel, out_shapes, scratch, *args):
    return pl.pallas_call(
        kernel,
        out_shape=[jax.ShapeDtypeStruct(s, F32) for s in out_shapes],
        scratch_shapes=[pltpu.VMEM(s, F32) for s in scratch],
        interpret=INTERPRET,
    )(*args)


def exchanged(block):
    rows, width = block.shape
    out = lax.all_to_all(block.reshape(32, rows // 32, width), "band", 0, 0, tiled=True)
    return out.reshape(rows, width)


def arranged(table):
    table = table.reshape(32, 32, 4, 8, 4).transpose(3, 1, 2, 4, 0)
    return jnp.broadcast_to(table[:, :, None], (8, 32, 2, 4, 4, 32)).reshape(2048, 128)


def per_device(voltages, chirp_phase):
    block = voltages[0, 0]
    band = lax.axis_index("band")
    history = passed_along(block[..., 3072 - HIST:], "seg", 1)

    i32 = jnp.int32
    lane = jnp.arange(1024, dtype=i32)[None, :]
    r_lane = 32 * band + lane % 32
    ka_lane = lane // 32
    t2c, t2s = unit(jnp.arange(32, dtype=i32)[None, :] * (32 * band + jnp.arange(32, dtype=i32)[:, None]), LENGTH, -1)
    q = jnp.arange(8, dtype=i32)[:, None]
    dd = jnp.arange(32, dtype=i32)[:, None]
    pac, pas = unit(32 * r_lane * (q % 4), LENGTH, -1)
    pbc, pbs = unit(128 * r_lane * dd, LENGTH, -1)
    kc_lane = 128 * band + ka_lane
    rl_lane = lane % 32
    rows = jnp.arange(256, dtype=i32)[:, None]

    t1c, t1s = lane_twiddle(-1, 128)
    lr, li = send_matrices()
    (send,) = call(column_forward_kernel, [(256, 2048)], [(1024, 512)],
                   block, history, jnp.asarray(t1c), jnp.asarray(t1s), t2c, t2s,
                   jnp.asarray(lr), jnp.asarray(li), pac, pas, pbc, pbs)
    received = exchanged(send)

    chirp_phase, send = lax.optimization_barrier((chirp_phase, send))
    ch_c, ch_s = [arranged(gathered(f(chirp_phase), "seg", 1)[0]) for f in (jnp.cos, jnp.sin)]
    back_c, back_s = unit((32 * (rows // 8) + lane % 32) * (kc_lane + 32 * (rows % 4)), LENGTH, 1)

    twc, tws = row_twiddle(-1)
    (sent,) = call(row_kernel, [(256, 2048)], [(1024, 256), (1024, 256)],
                   received, jnp.asarray(twc), jnp.asarray(tws), jnp.asarray(row_block(-1)),
                   jnp.asarray(row_block(1)), ch_c, ch_s, back_c, back_s)
    returned = exchanged(sent)

    cc, cs = lane_twiddle(1, 256)
    (out,) = call(column_inverse_kernel, [(2, 2, ROWS_DEV, 3072)], [(1024, 512)],
                  returned, jnp.asarray(receive_matrix()), jnp.asarray(cc), jnp.asarray(cs))
    return out[None, None]


def solution(mesh):
    in_specs = (P("seg", None, None, None, "band", None), P(None, "seg", "band"))
    out_specs = P("seg", None, None, None, "band", None)
    return jax.shard_map(
        per_device, mesh=mesh, in_specs=in_specs, out_specs=out_specs, check_vma=False
    )
```

```python
import math

import numpy as np
import jax
import jax.numpy as jnp
from jax import lax
from jax.experimental import pallas as pl
from jax.experimental.pallas import tpu as pltpu
from jax.sharding import PartitionSpec as P

INTERPRET = False
HIGHEST = lax.Precision.HIGHEST
F32 = jnp.float32
ROWS_DEV = 32
COLS = 4096
HIST = 1024
LENGTH = 1024 * 4096


def passed_along(block, axis, distance):
    devices = range(lax.axis_size(axis))
    route = [(i - distance, i) for i in devices if i - distance in devices]
    return lax.ppermute(block, axis, route)


def gathered(block, axis, dim):
    size = lax.axis_size(axis)
    pieces = [block]
    for shift in range(1, size):
        route = [((i + shift) % size, i) for i in range(size)]
        pieces.append(lax.ppermute(block, axis, route))
    ahead = jnp.stack(pieces, axis=0)
    ordered = jnp.roll(ahead, lax.axis_index(axis), axis=0)
    ordered = jnp.moveaxis(ordered, 0, dim)
    shape = list(block.shape)
    shape[dim] *= size
    return ordered.reshape(shape)


def fft_list(xr, xi, sign):
    n = len(xr)
    if n == 1:
        return list(xr), list(xi)
    er, ei = fft_list(xr[0::2], xi[0::2], sign)
    odd_r, odd_i = fft_list(xr[1::2], xi[1::2], sign)
    half = n // 2
    outr = [None] * n
    outi = [None] * n
    for k in range(half):
        a, b = odd_r[k], odd_i[k]
        if k == 0:
            tr, ti = a, b
        elif 4 * k == n:
            tr, ti = (-b, a) if sign > 0 else (b, -a)
        else:
            angle = sign * 2.0 * math.pi * k / n
            c, s = math.cos(angle), math.sin(angle)
            tr = a * c - b * s
            ti = a * s + b * c
        outr[k] = er[k] + tr
        outi[k] = ei[k] + ti
        outr[k + half] = er[k] - tr
        outi[k + half] = ei[k] - ti
    return outr, outi


BF16 = jnp.bfloat16


def split(x):
    hi = x.astype(BF16)
    return hi, (x - hi.astype(F32)).astype(BF16)


def dot3(a, b_hi, b_lo, dims=(((1,), (0,)), ((), ())), a_first=True):
    a_hi, a_lo = split(a)
    def one(x, y):
        if a_first:
            return lax.dot_general(x, y, dims, preferred_element_type=F32)
        return lax.dot_general(y, x, dims, preferred_element_type=F32)
    return one(a_hi, b_hi) + (one(a_lo, b_hi) + one(a_hi, b_lo))


def halves(m):
    hi = m.astype(BF16)
    lo = (m - hi.astype(np.float32)).astype(BF16)
    return jnp.asarray(hi), jnp.asarray(lo)


def unit(m, n, sign):
    angle = (m % n).astype(F32) * F32(sign * 2.0 * math.pi / n)
    return jnp.cos(angle), jnp.sin(angle)


def send_matrices():
    row = np.arange(256)
    dd, pp, ks = row // 8, (row // 4) % 2, row % 4
    k2 = 4 * dd + ks
    col = np.arange(512)
    pin, riin, lane = col // 256, (col // 128) % 2, col % 128
    ang = -2.0 * np.pi * np.outer(k2, lane) / 128.0
    c, s = np.cos(ang), np.sin(ang)
    same = (pp[:, None] == pin[None, :])
    real = np.where(riin[None, :] == 0, c, -s) * same
    imag = np.where(riin[None, :] == 0, s, c) * same
    return real.astype(np.float32), imag.astype(np.float32)


def row_block(sign):
    idx = np.arange(128)
    q, r = idx // 32, idx % 32
    ang = sign * 2.0 * np.pi * np.outer(r, r) / 32.0
    same = q[:, None] == q[None, :]
    wr = np.cos(ang) * same
    wi = np.sin(ang) * same
    top = np.concatenate([wr, wi], axis=1)
    bottom = np.concatenate([-wi, wr], axis=1)
    return np.concatenate([top, bottom], axis=0).astype(np.float32)


def row_twiddle(sign):
    g = np.arange(32)[:, None]
    r = (np.arange(512) % 32)[None, :]
    ang = sign * 2.0 * np.pi * (g * r) / 1024.0
    return np.cos(ang).astype(np.float32), np.sin(ang).astype(np.float32)


def receive_matrix():
    row = np.arange(512)
    riin, dd, pp, ks = row // 256, (row // 8) % 32, (row // 4) % 2, row % 4
    k2 = 4 * dd + ks
    col = np.arange(512)
    pout, riout, lc = col // 256, (col // 128) % 2, col % 128
    ang = 2.0 * np.pi * np.outer(k2, lc) / 128.0
    c, s = np.cos(ang), np.sin(ang)
    same = pp[:, None] == pout[None, :]
    val = np.where(riin[:, None] == 0,
                   np.where(riout[None, :] == 0, c, s),
                   np.where(riout[None, :] == 0, -s, c))
    return (val * same / LENGTH).astype(np.float32)


def lane_twiddle(sign, width):
    ka = np.arange(32)[:, None]
    lc = (np.arange(width) % 128)[None, :]
    ang = sign * 2.0 * np.pi * (ka * lc) / 4096.0
    return np.cos(ang).astype(np.float32), np.sin(ang).astype(np.float32)


def cmul(ar, ai, br, bi):
    return ar * br - ai * bi, ar * bi + ai * br


def column_forward_kernel(blk_ref, hist_ref, t1c, t1s, t2c, t2s, lrh, lrl, lih, lil, pac, pas, pbc, pbs,
                          out_ref, xs_ref):
    for p in range(2):
        xr, xi = [], []
        for t in range(32):
            if t < 8:
                xr.append(hist_ref[p, 0, :, t * 128:(t + 1) * 128])
                xi.append(hist_ref[p, 1, :, t * 128:(t + 1) * 128])
            else:
                xr.append(blk_ref[p, 0, :, (t - 8) * 128:(t - 7) * 128])
                xi.append(blk_ref[p, 1, :, (t - 8) * 128:(t - 7) * 128])
        ar, ai = fft_list(xr, xi, -1)
        for k in range(32):
            wc, ws = cmul(t1c[k:k + 1, :], t1s[k:k + 1, :], t2c[:, k:k + 1], t2s[:, k:k + 1])
            re, im = cmul(ar[k], ai[k], wc, ws)
            xs_ref[k * 32:(k + 1) * 32, p * 256:p * 256 + 128] = re
            xs_ref[k * 32:(k + 1) * 32, p * 256 + 128:p * 256 + 256] = im
    dims = (((1,), (1,)), ((), ()))
    for h in range(2):
        x = xs_ref[512 * h:512 * (h + 1), :]
        ore = dot3(x, lrh[...], lrl[...], dims, a_first=False)
        oim = dot3(x, lih[...], lil[...], dims, a_first=False)
        ac = pac[:, 512 * h:512 * (h + 1)]
        as_ = pas[:, 512 * h:512 * (h + 1)]
        for d in range(32):
            bc = pbc[d:d + 1, 512 * h:512 * (h + 1)]
            bs = pbs[d:d + 1, 512 * h:512 * (h + 1)]
            wc, ws = cmul(ac, as_, bc, bs)
            re, im = cmul(ore[8 * d:8 * d + 8], oim[8 * d:8 * d + 8], wc, ws)
            out_ref[8 * d:8 * d + 8, 1024 * h:1024 * h + 512] = re
            out_ref[8 * d:8 * d + 8, 1024 * h + 512:1024 * h + 1024] = im


def row_kernel(x_ref, twc_ref, tws_ref, bfh, bfl, bbh, bbl, ph_ref, pc_ref, ps_ref, out_ref, y_ref, w_ref):
    for h in range(2):
        row_half(h, x_ref, twc_ref, tws_ref, bfh, bfl, bbh, bbl, ph_ref, pc_ref, ps_ref, out_ref, y_ref, w_ref)


def row_half(h, x_ref, twc_ref, tws_ref, bfh, bfl, bbh, bbl, ph_ref, pc_ref, ps_ref, out_ref, y_ref, w_ref):
    base = 1024 * h
    lanes = slice(512 * h, 512 * (h + 1))
    er = [x_ref[8 * d:8 * d + 8, base:base + 512] for d in range(32)]
    ei = [x_ref[8 * d:8 * d + 8, base + 512:base + 1024] for d in range(32)]
    fr, fi = fft_list(er, ei, -1)
    for g in range(32):
        a, b = cmul(fr[g], fi[g], twc_ref[g:g + 1, :], tws_ref[g:g + 1, :])
        for j in range(4):
            y_ref[256 * j + 8 * g:256 * j + 8 * g + 8, 0:128] = a[:, 128 * j:128 * (j + 1)]
            y_ref[256 * j + 8 * g:256 * j + 8 * g + 8, 128:256] = b[:, 128 * j:128 * (j + 1)]
    z = dot3(y_ref[...], bfh[...], bfl[...])
    phase = ph_ref[1024 * h:1024 * (h + 1), :]
    re, im = cmul(z[:, 0:128], z[:, 128:256], jnp.cos(phase), jnp.sin(phase))
    y_ref[:, 0:128] = re
    y_ref[:, 128:256] = im
    w_ref[...] = dot3(y_ref[...], bbh[...], bbl[...])
    gr, gi = [], []
    for g in range(32):
        a = jnp.concatenate([w_ref[256 * j + 8 * g:256 * j + 8 * g + 8, 0:128] for j in range(4)], axis=1)
        b = jnp.concatenate([w_ref[256 * j + 8 * g:256 * j + 8 * g + 8, 128:256] for j in range(4)], axis=1)
        a, b = cmul(a, b, twc_ref[g:g + 1, :], -tws_ref[g:g + 1, :])
        gr.append(a)
        gi.append(b)
    ur, ui = fft_list(gr, gi, 1)
    for d in range(32):
        re, im = cmul(ur[d], ui[d], pc_ref[8 * d:8 * d + 8, lanes], ps_ref[8 * d:8 * d + 8, lanes])
        out_ref[8 * d:8 * d + 8, base:base + 512] = re
        out_ref[8 * d:8 * d + 8, base + 512:base + 1024] = im


def column_inverse_kernel(x_ref, mh_ref, ml_ref, twc_ref, tws_ref, out_ref, s_ref):
    lhs_re = jnp.concatenate([x_ref[:, 0:512].T, x_ref[:, 1024:1536].T], axis=0)
    lhs_im = jnp.concatenate([x_ref[:, 512:1024].T, x_ref[:, 1536:2048].T], axis=0)
    lhs = jnp.concatenate([lhs_re, lhs_im], axis=1)
    s_ref[...] = dot3(lhs, mh_ref[...], ml_ref[...])
    er, ei = [], []
    for k in range(32):
        rows = slice(32 * k, 32 * (k + 1))
        a = jnp.concatenate([s_ref[rows, 0:128], s_ref[rows, 256:384]], axis=1)
        b = jnp.concatenate([s_ref[rows, 128:256], s_ref[rows, 384:512]], axis=1)
        a, b = cmul(a, b, twc_ref[k:k + 1, :], tws_ref[k:k + 1, :])
        er.append(a)
        ei.append(b)
    tr, ti = fft_list(er, ei, 1)
    for t in range(8, 32):
        for p in range(2):
            out_ref[p, 0, :, (t - 8) * 128:(t - 7) * 128] = tr[t][:, 128 * p:128 * (p + 1)]
            out_ref[p, 1, :, (t - 8) * 128:(t - 7) * 128] = ti[t][:, 128 * p:128 * (p + 1)]


def call(kernel, out_shapes, scratch, *args):
    return pl.pallas_call(
        kernel,
        out_shape=[jax.ShapeDtypeStruct(s, F32) for s in out_shapes],
        scratch_shapes=[pltpu.VMEM(s, F32) for s in scratch],
        interpret=INTERPRET,
    )(*args)


def exchanged(block):
    rows, width = block.shape
    out = lax.all_to_all(block.reshape(32, rows // 32, width), "band", 0, 0, tiled=True)
    return out.reshape(rows, width)


def arranged(table):
    table = table.reshape(32, 32, 4, 8, 4).transpose(3, 1, 2, 4, 0)
    return jnp.broadcast_to(table[:, :, None], (8, 32, 2, 4, 4, 32)).reshape(2048, 128)


def per_device(voltages, chirp_phase):
    block = voltages[0, 0]
    band = lax.axis_index("band")
    history = passed_along(block[..., 3072 - HIST:], "seg", 1)

    i32 = jnp.int32
    lane = jnp.arange(1024, dtype=i32)[None, :]
    r_lane = 32 * band + lane % 32
    ka_lane = lane // 32
    t2c, t2s = unit(jnp.arange(32, dtype=i32)[None, :] * (32 * band + jnp.arange(32, dtype=i32)[:, None]), LENGTH, -1)
    q = jnp.arange(8, dtype=i32)[:, None]
    dd = jnp.arange(32, dtype=i32)[:, None]
    pac, pas = unit(32 * r_lane * (q % 4), LENGTH, -1)
    pbc, pbs = unit(128 * r_lane * dd, LENGTH, -1)
    kc_lane = 128 * band + ka_lane
    rl_lane = lane % 32
    rows = jnp.arange(256, dtype=i32)[:, None]

    t1c, t1s = lane_twiddle(-1, 128)
    lr, li = send_matrices()
    (send,) = call(column_forward_kernel, [(256, 2048)], [(1024, 512)],
                   block, history, jnp.asarray(t1c), jnp.asarray(t1s), t2c, t2s,
                   *halves(lr), *halves(li), pac, pas, pbc, pbs)
    received = exchanged(send)

    chirp_phase, send = lax.optimization_barrier((chirp_phase, send))
    chirp = arranged(gathered(chirp_phase, "seg", 1)[0])
    back_c, back_s = unit((32 * (rows // 8) + lane % 32) * (kc_lane + 32 * (rows % 4)), LENGTH, 1)

    twc, tws = row_twiddle(-1)
    (sent,) = call(row_kernel, [(256, 2048)], [(1024, 256), (1024, 256)],
                   received, jnp.asarray(twc), jnp.asarray(tws), *halves(row_block(-1)),
                   *halves(row_block(1)), chirp, back_c, back_s)
    returned = exchanged(sent)

    cc, cs = lane_twiddle(1, 256)
    (out,) = call(column_inverse_kernel, [(2, 2, ROWS_DEV, 3072)], [(1024, 512)],
                  returned, *halves(receive_matrix()), jnp.asarray(cc), jnp.asarray(cs))
    return out[None, None]


def solution(mesh):
    in_specs = (P("seg", None, None, None, "band", None), P(None, "seg", "band"))
    out_specs = P("seg", None, None, None, "band", None)
    return jax.shard_map(
        per_device, mesh=mesh, in_specs=in_specs, out_specs=out_specs, check_vma=False
    )
```

```python
import math

import numpy as np
import jax
import jax.numpy as jnp
from jax import lax
from jax.experimental import pallas as pl
from jax.experimental.pallas import tpu as pltpu
from jax.sharding import PartitionSpec as P

INTERPRET = False
HIGHEST = lax.Precision.HIGHEST
F32 = jnp.float32
ROWS_DEV = 32
COLS = 4096
HIST = 1024
LENGTH = 1024 * 4096


def passed_along(block, axis, distance):
    devices = range(lax.axis_size(axis))
    route = [(i - distance, i) for i in devices if i - distance in devices]
    return lax.ppermute(block, axis, route)


def gathered(block, axis, dim):
    size = lax.axis_size(axis)
    pieces = [block]
    for shift in range(1, size):
        route = [((i + shift) % size, i) for i in range(size)]
        pieces.append(lax.ppermute(block, axis, route))
    ahead = jnp.stack(pieces, axis=0)
    ordered = jnp.roll(ahead, lax.axis_index(axis), axis=0)
    ordered = jnp.moveaxis(ordered, 0, dim)
    shape = list(block.shape)
    shape[dim] *= size
    return ordered.reshape(shape)


def fft_list(xr, xi, sign):
    n = len(xr)
    if n == 1:
        return list(xr), list(xi)
    er, ei = fft_list(xr[0::2], xi[0::2], sign)
    odd_r, odd_i = fft_list(xr[1::2], xi[1::2], sign)
    half = n // 2
    outr = [None] * n
    outi = [None] * n
    for k in range(half):
        a, b = odd_r[k], odd_i[k]
        if k == 0:
            tr, ti = a, b
        elif 4 * k == n:
            tr, ti = (-b, a) if sign > 0 else (b, -a)
        else:
            angle = sign * 2.0 * math.pi * k / n
            c, s = math.cos(angle), math.sin(angle)
            tr = a * c - b * s
            ti = a * s + b * c
        outr[k] = er[k] + tr
        outi[k] = ei[k] + ti
        outr[k + half] = er[k] - tr
        outi[k + half] = ei[k] - ti
    return outr, outi


BF16 = jnp.bfloat16


def split(x):
    hi = x.astype(BF16)
    return hi, (x - hi.astype(F32)).astype(BF16)


def dot3(a, b_hi, b_lo, dims=(((1,), (0,)), ((), ())), a_first=True):
    a_hi, a_lo = split(a)
    def one(x, y):
        if a_first:
            return lax.dot_general(x, y, dims, preferred_element_type=F32)
        return lax.dot_general(y, x, dims, preferred_element_type=F32)
    return one(a_hi, b_hi) + (one(a_lo, b_hi) + one(a_hi, b_lo))


def halves(m):
    hi = m.astype(BF16)
    lo = (m - hi.astype(np.float32)).astype(BF16)
    return jnp.asarray(hi), jnp.asarray(lo)


def unit(m, n, sign):
    angle = (m % n).astype(F32) * F32(sign * 2.0 * math.pi / n)
    return jnp.cos(angle), jnp.sin(angle)


def send_matrices():
    row = np.arange(256)
    dd, pp, ks = row // 8, (row // 4) % 2, row % 4
    k2 = 4 * dd + ks
    col = np.arange(512)
    pin, riin, lane = col // 256, (col // 128) % 2, col % 128
    ang = -2.0 * np.pi * np.outer(k2, lane) / 128.0
    c, s = np.cos(ang), np.sin(ang)
    same = (pp[:, None] == pin[None, :])
    real = np.where(riin[None, :] == 0, c, -s) * same
    imag = np.where(riin[None, :] == 0, s, c) * same
    return real.astype(np.float32), imag.astype(np.float32)


def row_block(sign):
    idx = np.arange(128)
    q, r = idx // 32, idx % 32
    ang = sign * 2.0 * np.pi * np.outer(r, r) / 32.0
    same = q[:, None] == q[None, :]
    wr = np.cos(ang) * same
    wi = np.sin(ang) * same
    top = np.concatenate([wr, wi], axis=1)
    bottom = np.concatenate([-wi, wr], axis=1)
    return np.concatenate([top, bottom], axis=0).astype(np.float32)


def row_twiddle(sign):
    g = np.arange(32)[:, None]
    r = (np.arange(512) % 32)[None, :]
    ang = sign * 2.0 * np.pi * (g * r) / 1024.0
    return np.cos(ang).astype(np.float32), np.sin(ang).astype(np.float32)


def receive_matrix():
    row = np.arange(512)
    riin, dd, pp, ks = row // 256, (row // 8) % 32, (row // 4) % 2, row % 4
    k2 = 4 * dd + ks
    col = np.arange(512)
    pout, riout, lc = col // 256, (col // 128) % 2, col % 128
    ang = 2.0 * np.pi * np.outer(k2, lc) / 128.0
    c, s = np.cos(ang), np.sin(ang)
    same = pp[:, None] == pout[None, :]
    val = np.where(riin[:, None] == 0,
                   np.where(riout[None, :] == 0, c, s),
                   np.where(riout[None, :] == 0, -s, c))
    return (val * same / LENGTH).astype(np.float32)


def lane_twiddle(sign, width):
    ka = np.arange(32)[:, None]
    lc = (np.arange(width) % 128)[None, :]
    ang = sign * 2.0 * np.pi * (ka * lc) / 4096.0
    return np.cos(ang).astype(np.float32), np.sin(ang).astype(np.float32)


def cmul(ar, ai, br, bi):
    return ar * br - ai * bi, ar * bi + ai * br


def column_forward_kernel(blk_ref, hist_ref, t1c, t1s, t2c, t2s, lrh, lrl, lih, lil, pac, pas, pbc, pbs,
                          out_ref, xs_ref):
    for p in range(2):
        xr, xi = [], []
        for t in range(32):
            if t < 8:
                xr.append(hist_ref[p, 0, :, t * 128:(t + 1) * 128])
                xi.append(hist_ref[p, 1, :, t * 128:(t + 1) * 128])
            else:
                xr.append(blk_ref[p, 0, :, (t - 8) * 128:(t - 7) * 128])
                xi.append(blk_ref[p, 1, :, (t - 8) * 128:(t - 7) * 128])
        ar, ai = fft_list(xr, xi, -1)
        for k in range(32):
            wc, ws = cmul(t1c[k:k + 1, :], t1s[k:k + 1, :], t2c[:, k:k + 1], t2s[:, k:k + 1])
            re, im = cmul(ar[k], ai[k], wc, ws)
            xs_ref[k * 32:(k + 1) * 32, p * 256:p * 256 + 128] = re
            xs_ref[k * 32:(k + 1) * 32, p * 256 + 128:p * 256 + 256] = im
    dims = (((1,), (1,)), ((), ()))
    for h in range(2):
        x = xs_ref[512 * h:512 * (h + 1), :]
        ore = dot3(x, lrh[...], lrl[...], dims, a_first=False)
        oim = dot3(x, lih[...], lil[...], dims, a_first=False)
        ac = pac[:, 512 * h:512 * (h + 1)]
        as_ = pas[:, 512 * h:512 * (h + 1)]
        for d in range(32):
            bc = pbc[d:d + 1, 512 * h:512 * (h + 1)]
            bs = pbs[d:d + 1, 512 * h:512 * (h + 1)]
            wc, ws = cmul(ac, as_, bc, bs)
            re, im = cmul(ore[8 * d:8 * d + 8], oim[8 * d:8 * d + 8], wc, ws)
            out_ref[8 * d:8 * d + 8, 1024 * h:1024 * h + 512] = re
            out_ref[8 * d:8 * d + 8, 1024 * h + 512:1024 * h + 1024] = im


def row_kernel(x_ref, twc_ref, tws_ref, bfh, bfl, bbh, bbl, chc_ref, chs_ref, pc_ref, ps_ref, out_ref, y_ref, w_ref):
    for h in range(2):
        row_half(h, x_ref, twc_ref, tws_ref, bfh, bfl, bbh, bbl, chc_ref, chs_ref, pc_ref, ps_ref, out_ref, y_ref, w_ref)


def row_half(h, x_ref, twc_ref, tws_ref, bfh, bfl, bbh, bbl, chc_ref, chs_ref, pc_ref, ps_ref, out_ref, y_ref, w_ref):
    base = 1024 * h
    lanes = slice(512 * h, 512 * (h + 1))
    er = [x_ref[8 * d:8 * d + 8, base:base + 512] for d in range(32)]
    ei = [x_ref[8 * d:8 * d + 8, base + 512:base + 1024] for d in range(32)]
    fr, fi = fft_list(er, ei, -1)
    for g in range(32):
        a, b = cmul(fr[g], fi[g], twc_ref[g:g + 1, :], tws_ref[g:g + 1, :])
        for p in range(2):
            for j in range(4):
                at = 512 * p + 128 * j + 4 * g
                y_ref[at:at + 4, 0:128] = a[4 * p:4 * p + 4, 128 * j:128 * (j + 1)]
                y_ref[at:at + 4, 128:256] = b[4 * p:4 * p + 4, 128 * j:128 * (j + 1)]
    z = dot3(y_ref[...], bfh[...], bfl[...])
    c = chc_ref[512 * h:512 * (h + 1), :]
    s = chs_ref[512 * h:512 * (h + 1), :]
    for p in range(2):
        rows = slice(512 * p, 512 * (p + 1))
        re, im = cmul(z[rows, 0:128], z[rows, 128:256], c, s)
        y_ref[rows, 0:128] = re
        y_ref[rows, 128:256] = im
    w_ref[...] = dot3(y_ref[...], bbh[...], bbl[...])
    gr, gi = [], []
    for g in range(32):
        pa, pb = [], []
        for j in range(4):
            lo, hi = 128 * j + 4 * g, 512 + 128 * j + 4 * g
            pa.append(jnp.concatenate([w_ref[lo:lo + 4, 0:128], w_ref[hi:hi + 4, 0:128]], axis=0))
            pb.append(jnp.concatenate([w_ref[lo:lo + 4, 128:256], w_ref[hi:hi + 4, 128:256]], axis=0))
        a, b = cmul(jnp.concatenate(pa, axis=1), jnp.concatenate(pb, axis=1), twc_ref[g:g + 1, :], -tws_ref[g:g + 1, :])
        gr.append(a)
        gi.append(b)
    ur, ui = fft_list(gr, gi, 1)
    for d in range(32):
        re, im = cmul(ur[d], ui[d], pc_ref[8 * d:8 * d + 8, lanes], ps_ref[8 * d:8 * d + 8, lanes])
        out_ref[8 * d:8 * d + 8, base:base + 512] = re
        out_ref[8 * d:8 * d + 8, base + 512:base + 1024] = im


def column_inverse_kernel(x_ref, mh_ref, ml_ref, twc_ref, tws_ref, out_ref, s_ref):
    lhs_re = jnp.concatenate([x_ref[:, 0:512].T, x_ref[:, 1024:1536].T], axis=0)
    lhs_im = jnp.concatenate([x_ref[:, 512:1024].T, x_ref[:, 1536:2048].T], axis=0)
    lhs = jnp.concatenate([lhs_re, lhs_im], axis=1)
    s_ref[...] = dot3(lhs, mh_ref[...], ml_ref[...])
    er, ei = [], []
    for k in range(32):
        rows = slice(32 * k, 32 * (k + 1))
        a = jnp.concatenate([s_ref[rows, 0:128], s_ref[rows, 256:384]], axis=1)
        b = jnp.concatenate([s_ref[rows, 128:256], s_ref[rows, 384:512]], axis=1)
        a, b = cmul(a, b, twc_ref[k:k + 1, :], tws_ref[k:k + 1, :])
        er.append(a)
        ei.append(b)
    tr, ti = fft_list(er, ei, 1)
    for t in range(8, 32):
        for p in range(2):
            out_ref[p, 0, :, (t - 8) * 128:(t - 7) * 128] = tr[t][:, 128 * p:128 * (p + 1)]
            out_ref[p, 1, :, (t - 8) * 128:(t - 7) * 128] = ti[t][:, 128 * p:128 * (p + 1)]


def call(kernel, out_shapes, scratch, *args):
    return pl.pallas_call(
        kernel,
        out_shape=[jax.ShapeDtypeStruct(s, F32) for s in out_shapes],
        scratch_shapes=[pltpu.VMEM(s, F32) for s in scratch],
        interpret=INTERPRET,
    )(*args)


def exchanged(block):
    rows, width = block.shape
    out = lax.all_to_all(block.reshape(32, rows // 32, width), "band", 0, 0, tiled=True)
    return out.reshape(rows, width)


def arranged(table):
    return table.reshape(32, 32, 4, 8, 4).transpose(3, 1, 2, 4, 0).reshape(1024, 128)


def per_device(voltages, chirp_phase):
    block = voltages[0, 0]
    band = lax.axis_index("band")
    history = passed_along(block[..., 3072 - HIST:], "seg", 1)

    i32 = jnp.int32
    lane = jnp.arange(1024, dtype=i32)[None, :]
    r_lane = 32 * band + lane % 32
    ka_lane = lane // 32
    t2c, t2s = unit(jnp.arange(32, dtype=i32)[None, :] * (32 * band + jnp.arange(32, dtype=i32)[:, None]), LENGTH, -1)
    q = jnp.arange(8, dtype=i32)[:, None]
    dd = jnp.arange(32, dtype=i32)[:, None]
    pac, pas = unit(32 * r_lane * (q % 4), LENGTH, -1)
    pbc, pbs = unit(128 * r_lane * dd, LENGTH, -1)
    kc_lane = 128 * band + ka_lane
    rl_lane = lane % 32
    rows = jnp.arange(256, dtype=i32)[:, None]

    t1c, t1s = lane_twiddle(-1, 128)
    lr, li = send_matrices()
    (send,) = call(column_forward_kernel, [(256, 2048)], [(1024, 512)],
                   block, history, jnp.asarray(t1c), jnp.asarray(t1s), t2c, t2s,
                   *halves(lr), *halves(li), pac, pas, pbc, pbs)
    received = exchanged(send)

    chirp_phase, send = lax.optimization_barrier((chirp_phase, send))
    phases = gathered(chirp_phase, "seg", 1)[0]
    ch_c, ch_s = arranged(jnp.cos(phases)), arranged(jnp.sin(phases))
    back_c, back_s = unit((32 * (rows // 8) + lane % 32) * (kc_lane + 32 * (rows % 4)), LENGTH, 1)

    twc, tws = row_twiddle(-1)
    (sent,) = call(row_kernel, [(256, 2048)], [(1024, 256), (1024, 256)],
                   received, jnp.asarray(twc), jnp.asarray(tws), *halves(row_block(-1)),
                   *halves(row_block(1)), ch_c, ch_s, back_c, back_s)
    returned = exchanged(sent)

    cc, cs = lane_twiddle(1, 256)
    (out,) = call(column_inverse_kernel, [(2, 2, ROWS_DEV, 3072)], [(1024, 512)],
                  returned, *halves(receive_matrix()), jnp.asarray(cc), jnp.asarray(cs))
    return out[None, None]


def solution(mesh):
    in_specs = (P("seg", None, None, None, "band", None), P(None, "seg", "band"))
    out_specs = P("seg", None, None, None, "band", None)
    return jax.shard_map(
        per_device, mesh=mesh, in_specs=in_specs, out_specs=out_specs, check_vma=False
    )
```

```python
import math

import numpy as np
import jax
import jax.numpy as jnp
from jax import lax
from jax.experimental import pallas as pl
from jax.experimental.pallas import tpu as pltpu
from jax.sharding import PartitionSpec as P

INTERPRET = False
HIGHEST = lax.Precision.HIGHEST
F32 = jnp.float32
ROWS_DEV = 32
COLS = 4096
HIST = 1024
LENGTH = 1024 * 4096


def passed_along(block, axis, distance):
    devices = range(lax.axis_size(axis))
    route = [(i - distance, i) for i in devices if i - distance in devices]
    return lax.ppermute(block, axis, route)


def gathered(block, axis, dim):
    size = lax.axis_size(axis)
    pieces = [block]
    for shift in range(1, size):
        route = [((i + shift) % size, i) for i in range(size)]
        pieces.append(lax.ppermute(block, axis, route))
    ahead = jnp.stack(pieces, axis=0)
    ordered = jnp.roll(ahead, lax.axis_index(axis), axis=0)
    ordered = jnp.moveaxis(ordered, 0, dim)
    shape = list(block.shape)
    shape[dim] *= size
    return ordered.reshape(shape)


def fft_list(xr, xi, sign):
    n = len(xr)
    if n == 1:
        return list(xr), list(xi)
    er, ei = fft_list(xr[0::2], xi[0::2], sign)
    odd_r, odd_i = fft_list(xr[1::2], xi[1::2], sign)
    half = n // 2
    outr = [None] * n
    outi = [None] * n
    for k in range(half):
        a, b = odd_r[k], odd_i[k]
        if k == 0:
            tr, ti = a, b
        elif 4 * k == n:
            tr, ti = (-b, a) if sign > 0 else (b, -a)
        else:
            angle = sign * 2.0 * math.pi * k / n
            c, s = math.cos(angle), math.sin(angle)
            tr = a * c - b * s
            ti = a * s + b * c
        outr[k] = er[k] + tr
        outi[k] = ei[k] + ti
        outr[k + half] = er[k] - tr
        outi[k + half] = ei[k] - ti
    return outr, outi


BF16 = jnp.bfloat16


def split(x):
    hi = x.astype(BF16)
    return hi, (x - hi.astype(F32)).astype(BF16)


def dot3(a, b_hi, b_lo, dims=(((1,), (0,)), ((), ())), a_first=True):
    a_hi, a_lo = split(a)
    def one(x, y):
        if a_first:
            return lax.dot_general(x, y, dims, preferred_element_type=F32)
        return lax.dot_general(y, x, dims, preferred_element_type=F32)
    return one(a_hi, b_hi) + (one(a_lo, b_hi) + one(a_hi, b_lo))


def halves(m):
    hi = m.astype(BF16)
    lo = (m - hi.astype(np.float32)).astype(BF16)
    return jnp.asarray(hi), jnp.asarray(lo)


def unit(m, n, sign):
    angle = (m % n).astype(F32) * F32(sign * 2.0 * math.pi / n)
    return jnp.cos(angle), jnp.sin(angle)


def send_matrices():
    row = np.arange(256)
    dd, pp, ks = row // 8, (row // 4) % 2, row % 4
    k2 = 4 * dd + ks
    col = np.arange(512)
    pin, riin, lane = col // 256, (col // 128) % 2, col % 128
    ang = -2.0 * np.pi * np.outer(k2, lane) / 128.0
    c, s = np.cos(ang), np.sin(ang)
    same = (pp[:, None] == pin[None, :])
    real = np.where(riin[None, :] == 0, c, -s) * same
    imag = np.where(riin[None, :] == 0, s, c) * same
    return real.astype(np.float32), imag.astype(np.float32)


def row_block(sign):
    idx = np.arange(128)
    q, r = idx // 32, idx % 32
    ang = sign * 2.0 * np.pi * np.outer(r, r) / 32.0
    same = q[:, None] == q[None, :]
    wr = np.cos(ang) * same
    wi = np.sin(ang) * same
    top = np.concatenate([wr, wi], axis=1)
    bottom = np.concatenate([-wi, wr], axis=1)
    return np.concatenate([top, bottom], axis=0).astype(np.float32)


def row_twiddle(sign):
    g = np.arange(32)[:, None]
    r = (np.arange(512) % 32)[None, :]
    ang = sign * 2.0 * np.pi * (g * r) / 1024.0
    return np.cos(ang).astype(np.float32), np.sin(ang).astype(np.float32)


def receive_matrix():
    row = np.arange(512)
    riin, dd, pp, ks = row // 256, (row // 8) % 32, (row // 4) % 2, row % 4
    k2 = 4 * dd + ks
    col = np.arange(512)
    pout, riout, lc = col // 256, (col // 128) % 2, col % 128
    ang = 2.0 * np.pi * np.outer(k2, lc) / 128.0
    c, s = np.cos(ang), np.sin(ang)
    same = pp[:, None] == pout[None, :]
    val = np.where(riin[:, None] == 0,
                   np.where(riout[None, :] == 0, c, s),
                   np.where(riout[None, :] == 0, -s, c))
    return (val * same / LENGTH).astype(np.float32)


def lane_twiddle(sign, width):
    ka = np.arange(32)[:, None]
    lc = (np.arange(width) % 128)[None, :]
    ang = sign * 2.0 * np.pi * (ka * lc) / 4096.0
    return np.cos(ang).astype(np.float32), np.sin(ang).astype(np.float32)


def cmul(ar, ai, br, bi):
    return ar * br - ai * bi, ar * bi + ai * br


def column_forward_kernel(blk_ref, hist0_ref, hist1_ref, t1c, t1s, t2c, t2s, lrh, lrl, lih, lil, pac, pas, pbc, pbs,
                          out_ref, xs_ref):
    for p, hist_ref in enumerate((hist0_ref, hist1_ref)):
        xr, xi = [], []
        for t in range(32):
            if t < 8:
                xr.append(hist_ref[0, :, t * 128:(t + 1) * 128])
                xi.append(hist_ref[1, :, t * 128:(t + 1) * 128])
            else:
                xr.append(blk_ref[p, 0, :, (t - 8) * 128:(t - 7) * 128])
                xi.append(blk_ref[p, 1, :, (t - 8) * 128:(t - 7) * 128])
        ar, ai = fft_list(xr, xi, -1)
        for k in range(32):
            wc, ws = cmul(t1c[k:k + 1, :], t1s[k:k + 1, :], t2c[:, k:k + 1], t2s[:, k:k + 1])
            re, im = cmul(ar[k], ai[k], wc, ws)
            xs_ref[k * 32:(k + 1) * 32, p * 256:p * 256 + 128] = re
            xs_ref[k * 32:(k + 1) * 32, p * 256 + 128:p * 256 + 256] = im
    dims = (((1,), (1,)), ((), ()))
    for h in range(2):
        x = xs_ref[512 * h:512 * (h + 1), :]
        ore = dot3(x, lrh[...], lrl[...], dims, a_first=False)
        oim = dot3(x, lih[...], lil[...], dims, a_first=False)
        ac = pac[:, 512 * h:512 * (h + 1)]
        as_ = pas[:, 512 * h:512 * (h + 1)]
        for d in range(32):
            bc = pbc[d:d + 1, 512 * h:512 * (h + 1)]
            bs = pbs[d:d + 1, 512 * h:512 * (h + 1)]
            wc, ws = cmul(ac, as_, bc, bs)
            re, im = cmul(ore[8 * d:8 * d + 8], oim[8 * d:8 * d + 8], wc, ws)
            out_ref[8 * d:8 * d + 8, 1024 * h:1024 * h + 512] = re
            out_ref[8 * d:8 * d + 8, 1024 * h + 512:1024 * h + 1024] = im


def row_kernel(x_ref, twc_ref, tws_ref, bfh, bfl, bbh, bbl, chc_ref, chs_ref, pc_ref, ps_ref, out_ref, y_ref, w_ref):
    for h in range(2):
        row_half(h, x_ref, twc_ref, tws_ref, bfh, bfl, bbh, bbl, chc_ref, chs_ref, pc_ref, ps_ref, out_ref, y_ref, w_ref)


def row_half(h, x_ref, twc_ref, tws_ref, bfh, bfl, bbh, bbl, chc_ref, chs_ref, pc_ref, ps_ref, out_ref, y_ref, w_ref):
    base = 1024 * h
    lanes = slice(512 * h, 512 * (h + 1))
    er = [x_ref[8 * d:8 * d + 8, base:base + 512] for d in range(32)]
    ei = [x_ref[8 * d:8 * d + 8, base + 512:base + 1024] for d in range(32)]
    fr, fi = fft_list(er, ei, -1)
    for g in range(32):
        a, b = cmul(fr[g], fi[g], twc_ref[g:g + 1, :], tws_ref[g:g + 1, :])
        for p in range(2):
            for j in range(4):
                at = 512 * p + 128 * j + 4 * g
                y_ref[at:at + 4, 0:128] = a[4 * p:4 * p + 4, 128 * j:128 * (j + 1)]
                y_ref[at:at + 4, 128:256] = b[4 * p:4 * p + 4, 128 * j:128 * (j + 1)]
    z = dot3(y_ref[...], bfh[...], bfl[...])
    c = chc_ref[512 * h:512 * (h + 1), :]
    s = chs_ref[512 * h:512 * (h + 1), :]
    for p in range(2):
        rows = slice(512 * p, 512 * (p + 1))
        re, im = cmul(z[rows, 0:128], z[rows, 128:256], c, s)
        y_ref[rows, 0:128] = re
        y_ref[rows, 128:256] = im
    w_ref[...] = dot3(y_ref[...], bbh[...], bbl[...])
    gr, gi = [], []
    for g in range(32):
        pa, pb = [], []
        for j in range(4):
            lo, hi = 128 * j + 4 * g, 512 + 128 * j + 4 * g
            pa.append(jnp.concatenate([w_ref[lo:lo + 4, 0:128], w_ref[hi:hi + 4, 0:128]], axis=0))
            pb.append(jnp.concatenate([w_ref[lo:lo + 4, 128:256], w_ref[hi:hi + 4, 128:256]], axis=0))
        a, b = cmul(jnp.concatenate(pa, axis=1), jnp.concatenate(pb, axis=1), twc_ref[g:g + 1, :], -tws_ref[g:g + 1, :])
        gr.append(a)
        gi.append(b)
    ur, ui = fft_list(gr, gi, 1)
    for d in range(32):
        re, im = cmul(ur[d], ui[d], pc_ref[8 * d:8 * d + 8, lanes], ps_ref[8 * d:8 * d + 8, lanes])
        out_ref[8 * d:8 * d + 8, base:base + 512] = re
        out_ref[8 * d:8 * d + 8, base + 512:base + 1024] = im


def column_inverse_kernel(x_ref, mh_ref, ml_ref, twc_ref, tws_ref, out_ref, s_ref):
    lhs_re = jnp.concatenate([x_ref[:, 0:512].T, x_ref[:, 1024:1536].T], axis=0)
    lhs_im = jnp.concatenate([x_ref[:, 512:1024].T, x_ref[:, 1536:2048].T], axis=0)
    lhs = jnp.concatenate([lhs_re, lhs_im], axis=1)
    s_ref[...] = dot3(lhs, mh_ref[...], ml_ref[...])
    er, ei = [], []
    for k in range(32):
        rows = slice(32 * k, 32 * (k + 1))
        a = jnp.concatenate([s_ref[rows, 0:128], s_ref[rows, 256:384]], axis=1)
        b = jnp.concatenate([s_ref[rows, 128:256], s_ref[rows, 384:512]], axis=1)
        a, b = cmul(a, b, twc_ref[k:k + 1, :], tws_ref[k:k + 1, :])
        er.append(a)
        ei.append(b)
    tr, ti = fft_list(er, ei, 1)
    for t in range(8, 32):
        for p in range(2):
            out_ref[p, 0, :, (t - 8) * 128:(t - 7) * 128] = tr[t][:, 128 * p:128 * (p + 1)]
            out_ref[p, 1, :, (t - 8) * 128:(t - 7) * 128] = ti[t][:, 128 * p:128 * (p + 1)]


def call(kernel, out_shapes, scratch, *args):
    return pl.pallas_call(
        kernel,
        out_shape=[jax.ShapeDtypeStruct(s, F32) for s in out_shapes],
        scratch_shapes=[pltpu.VMEM(s, F32) for s in scratch],
        interpret=INTERPRET,
    )(*args)


def exchanged(block):
    rows, width = block.shape
    out = lax.all_to_all(block.reshape(32, rows // 32, width), "band", 0, 0, tiled=True)
    return out.reshape(rows, width)


def arranged(table):
    return table.reshape(32, 32, 4, 8, 4).transpose(3, 1, 2, 4, 0).reshape(1024, 128)


def per_device(voltages, chirp_phase):
    block = voltages[0, 0]
    band = lax.axis_index("band")
    history = [passed_along(block[p, :, :, 3072 - HIST:], "seg", 1) for p in range(2)]

    i32 = jnp.int32
    lane = jnp.arange(1024, dtype=i32)[None, :]
    r_lane = 32 * band + lane % 32
    ka_lane = lane // 32
    t2c, t2s = unit(jnp.arange(32, dtype=i32)[None, :] * (32 * band + jnp.arange(32, dtype=i32)[:, None]), LENGTH, -1)
    q = jnp.arange(8, dtype=i32)[:, None]
    dd = jnp.arange(32, dtype=i32)[:, None]
    pac, pas = unit(32 * r_lane * (q % 4), LENGTH, -1)
    pbc, pbs = unit(128 * r_lane * dd, LENGTH, -1)
    kc_lane = 128 * band + ka_lane
    rl_lane = lane % 32
    rows = jnp.arange(256, dtype=i32)[:, None]

    back_c, back_s = unit((32 * (rows // 8) + lane % 32) * (kc_lane + 32 * (rows % 4)), LENGTH, 1)
    back_c, back_s, history = lax.optimization_barrier((back_c, back_s, history))

    t1c, t1s = lane_twiddle(-1, 128)
    lr, li = send_matrices()
    (send,) = call(column_forward_kernel, [(256, 2048)], [(1024, 512)],
                   block, *history, jnp.asarray(t1c), jnp.asarray(t1s), t2c, t2s,
                   *halves(lr), *halves(li), pac, pas, pbc, pbs)
    received = exchanged(send)

    chirp_phase, send = lax.optimization_barrier((chirp_phase, send))
    phases = gathered(chirp_phase, "seg", 1)[0]
    ch_c, ch_s = arranged(jnp.cos(phases)), arranged(jnp.sin(phases))

    twc, tws = row_twiddle(-1)
    (sent,) = call(row_kernel, [(256, 2048)], [(1024, 256), (1024, 256)],
                   received, jnp.asarray(twc), jnp.asarray(tws), *halves(row_block(-1)),
                   *halves(row_block(1)), ch_c, ch_s, back_c, back_s)
    returned = exchanged(sent)

    cc, cs = lane_twiddle(1, 256)
    (out,) = call(column_inverse_kernel, [(2, 2, ROWS_DEV, 3072)], [(1024, 512)],
                  returned, *halves(receive_matrix()), jnp.asarray(cc), jnp.asarray(cs))
    return out[None, None]


def solution(mesh):
    in_specs = (P("seg", None, None, None, "band", None), P(None, "seg", "band"))
    out_specs = P("seg", None, None, None, "band", None)
    return jax.shard_map(
        per_device, mesh=mesh, in_specs=in_specs, out_specs=out_specs, check_vma=False
    )
```

```python
import math

import numpy as np
import jax
import jax.numpy as jnp
from jax import lax
from jax.experimental import pallas as pl
from jax.experimental.pallas import tpu as pltpu
from jax.sharding import PartitionSpec as P

INTERPRET = False
HIGHEST = lax.Precision.HIGHEST
F32 = jnp.float32
ROWS_DEV = 32
COLS = 4096
HIST = 1024
LENGTH = 1024 * 4096


def passed_along(block, axis, distance):
    devices = range(lax.axis_size(axis))
    route = [(i - distance, i) for i in devices if i - distance in devices]
    return lax.ppermute(block, axis, route)


def gathered(block, axis, dim):
    size = lax.axis_size(axis)
    pieces = [block]
    for shift in range(1, size):
        route = [((i + shift) % size, i) for i in range(size)]
        pieces.append(lax.ppermute(block, axis, route))
    ahead = jnp.stack(pieces, axis=0)
    ordered = jnp.roll(ahead, lax.axis_index(axis), axis=0)
    ordered = jnp.moveaxis(ordered, 0, dim)
    shape = list(block.shape)
    shape[dim] *= size
    return ordered.reshape(shape)


def fft_list(xr, xi, sign):
    n = len(xr)
    if n == 1:
        return list(xr), list(xi)
    er, ei = fft_list(xr[0::2], xi[0::2], sign)
    odd_r, odd_i = fft_list(xr[1::2], xi[1::2], sign)
    half = n // 2
    outr = [None] * n
    outi = [None] * n
    for k in range(half):
        a, b = odd_r[k], odd_i[k]
        if k == 0:
            tr, ti = a, b
        elif 4 * k == n:
            tr, ti = (-b, a) if sign > 0 else (b, -a)
        else:
            angle = sign * 2.0 * math.pi * k / n
            c, s = math.cos(angle), math.sin(angle)
            tr = a * c - b * s
            ti = a * s + b * c
        outr[k] = er[k] + tr
        outi[k] = ei[k] + ti
        outr[k + half] = er[k] - tr
        outi[k + half] = ei[k] - ti
    return outr, outi


BF16 = jnp.bfloat16


def split(x):
    hi = x.astype(BF16)
    return hi, (x - hi.astype(F32)).astype(BF16)


def dot3(a, b_hi, b_lo, dims=(((1,), (0,)), ((), ())), a_first=True):
    a_hi, a_lo = split(a)
    def one(x, y):
        if a_first:
            return lax.dot_general(x, y, dims, preferred_element_type=F32)
        return lax.dot_general(y, x, dims, preferred_element_type=F32)
    return one(a_hi, b_hi) + (one(a_lo, b_hi) + one(a_hi, b_lo))


def halves(m):
    hi = m.astype(BF16)
    lo = (m - hi.astype(np.float32)).astype(BF16)
    return jnp.asarray(hi), jnp.asarray(lo)


def unit(m, n, sign):
    angle = (m % n).astype(F32) * F32(sign * 2.0 * math.pi / n)
    return jnp.cos(angle), jnp.sin(angle)


def send_matrices():
    row = np.arange(256)
    dd, pp, ks = row // 8, (row // 4) % 2, row % 4
    k2 = 4 * dd + ks
    col = np.arange(512)
    pin, riin, lane = col // 256, (col // 128) % 2, col % 128
    ang = -2.0 * np.pi * np.outer(k2, lane) / 128.0
    c, s = np.cos(ang), np.sin(ang)
    same = (pp[:, None] == pin[None, :])
    real = np.where(riin[None, :] == 0, c, -s) * same
    imag = np.where(riin[None, :] == 0, s, c) * same
    return real.astype(np.float32), imag.astype(np.float32)


def row_block(sign):
    idx = np.arange(128)
    q, r = idx // 32, idx % 32
    ang = sign * 2.0 * np.pi * np.outer(r, r) / 32.0
    same = q[:, None] == q[None, :]
    wr = np.cos(ang) * same
    wi = np.sin(ang) * same
    top = np.concatenate([wr, wi], axis=1)
    bottom = np.concatenate([-wi, wr], axis=1)
    return np.concatenate([top, bottom], axis=0).astype(np.float32)


def row_twiddle(sign):
    g = np.arange(32)[:, None]
    r = (np.arange(512) % 32)[None, :]
    ang = sign * 2.0 * np.pi * (g * r) / 1024.0
    return np.cos(ang).astype(np.float32), np.sin(ang).astype(np.float32)


def receive_matrix():
    row = np.arange(512)
    riin, dd, pp, ks = row // 256, (row // 8) % 32, (row // 4) % 2, row % 4
    k2 = 4 * dd + ks
    col = np.arange(512)
    pout, riout, lc = col // 256, (col // 128) % 2, col % 128
    ang = 2.0 * np.pi * np.outer(k2, lc) / 128.0
    c, s = np.cos(ang), np.sin(ang)
    same = pp[:, None] == pout[None, :]
    val = np.where(riin[:, None] == 0,
                   np.where(riout[None, :] == 0, c, s),
                   np.where(riout[None, :] == 0, -s, c))
    return (val * same / LENGTH).astype(np.float32)


def lane_twiddle(sign, width):
    ka = np.arange(32)[:, None]
    lc = (np.arange(width) % 128)[None, :]
    ang = sign * 2.0 * np.pi * (ka * lc) / 4096.0
    return np.cos(ang).astype(np.float32), np.sin(ang).astype(np.float32)


def cmul(ar, ai, br, bi):
    return ar * br - ai * bi, ar * bi + ai * br


def column_forward_kernel(blk_ref, hist0_ref, hist1_ref, t1c, t1s, t2c, t2s, lrh, lrl, lih, lil, pac, pas, pbc, pbs,
                          out_ref, xs_ref):
    for p, hist_ref in enumerate((hist0_ref, hist1_ref)):
        xr, xi = [], []
        for t in range(32):
            if t < 8:
                xr.append(hist_ref[0, :, t * 128:(t + 1) * 128])
                xi.append(hist_ref[1, :, t * 128:(t + 1) * 128])
            else:
                xr.append(blk_ref[p, 0, :, (t - 8) * 128:(t - 7) * 128])
                xi.append(blk_ref[p, 1, :, (t - 8) * 128:(t - 7) * 128])
        ar, ai = fft_list(xr, xi, -1)
        for k in range(32):
            wc, ws = cmul(t1c[k:k + 1, :], t1s[k:k + 1, :], t2c[:, k:k + 1], t2s[:, k:k + 1])
            re, im = cmul(ar[k], ai[k], wc, ws)
            xs_ref[k * 32:(k + 1) * 32, p * 256:p * 256 + 128] = re
            xs_ref[k * 32:(k + 1) * 32, p * 256 + 128:p * 256 + 256] = im
    dims = (((1,), (1,)), ((), ()))
    for h in range(2):
        x = xs_ref[512 * h:512 * (h + 1), :]
        ore = dot3(x, lrh[...], lrl[...], dims, a_first=False)
        oim = dot3(x, lih[...], lil[...], dims, a_first=False)
        ac = pac[:, 512 * h:512 * (h + 1)]
        as_ = pas[:, 512 * h:512 * (h + 1)]
        for d in range(32):
            bc = pbc[d:d + 1, 512 * h:512 * (h + 1)]
            bs = pbs[d:d + 1, 512 * h:512 * (h + 1)]
            wc, ws = cmul(ac, as_, bc, bs)
            re, im = cmul(ore[8 * d:8 * d + 8], oim[8 * d:8 * d + 8], wc, ws)
            out_ref[8 * d:8 * d + 8, 1024 * h:1024 * h + 512] = re
            out_ref[8 * d:8 * d + 8, 1024 * h + 512:1024 * h + 1024] = im


def row_kernel(x_ref, twc_ref, tws_ref, bfh, bfl, bbh, bbl, chc_ref, chs_ref, ac_ref, as_ref, bc_ref, bs_ref,
               cc_ref, cs_ref, out_ref, y_ref, w_ref):
    tw_refs = (ac_ref, as_ref, bc_ref, bs_ref, cc_ref, cs_ref)
    for h in range(2):
        row_half(h, x_ref, twc_ref, tws_ref, bfh, bfl, bbh, bbl, chc_ref, chs_ref, tw_refs, out_ref, y_ref, w_ref)


def row_half(h, x_ref, twc_ref, tws_ref, bfh, bfl, bbh, bbl, chc_ref, chs_ref, tw_refs, out_ref, y_ref, w_ref):
    base = 1024 * h
    lanes = slice(512 * h, 512 * (h + 1))
    er = [x_ref[8 * d:8 * d + 8, base:base + 512] for d in range(32)]
    ei = [x_ref[8 * d:8 * d + 8, base + 512:base + 1024] for d in range(32)]
    fr, fi = fft_list(er, ei, -1)
    for g in range(32):
        a, b = cmul(fr[g], fi[g], twc_ref[g:g + 1, :], tws_ref[g:g + 1, :])
        for p in range(2):
            for j in range(4):
                at = 512 * p + 128 * j + 4 * g
                y_ref[at:at + 4, 0:128] = a[4 * p:4 * p + 4, 128 * j:128 * (j + 1)]
                y_ref[at:at + 4, 128:256] = b[4 * p:4 * p + 4, 128 * j:128 * (j + 1)]
    z = dot3(y_ref[...], bfh[...], bfl[...])
    c = chc_ref[512 * h:512 * (h + 1), :]
    s = chs_ref[512 * h:512 * (h + 1), :]
    for p in range(2):
        rows = slice(512 * p, 512 * (p + 1))
        re, im = cmul(z[rows, 0:128], z[rows, 128:256], c, s)
        y_ref[rows, 0:128] = re
        y_ref[rows, 128:256] = im
    w_ref[...] = dot3(y_ref[...], bbh[...], bbl[...])
    gr, gi = [], []
    for g in range(32):
        pa, pb = [], []
        for j in range(4):
            lo, hi = 128 * j + 4 * g, 512 + 128 * j + 4 * g
            pa.append(jnp.concatenate([w_ref[lo:lo + 4, 0:128], w_ref[hi:hi + 4, 0:128]], axis=0))
            pb.append(jnp.concatenate([w_ref[lo:lo + 4, 128:256], w_ref[hi:hi + 4, 128:256]], axis=0))
        a, b = cmul(jnp.concatenate(pa, axis=1), jnp.concatenate(pb, axis=1), twc_ref[g:g + 1, :], -tws_ref[g:g + 1, :])
        gr.append(a)
        gi.append(b)
    ur, ui = fft_list(gr, gi, 1)
    ac_ref, as_ref, bc_ref, bs_ref, cc_ref, cs_ref = tw_refs
    ac = ac_ref[:, lanes]
    as_ = as_ref[:, lanes]
    for d in range(32):
        wc, ws = cmul(bc_ref[d:d + 1, lanes], bs_ref[d:d + 1, lanes], cc_ref[8 * d:8 * d + 8, 0:1], cs_ref[8 * d:8 * d + 8, 0:1])
        wc, ws = cmul(wc, ws, ac, as_)
        re, im = cmul(ur[d], ui[d], wc, ws)
        out_ref[8 * d:8 * d + 8, base:base + 512] = re
        out_ref[8 * d:8 * d + 8, base + 512:base + 1024] = im


def column_inverse_kernel(x_ref, mh_ref, ml_ref, twc_ref, tws_ref, out_ref, s_ref):
    lhs_re = jnp.concatenate([x_ref[:, 0:512].T, x_ref[:, 1024:1536].T], axis=0)
    lhs_im = jnp.concatenate([x_ref[:, 512:1024].T, x_ref[:, 1536:2048].T], axis=0)
    lhs = jnp.concatenate([lhs_re, lhs_im], axis=1)
    s_ref[...] = dot3(lhs, mh_ref[...], ml_ref[...])
    er, ei = [], []
    for k in range(32):
        rows = slice(32 * k, 32 * (k + 1))
        a = jnp.concatenate([s_ref[rows, 0:128], s_ref[rows, 256:384]], axis=1)
        b = jnp.concatenate([s_ref[rows, 128:256], s_ref[rows, 384:512]], axis=1)
        a, b = cmul(a, b, twc_ref[k:k + 1, :], tws_ref[k:k + 1, :])
        er.append(a)
        ei.append(b)
    tr, ti = fft_list(er, ei, 1)
    for t in range(8, 32):
        for p in range(2):
            out_ref[p, 0, :, (t - 8) * 128:(t - 7) * 128] = tr[t][:, 128 * p:128 * (p + 1)]
            out_ref[p, 1, :, (t - 8) * 128:(t - 7) * 128] = ti[t][:, 128 * p:128 * (p + 1)]


def call(kernel, out_shapes, scratch, *args):
    return pl.pallas_call(
        kernel,
        out_shape=[jax.ShapeDtypeStruct(s, F32) for s in out_shapes],
        scratch_shapes=[pltpu.VMEM(s, F32) for s in scratch],
        interpret=INTERPRET,
    )(*args)


def exchanged(block):
    rows, width = block.shape
    out = lax.all_to_all(block.reshape(32, rows // 32, width), "band", 0, 0, tiled=True)
    return out.reshape(rows, width)


def arranged(table):
    return table.reshape(32, 32, 4, 8, 4).transpose(3, 1, 2, 4, 0).reshape(1024, 128)


def per_device(voltages, chirp_phase):
    block = voltages[0, 0]
    band = lax.axis_index("band")
    history = [passed_along(block[p, :, :, 3072 - HIST:], "seg", 1) for p in range(2)]

    i32 = jnp.int32
    lane = jnp.arange(1024, dtype=i32)[None, :]
    r_lane = 32 * band + lane % 32
    ka_lane = lane // 32
    t2c, t2s = unit(jnp.arange(32, dtype=i32)[None, :] * (32 * band + jnp.arange(32, dtype=i32)[:, None]), LENGTH, -1)
    q = jnp.arange(8, dtype=i32)[:, None]
    dd = jnp.arange(32, dtype=i32)[:, None]
    pac, pas = unit(32 * r_lane * (q % 4), LENGTH, -1)
    pbc, pbs = unit(128 * r_lane * dd, LENGTH, -1)
    kc_lane = 128 * band + ka_lane
    rl_lane = lane % 32
    rows = jnp.arange(256, dtype=i32)[:, None]

    bac, bas = unit(rl_lane * (kc_lane + 32 * (q % 4)), LENGTH, 1)
    bbc, bbs = unit(32 * dd * kc_lane, LENGTH, 1)
    bcc, bcs = unit(jnp.broadcast_to(1024 * (rows // 8) * (rows % 4), (256, 128)), LENGTH, 1)

    t1c, t1s = lane_twiddle(-1, 128)
    lr, li = send_matrices()
    (send,) = call(column_forward_kernel, [(256, 2048)], [(1024, 512)],
                   block, *history, jnp.asarray(t1c), jnp.asarray(t1s), t2c, t2s,
                   *halves(lr), *halves(li), pac, pas, pbc, pbs)
    received = exchanged(send)

    chirp_phase, send = lax.optimization_barrier((chirp_phase, send))
    phases = gathered(chirp_phase, "seg", 1)[0]
    ch_c, ch_s = arranged(jnp.cos(phases)), arranged(jnp.sin(phases))

    twc, tws = row_twiddle(-1)
    (sent,) = call(row_kernel, [(256, 2048)], [(1024, 256), (1024, 256)],
                   received, jnp.asarray(twc), jnp.asarray(tws), *halves(row_block(-1)),
                   *halves(row_block(1)), ch_c, ch_s, bac, bas, bbc, bbs, bcc, bcs)
    returned = exchanged(sent)

    cc, cs = lane_twiddle(1, 256)
    (out,) = call(column_inverse_kernel, [(2, 2, ROWS_DEV, 3072)], [(1024, 512)],
                  returned, *halves(receive_matrix()), jnp.asarray(cc), jnp.asarray(cs))
    return out[None, None]


def solution(mesh):
    in_specs = (P("seg", None, None, None, "band", None), P(None, "seg", "band"))
    out_specs = P("seg", None, None, None, "band", None)
    return jax.shard_map(
        per_device, mesh=mesh, in_specs=in_specs, out_specs=out_specs, check_vma=False
    )
```

```python
import math

import numpy as np
import jax
import jax.numpy as jnp
from jax import lax
from jax.experimental import pallas as pl
from jax.experimental.pallas import tpu as pltpu
from jax.sharding import PartitionSpec as P

INTERPRET = False
HIGHEST = lax.Precision.HIGHEST
F32 = jnp.float32
ROWS_DEV = 32
COLS = 4096
HIST = 1024
LENGTH = 1024 * 4096


def passed_along(block, axis, distance):
    devices = range(lax.axis_size(axis))
    route = [(i - distance, i) for i in devices if i - distance in devices]
    return lax.ppermute(block, axis, route)


def gathered(block, axis, dim):
    size = lax.axis_size(axis)
    pieces = [block]
    for shift in range(1, size):
        route = [((i + shift) % size, i) for i in range(size)]
        pieces.append(lax.ppermute(block, axis, route))
    ahead = jnp.stack(pieces, axis=0)
    ordered = jnp.roll(ahead, lax.axis_index(axis), axis=0)
    ordered = jnp.moveaxis(ordered, 0, dim)
    shape = list(block.shape)
    shape[dim] *= size
    return ordered.reshape(shape)


def fft_list(xr, xi, sign):
    n = len(xr)
    if n == 1:
        return list(xr), list(xi)
    er, ei = fft_list(xr[0::2], xi[0::2], sign)
    odd_r, odd_i = fft_list(xr[1::2], xi[1::2], sign)
    half = n // 2
    outr = [None] * n
    outi = [None] * n
    for k in range(half):
        a, b = odd_r[k], odd_i[k]
        if k == 0:
            tr, ti = a, b
        elif 4 * k == n:
            tr, ti = (-b, a) if sign > 0 else (b, -a)
        else:
            angle = sign * 2.0 * math.pi * k / n
            c, s = math.cos(angle), math.sin(angle)
            tr = a * c - b * s
            ti = a * s + b * c
        outr[k] = er[k] + tr
        outi[k] = ei[k] + ti
        outr[k + half] = er[k] - tr
        outi[k + half] = ei[k] - ti
    return outr, outi


BF16 = jnp.bfloat16


def split(x):
    hi = x.astype(BF16)
    return hi, (x - hi.astype(F32)).astype(BF16)


def dot3(a, b_hi, b_lo, dims=(((1,), (0,)), ((), ())), a_first=True):
    a_hi, a_lo = split(a)
    def one(x, y):
        if a_first:
            return lax.dot_general(x, y, dims, preferred_element_type=F32)
        return lax.dot_general(y, x, dims, preferred_element_type=F32)
    return one(a_hi, b_hi) + (one(a_lo, b_hi) + one(a_hi, b_lo))


def halves(m):
    hi = m.astype(BF16)
    lo = (m - hi.astype(np.float32)).astype(BF16)
    return jnp.asarray(hi), jnp.asarray(lo)


def unit(m, n, sign):
    angle = (m % n).astype(F32) * F32(sign * 2.0 * math.pi / n)
    return jnp.cos(angle), jnp.sin(angle)


def send_matrices():
    row = np.arange(256)
    dd, pp, ks = row // 8, (row // 4) % 2, row % 4
    k2 = 4 * dd + ks
    col = np.arange(512)
    pin, riin, lane = col // 256, (col // 128) % 2, col % 128
    ang = -2.0 * np.pi * np.outer(k2, lane) / 128.0
    c, s = np.cos(ang), np.sin(ang)
    same = (pp[:, None] == pin[None, :])
    real = np.where(riin[None, :] == 0, c, -s) * same
    imag = np.where(riin[None, :] == 0, s, c) * same
    return real.astype(np.float32), imag.astype(np.float32)


def row_block(sign):
    idx = np.arange(128)
    q, r = idx // 32, idx % 32
    ang = sign * 2.0 * np.pi * np.outer(r, r) / 32.0
    same = q[:, None] == q[None, :]
    wr = np.cos(ang) * same
    wi = np.sin(ang) * same
    top = np.concatenate([wr, wi], axis=1)
    bottom = np.concatenate([-wi, wr], axis=1)
    return np.concatenate([top, bottom], axis=0).astype(np.float32)


def row_twiddle(sign):
    g = np.arange(32)[:, None]
    r = (np.arange(512) % 32)[None, :]
    ang = sign * 2.0 * np.pi * (g * r) / 1024.0
    return np.cos(ang).astype(np.float32), np.sin(ang).astype(np.float32)


def receive_matrix():
    row = np.arange(512)
    riin, dd, pp, ks = row // 256, (row // 8) % 32, (row // 4) % 2, row % 4
    k2 = 4 * dd + ks
    col = np.arange(512)
    pout, riout, lc = col // 256, (col // 128) % 2, col % 128
    ang = 2.0 * np.pi * np.outer(k2, lc) / 128.0
    c, s = np.cos(ang), np.sin(ang)
    same = pp[:, None] == pout[None, :]
    val = np.where(riin[:, None] == 0,
                   np.where(riout[None, :] == 0, c, s),
                   np.where(riout[None, :] == 0, -s, c))
    return (val * same / LENGTH).astype(np.float32)


def lane_twiddle(sign, width):
    ka = np.arange(32)[:, None]
    lc = (np.arange(width) % 128)[None, :]
    ang = sign * 2.0 * np.pi * (ka * lc) / 4096.0
    return np.cos(ang).astype(np.float32), np.sin(ang).astype(np.float32)


def cmul(ar, ai, br, bi):
    return ar * br - ai * bi, ar * bi + ai * br


def column_forward_kernel(blk_ref, hist_ref, t1c, t1s, t2c, t2s, lrh, lrl, lih, lil, pac, pas, pbc, pbs,
                          out_ref, xs_ref):
    for p in range(2):
        xr, xi = [], []
        for t in range(32):
            if t < 8:
                xr.append(hist_ref[p, 0, :, t * 128:(t + 1) * 128])
                xi.append(hist_ref[p, 1, :, t * 128:(t + 1) * 128])
            else:
                xr.append(blk_ref[p, 0, :, (t - 8) * 128:(t - 7) * 128])
                xi.append(blk_ref[p, 1, :, (t - 8) * 128:(t - 7) * 128])
        ar, ai = fft_list(xr, xi, -1)
        for k in range(32):
            wc, ws = cmul(t1c[k:k + 1, :], t1s[k:k + 1, :], t2c[:, k:k + 1], t2s[:, k:k + 1])
            re, im = cmul(ar[k], ai[k], wc, ws)
            xs_ref[k * 32:(k + 1) * 32, p * 256:p * 256 + 128] = re
            xs_ref[k * 32:(k + 1) * 32, p * 256 + 128:p * 256 + 256] = im
    dims = (((1,), (1,)), ((), ()))
    for h in range(2):
        x = xs_ref[512 * h:512 * (h + 1), :]
        ore = dot3(x, lrh[...], lrl[...], dims, a_first=False)
        oim = dot3(x, lih[...], lil[...], dims, a_first=False)
        ac = pac[:, 512 * h:512 * (h + 1)]
        as_ = pas[:, 512 * h:512 * (h + 1)]
        for d in range(32):
            bc = pbc[d:d + 1, 512 * h:512 * (h + 1)]
            bs = pbs[d:d + 1, 512 * h:512 * (h + 1)]
            wc, ws = cmul(ac, as_, bc, bs)
            re, im = cmul(ore[8 * d:8 * d + 8], oim[8 * d:8 * d + 8], wc, ws)
            out_ref[8 * d:8 * d + 8, 1024 * h:1024 * h + 512] = re
            out_ref[8 * d:8 * d + 8, 1024 * h + 512:1024 * h + 1024] = im


def row_kernel(x_ref, twc_ref, tws_ref, bfh, bfl, bbh, bbl, chc_ref, chs_ref, pc_ref, ps_ref, out_ref, y_ref, w_ref):
    for h in range(2):
        row_half(h, x_ref, twc_ref, tws_ref, bfh, bfl, bbh, bbl, chc_ref, chs_ref, pc_ref, ps_ref, out_ref, y_ref, w_ref)


def row_half(h, x_ref, twc_ref, tws_ref, bfh, bfl, bbh, bbl, chc_ref, chs_ref, pc_ref, ps_ref, out_ref, y_ref, w_ref):
    base = 1024 * h
    lanes = slice(512 * h, 512 * (h + 1))
    er = [x_ref[8 * d:8 * d + 8, base:base + 512] for d in range(32)]
    ei = [x_ref[8 * d:8 * d + 8, base + 512:base + 1024] for d in range(32)]
    fr, fi = fft_list(er, ei, -1)
    for g in range(32):
        a, b = cmul(fr[g], fi[g], twc_ref[g:g + 1, :], tws_ref[g:g + 1, :])
        for p in range(2):
            for j in range(4):
                at = 512 * p + 128 * j + 4 * g
                y_ref[at:at + 4, 0:128] = a[4 * p:4 * p + 4, 128 * j:128 * (j + 1)]
                y_ref[at:at + 4, 128:256] = b[4 * p:4 * p + 4, 128 * j:128 * (j + 1)]
    z = dot3(y_ref[...], bfh[...], bfl[...])
    c = chc_ref[512 * h:512 * (h + 1), :]
    s = chs_ref[512 * h:512 * (h + 1), :]
    for p in range(2):
        rows = slice(512 * p, 512 * (p + 1))
        re, im = cmul(z[rows, 0:128], z[rows, 128:256], c, s)
        y_ref[rows, 0:128] = re
        y_ref[rows, 128:256] = im
    w_ref[...] = dot3(y_ref[...], bbh[...], bbl[...])
    gr, gi = [], []
    for g in range(32):
        pa, pb = [], []
        for j in range(4):
            lo, hi = 128 * j + 4 * g, 512 + 128 * j + 4 * g
            pa.append(jnp.concatenate([w_ref[lo:lo + 4, 0:128], w_ref[hi:hi + 4, 0:128]], axis=0))
            pb.append(jnp.concatenate([w_ref[lo:lo + 4, 128:256], w_ref[hi:hi + 4, 128:256]], axis=0))
        a, b = cmul(jnp.concatenate(pa, axis=1), jnp.concatenate(pb, axis=1), twc_ref[g:g + 1, :], -tws_ref[g:g + 1, :])
        gr.append(a)
        gi.append(b)
    ur, ui = fft_list(gr, gi, 1)
    for d in range(32):
        re, im = cmul(ur[d], ui[d], pc_ref[8 * d:8 * d + 8, lanes], ps_ref[8 * d:8 * d + 8, lanes])
        out_ref[8 * d:8 * d + 8, base:base + 512] = re
        out_ref[8 * d:8 * d + 8, base + 512:base + 1024] = im


def column_inverse_kernel(x_ref, mh_ref, ml_ref, twc_ref, tws_ref, out_ref, s_ref):
    lhs_re = jnp.concatenate([x_ref[:, 0:512].T, x_ref[:, 1024:1536].T], axis=0)
    lhs_im = jnp.concatenate([x_ref[:, 512:1024].T, x_ref[:, 1536:2048].T], axis=0)
    lhs = jnp.concatenate([lhs_re, lhs_im], axis=1)
    s_ref[...] = dot3(lhs, mh_ref[...], ml_ref[...])
    er, ei = [], []
    for k in range(32):
        rows = slice(32 * k, 32 * (k + 1))
        a = jnp.concatenate([s_ref[rows, 0:128], s_ref[rows, 256:384]], axis=1)
        b = jnp.concatenate([s_ref[rows, 128:256], s_ref[rows, 384:512]], axis=1)
        a, b = cmul(a, b, twc_ref[k:k + 1, :], tws_ref[k:k + 1, :])
        er.append(a)
        ei.append(b)
    tr, ti = fft_list(er, ei, 1)
    for t in range(8, 32):
        for p in range(2):
            out_ref[p, 0, :, (t - 8) * 128:(t - 7) * 128] = tr[t][:, 128 * p:128 * (p + 1)]
            out_ref[p, 1, :, (t - 8) * 128:(t - 7) * 128] = ti[t][:, 128 * p:128 * (p + 1)]


def call(kernel, out_shapes, scratch, *args):
    return pl.pallas_call(
        kernel,
        out_shape=[jax.ShapeDtypeStruct(s, F32) for s in out_shapes],
        scratch_shapes=[pltpu.VMEM(s, F32) for s in scratch],
        interpret=INTERPRET,
    )(*args)


def exchanged(block):
    rows, width = block.shape
    out = lax.all_to_all(block.reshape(32, rows // 32, width), "band", 0, 0, tiled=True)
    return out.reshape(rows, width)


def arranged(table):
    return table.reshape(32, 32, 4, 8, 4).transpose(3, 1, 2, 4, 0).reshape(1024, 128)


def per_device(voltages, chirp_phase):
    block = voltages[0, 0]
    band = lax.axis_index("band")
    history = passed_along(block[..., 3072 - HIST:], "seg", 1)

    i32 = jnp.int32
    lane = jnp.arange(1024, dtype=i32)[None, :]
    r_lane = 32 * band + lane % 32
    ka_lane = lane // 32
    t2c, t2s = unit(jnp.arange(32, dtype=i32)[None, :] * (32 * band + jnp.arange(32, dtype=i32)[:, None]), LENGTH, -1)
    q = jnp.arange(8, dtype=i32)[:, None]
    dd = jnp.arange(32, dtype=i32)[:, None]
    pac, pas = unit(32 * r_lane * (q % 4), LENGTH, -1)
    pbc, pbs = unit(128 * r_lane * dd, LENGTH, -1)
    kc_lane = 128 * band + ka_lane
    rl_lane = lane % 32
    rows = jnp.arange(256, dtype=i32)[:, None]

    back_c, back_s = unit((32 * (rows // 8) + lane % 32) * (kc_lane + 32 * (rows % 4)), LENGTH, 1)
    back_c, back_s, history = lax.optimization_barrier((back_c, back_s, history))

    t1c, t1s = lane_twiddle(-1, 128)
    lr, li = send_matrices()
    (send,) = call(column_forward_kernel, [(256, 2048)], [(1024, 512)],
                   block, history, jnp.asarray(t1c), jnp.asarray(t1s), t2c, t2s,
                   *halves(lr), *halves(li), pac, pas, pbc, pbs)
    received = exchanged(send)

    chirp_phase, send = lax.optimization_barrier((chirp_phase, send))
    phases = gathered(chirp_phase, "seg", 1)[0]
    ch_c, ch_s = arranged(jnp.cos(phases)), arranged(jnp.sin(phases))

    twc, tws = row_twiddle(-1)
    (sent,) = call(row_kernel, [(256, 2048)], [(1024, 256), (1024, 256)],
                   received, jnp.asarray(twc), jnp.asarray(tws), *halves(row_block(-1)),
                   *halves(row_block(1)), ch_c, ch_s, back_c, back_s)
    returned = exchanged(sent)

    cc, cs = lane_twiddle(1, 256)
    (out,) = call(column_inverse_kernel, [(2, 2, ROWS_DEV, 3072)], [(1024, 512)],
                  returned, *halves(receive_matrix()), jnp.asarray(cc), jnp.asarray(cs))
    return out[None, None]


def solution(mesh):
    in_specs = (P("seg", None, None, None, "band", None), P(None, "seg", "band"))
    out_specs = P("seg", None, None, None, "band", None)
    return jax.shard_map(
        per_device, mesh=mesh, in_specs=in_specs, out_specs=out_specs, check_vma=False
    )
```

```python
import math

import numpy as np
import jax
import jax.numpy as jnp
from jax import lax
from jax.experimental import pallas as pl
from jax.experimental.pallas import tpu as pltpu
from jax.sharding import PartitionSpec as P

INTERPRET = False
HIGHEST = lax.Precision.HIGHEST
F32 = jnp.float32
ROWS_DEV = 32
COLS = 4096
HIST = 1024
LENGTH = 1024 * 4096


def passed_along(block, axis, distance):
    devices = range(lax.axis_size(axis))
    route = [(i - distance, i) for i in devices if i - distance in devices]
    return lax.ppermute(block, axis, route)


def gathered(block, axis, dim):
    size = lax.axis_size(axis)
    pieces = [block]
    for shift in range(1, size):
        route = [((i + shift) % size, i) for i in range(size)]
        pieces.append(lax.ppermute(block, axis, route))
    ahead = jnp.stack(pieces, axis=0)
    ordered = jnp.roll(ahead, lax.axis_index(axis), axis=0)
    ordered = jnp.moveaxis(ordered, 0, dim)
    shape = list(block.shape)
    shape[dim] *= size
    return ordered.reshape(shape)


def fft_list(xr, xi, sign):
    n = len(xr)
    if n == 1:
        return list(xr), list(xi)
    er, ei = fft_list(xr[0::2], xi[0::2], sign)
    odd_r, odd_i = fft_list(xr[1::2], xi[1::2], sign)
    half = n // 2
    outr = [None] * n
    outi = [None] * n
    for k in range(half):
        a, b = odd_r[k], odd_i[k]
        if k == 0:
            tr, ti = a, b
        elif 4 * k == n:
            tr, ti = (-b, a) if sign > 0 else (b, -a)
        else:
            angle = sign * 2.0 * math.pi * k / n
            c, s = math.cos(angle), math.sin(angle)
            tr = a * c - b * s
            ti = a * s + b * c
        outr[k] = er[k] + tr
        outi[k] = ei[k] + ti
        outr[k + half] = er[k] - tr
        outi[k + half] = ei[k] - ti
    return outr, outi


BF16 = jnp.bfloat16


def split(x):
    hi = x.astype(BF16)
    return hi, (x - hi.astype(F32)).astype(BF16)


def dot3(a, b_hi, b_lo, dims=(((1,), (0,)), ((), ())), a_first=True):
    a_hi, a_lo = split(a)
    def one(x, y):
        if a_first:
            return lax.dot_general(x, y, dims, preferred_element_type=F32)
        return lax.dot_general(y, x, dims, preferred_element_type=F32)
    return one(a_hi, b_hi) + (one(a_lo, b_hi) + one(a_hi, b_lo))


def halves(m):
    hi = m.astype(BF16)
    lo = (m - hi.astype(np.float32)).astype(BF16)
    return jnp.asarray(hi), jnp.asarray(lo)


def unit(m, n, sign):
    angle = (m % n).astype(F32) * F32(sign * 2.0 * math.pi / n)
    return jnp.cos(angle), jnp.sin(angle)


def send_matrices():
    row = np.arange(256)
    dd, pp, ks = row // 8, (row // 4) % 2, row % 4
    k2 = 4 * dd + ks
    col = np.arange(512)
    pin, riin, lane = col // 256, (col // 128) % 2, col % 128
    ang = -2.0 * np.pi * np.outer(k2, lane) / 128.0
    c, s = np.cos(ang), np.sin(ang)
    same = (pp[:, None] == pin[None, :])
    real = np.where(riin[None, :] == 0, c, -s) * same
    imag = np.where(riin[None, :] == 0, s, c) * same
    return real.astype(np.float32), imag.astype(np.float32)


def row_block(sign):
    idx = np.arange(128)
    q, r = idx // 32, idx % 32
    ang = sign * 2.0 * np.pi * np.outer(r, r) / 32.0
    same = q[:, None] == q[None, :]
    wr = np.cos(ang) * same
    wi = np.sin(ang) * same
    top = np.concatenate([wr, wi], axis=1)
    bottom = np.concatenate([-wi, wr], axis=1)
    return np.concatenate([top, bottom], axis=0).astype(np.float32)


def row_twiddle(sign):
    g = np.arange(32)[:, None]
    r = (np.arange(512) % 32)[None, :]
    ang = sign * 2.0 * np.pi * (g * r) / 1024.0
    return np.cos(ang).astype(np.float32), np.sin(ang).astype(np.float32)


def receive_matrix():
    row = np.arange(512)
    riin, dd, pp, ks = row // 256, (row // 8) % 32, (row // 4) % 2, row % 4
    k2 = 4 * dd + ks
    col = np.arange(512)
    pout, riout, lc = col // 256, (col // 128) % 2, col % 128
    ang = 2.0 * np.pi * np.outer(k2, lc) / 128.0
    c, s = np.cos(ang), np.sin(ang)
    same = pp[:, None] == pout[None, :]
    val = np.where(riin[:, None] == 0,
                   np.where(riout[None, :] == 0, c, s),
                   np.where(riout[None, :] == 0, -s, c))
    return (val * same / LENGTH).astype(np.float32)


def built_send_matrices(index):
    row, col = index[:256][:, None], index[None, :]
    pp, k2 = (row // 4) % 2, 4 * (row // 8) + row % 4
    pin, riin, lane = col // 256, (col // 128) % 2, col % 128
    c, s = unit(k2 * lane, 128, -1)
    same = (pp == pin).astype(F32)
    return jnp.where(riin == 0, c, -s) * same, jnp.where(riin == 0, s, c) * same


def built_receive_matrix(index):
    row, col = index[:, None], index[None, :]
    riin, pp, k2 = row // 256, (row // 4) % 2, 4 * ((row // 8) % 32) + row % 4
    pout, riout, lc = col // 256, (col // 128) % 2, col % 128
    c, s = unit(k2 * lc, 128, 1)
    val = jnp.where(riin == 0, jnp.where(riout == 0, c, s), jnp.where(riout == 0, -s, c))
    return val * (pp == pout).astype(F32) * F32(1.0 / LENGTH)


def split_matrix(m):
    hi = lax.reduce_precision(m, exponent_bits=8, mantissa_bits=7)
    return hi.astype(BF16), (m - hi).astype(BF16)


def lane_twiddle(sign, width):
    ka = np.arange(32)[:, None]
    lc = (np.arange(width) % 128)[None, :]
    ang = sign * 2.0 * np.pi * (ka * lc) / 4096.0
    return np.cos(ang).astype(np.float32), np.sin(ang).astype(np.float32)


def cmul(ar, ai, br, bi):
    return ar * br - ai * bi, ar * bi + ai * br


def column_forward_kernel(blk_ref, hist_ref, t1c, t1s, t2c, t2s, lrh, lrl, lih, lil, pac, pas, pbc, pbs,
                          out_ref, xs_ref):
    for p in range(2):
        xr, xi = [], []
        for t in range(32):
            if t < 8:
                xr.append(hist_ref[p, 0, :, t * 128:(t + 1) * 128])
                xi.append(hist_ref[p, 1, :, t * 128:(t + 1) * 128])
            else:
                xr.append(blk_ref[p, 0, :, (t - 8) * 128:(t - 7) * 128])
                xi.append(blk_ref[p, 1, :, (t - 8) * 128:(t - 7) * 128])
        ar, ai = fft_list(xr, xi, -1)
        for k in range(32):
            wc, ws = cmul(t1c[k:k + 1, :], t1s[k:k + 1, :], t2c[:, k:k + 1], t2s[:, k:k + 1])
            re, im = cmul(ar[k], ai[k], wc, ws)
            xs_ref[k * 32:(k + 1) * 32, p * 256:p * 256 + 128] = re
            xs_ref[k * 32:(k + 1) * 32, p * 256 + 128:p * 256 + 256] = im
    dims = (((1,), (1,)), ((), ()))
    for h in range(2):
        x = xs_ref[512 * h:512 * (h + 1), :]
        ore = dot3(x, lrh[...], lrl[...], dims, a_first=False)
        oim = dot3(x, lih[...], lil[...], dims, a_first=False)
        ac = pac[:, 512 * h:512 * (h + 1)]
        as_ = pas[:, 512 * h:512 * (h + 1)]
        for d in range(32):
            bc = pbc[d:d + 1, 512 * h:512 * (h + 1)]
            bs = pbs[d:d + 1, 512 * h:512 * (h + 1)]
            wc, ws = cmul(ac, as_, bc, bs)
            re, im = cmul(ore[8 * d:8 * d + 8], oim[8 * d:8 * d + 8], wc, ws)
            out_ref[8 * d:8 * d + 8, 1024 * h:1024 * h + 512] = re
            out_ref[8 * d:8 * d + 8, 1024 * h + 512:1024 * h + 1024] = im


def row_kernel(x_ref, twc_ref, tws_ref, bfh, bfl, bbh, bbl, chc_ref, chs_ref, pc_ref, ps_ref, out_ref, y_ref, w_ref):
    for h in range(2):
        row_half(h, x_ref, twc_ref, tws_ref, bfh, bfl, bbh, bbl, chc_ref, chs_ref, pc_ref, ps_ref, out_ref, y_ref, w_ref)


def row_half(h, x_ref, twc_ref, tws_ref, bfh, bfl, bbh, bbl, chc_ref, chs_ref, pc_ref, ps_ref, out_ref, y_ref, w_ref):
    base = 1024 * h
    lanes = slice(512 * h, 512 * (h + 1))
    er = [x_ref[8 * d:8 * d + 8, base:base + 512] for d in range(32)]
    ei = [x_ref[8 * d:8 * d + 8, base + 512:base + 1024] for d in range(32)]
    fr, fi = fft_list(er, ei, -1)
    for g in range(32):
        a, b = cmul(fr[g], fi[g], twc_ref[g:g + 1, :], tws_ref[g:g + 1, :])
        for p in range(2):
            for j in range(4):
                at = 512 * p + 128 * j + 4 * g
                y_ref[at:at + 4, 0:128] = a[4 * p:4 * p + 4, 128 * j:128 * (j + 1)]
                y_ref[at:at + 4, 128:256] = b[4 * p:4 * p + 4, 128 * j:128 * (j + 1)]
    z = dot3(y_ref[...], bfh[...], bfl[...])
    c = chc_ref[512 * h:512 * (h + 1), :]
    s = chs_ref[512 * h:512 * (h + 1), :]
    for p in range(2):
        rows = slice(512 * p, 512 * (p + 1))
        re, im = cmul(z[rows, 0:128], z[rows, 128:256], c, s)
        y_ref[rows, 0:128] = re
        y_ref[rows, 128:256] = im
    w_ref[...] = dot3(y_ref[...], bbh[...], bbl[...])
    gr, gi = [], []
    for g in range(32):
        pa, pb = [], []
        for j in range(4):
            lo, hi = 128 * j + 4 * g, 512 + 128 * j + 4 * g
            pa.append(jnp.concatenate([w_ref[lo:lo + 4, 0:128], w_ref[hi:hi + 4, 0:128]], axis=0))
            pb.append(jnp.concatenate([w_ref[lo:lo + 4, 128:256], w_ref[hi:hi + 4, 128:256]], axis=0))
        a, b = cmul(jnp.concatenate(pa, axis=1), jnp.concatenate(pb, axis=1), twc_ref[g:g + 1, :], -tws_ref[g:g + 1, :])
        gr.append(a)
        gi.append(b)
    ur, ui = fft_list(gr, gi, 1)
    for d in range(32):
        re, im = cmul(ur[d], ui[d], pc_ref[8 * d:8 * d + 8, lanes], ps_ref[8 * d:8 * d + 8, lanes])
        out_ref[8 * d:8 * d + 8, base:base + 512] = re
        out_ref[8 * d:8 * d + 8, base + 512:base + 1024] = im


def column_inverse_kernel(x_ref, mh_ref, ml_ref, twc_ref, tws_ref, out_ref, s_ref):
    lhs_re = jnp.concatenate([x_ref[:, 0:512].T, x_ref[:, 1024:1536].T], axis=0)
    lhs_im = jnp.concatenate([x_ref[:, 512:1024].T, x_ref[:, 1536:2048].T], axis=0)
    lhs = jnp.concatenate([lhs_re, lhs_im], axis=1)
    s_ref[...] = dot3(lhs, mh_ref[...], ml_ref[...])
    er, ei = [], []
    for k in range(32):
        rows = slice(32 * k, 32 * (k + 1))
        a = jnp.concatenate([s_ref[rows, 0:128], s_ref[rows, 256:384]], axis=1)
        b = jnp.concatenate([s_ref[rows, 128:256], s_ref[rows, 384:512]], axis=1)
        a, b = cmul(a, b, twc_ref[k:k + 1, :], tws_ref[k:k + 1, :])
        er.append(a)
        ei.append(b)
    tr, ti = fft_list(er, ei, 1)
    for t in range(8, 32):
        for p in range(2):
            out_ref[p, 0, :, (t - 8) * 128:(t - 7) * 128] = tr[t][:, 128 * p:128 * (p + 1)]
            out_ref[p, 1, :, (t - 8) * 128:(t - 7) * 128] = ti[t][:, 128 * p:128 * (p + 1)]


def call(kernel, out_shapes, scratch, *args):
    return pl.pallas_call(
        kernel,
        out_shape=[jax.ShapeDtypeStruct(s, F32) for s in out_shapes],
        scratch_shapes=[pltpu.VMEM(s, F32) for s in scratch],
        interpret=INTERPRET,
    )(*args)


def exchanged(block):
    rows, width = block.shape
    out = lax.all_to_all(block.reshape(32, rows // 32, width), "band", 0, 0, tiled=True)
    return out.reshape(rows, width)


def arranged(table):
    return table.reshape(32, 32, 4, 8, 4).transpose(3, 1, 2, 4, 0).reshape(1024, 128)


def per_device(voltages, chirp_phase):
    block = voltages[0, 0]
    band = lax.axis_index("band")
    history = passed_along(block[..., 3072 - HIST:], "seg", 1)

    i32 = jnp.int32
    lane = jnp.arange(1024, dtype=i32)[None, :]
    r_lane = 32 * band + lane % 32
    ka_lane = lane // 32
    t2c, t2s = unit(jnp.arange(32, dtype=i32)[None, :] * (32 * band + jnp.arange(32, dtype=i32)[:, None]), LENGTH, -1)
    q = jnp.arange(8, dtype=i32)[:, None]
    dd = jnp.arange(32, dtype=i32)[:, None]
    pac, pas = unit(32 * r_lane * (q % 4), LENGTH, -1)
    pbc, pbs = unit(128 * r_lane * dd, LENGTH, -1)
    kc_lane = 128 * band + ka_lane
    rl_lane = lane % 32
    rows = jnp.arange(256, dtype=i32)[:, None]

    back_c, back_s = unit((32 * (rows // 8) + lane % 32) * (kc_lane + 32 * (rows % 4)), LENGTH, 1)
    back_c, back_s, history = lax.optimization_barrier((back_c, back_s, history))

    t1c, t1s = lane_twiddle(-1, 128)
    index = lax.optimization_barrier(jnp.arange(512, dtype=jnp.int32))
    lr, li = built_send_matrices(index)
    (send,) = call(column_forward_kernel, [(256, 2048)], [(1024, 512)],
                   block, history, jnp.asarray(t1c), jnp.asarray(t1s), t2c, t2s,
                   *split_matrix(lr), *split_matrix(li), pac, pas, pbc, pbs)
    received = exchanged(send)

    chirp_phase, send = lax.optimization_barrier((chirp_phase, send))
    phases = gathered(chirp_phase, "seg", 1)[0]
    ch_c, ch_s = arranged(jnp.cos(phases)), arranged(jnp.sin(phases))

    twc, tws = row_twiddle(-1)
    (sent,) = call(row_kernel, [(256, 2048)], [(1024, 256), (1024, 256)],
                   received, jnp.asarray(twc), jnp.asarray(tws), *halves(row_block(-1)),
                   *halves(row_block(1)), ch_c, ch_s, back_c, back_s)
    returned = exchanged(sent)

    cc, cs = lane_twiddle(1, 256)
    (out,) = call(column_inverse_kernel, [(2, 2, ROWS_DEV, 3072)], [(1024, 512)],
                  returned, *split_matrix(built_receive_matrix(index)), jnp.asarray(cc), jnp.asarray(cs))
    return out[None, None]


def solution(mesh):
    in_specs = (P("seg", None, None, None, "band", None), P(None, "seg", "band"))
    out_specs = P("seg", None, None, None, "band", None)
    return jax.shard_map(
        per_device, mesh=mesh, in_specs=in_specs, out_specs=out_specs, check_vma=False
    )
```

```python
import math

import numpy as np
import jax
import jax.numpy as jnp
from jax import lax
from jax.experimental import pallas as pl
from jax.experimental.pallas import tpu as pltpu
from jax.sharding import PartitionSpec as P

INTERPRET = False
HIGHEST = lax.Precision.HIGHEST
F32 = jnp.float32
ROWS_DEV = 32
COLS = 4096
HIST = 1024
LENGTH = 1024 * 4096


def passed_along(block, axis, distance):
    devices = range(lax.axis_size(axis))
    route = [(i - distance, i) for i in devices if i - distance in devices]
    return lax.ppermute(block, axis, route)


def gathered(block, axis, dim):
    size = lax.axis_size(axis)
    pieces = [block]
    for shift in range(1, size):
        route = [((i + shift) % size, i) for i in range(size)]
        pieces.append(lax.ppermute(block, axis, route))
    ahead = jnp.stack(pieces, axis=0)
    ordered = jnp.roll(ahead, lax.axis_index(axis), axis=0)
    ordered = jnp.moveaxis(ordered, 0, dim)
    shape = list(block.shape)
    shape[dim] *= size
    return ordered.reshape(shape)


def fft_list(xr, xi, sign):
    n = len(xr)
    if n == 1:
        return list(xr), list(xi)
    er, ei = fft_list(xr[0::2], xi[0::2], sign)
    odd_r, odd_i = fft_list(xr[1::2], xi[1::2], sign)
    half = n // 2
    outr = [None] * n
    outi = [None] * n
    for k in range(half):
        a, b = odd_r[k], odd_i[k]
        if k == 0:
            tr, ti = a, b
        elif 4 * k == n:
            tr, ti = (-b, a) if sign > 0 else (b, -a)
        else:
            angle = sign * 2.0 * math.pi * k / n
            c, s = math.cos(angle), math.sin(angle)
            tr = a * c - b * s
            ti = a * s + b * c
        outr[k] = er[k] + tr
        outi[k] = ei[k] + ti
        outr[k + half] = er[k] - tr
        outi[k + half] = ei[k] - ti
    return outr, outi


BF16 = jnp.bfloat16


def split(x):
    hi = x.astype(BF16)
    return hi, (x - hi.astype(F32)).astype(BF16)


def dot3(a, b_hi, b_lo, dims=(((1,), (0,)), ((), ())), a_first=True):
    a_hi, a_lo = split(a)
    def one(x, y):
        if a_first:
            return lax.dot_general(x, y, dims, preferred_element_type=F32)
        return lax.dot_general(y, x, dims, preferred_element_type=F32)
    return one(a_hi, b_hi) + (one(a_lo, b_hi) + one(a_hi, b_lo))


def halves(m):
    hi = m.astype(BF16)
    lo = (m - hi.astype(np.float32)).astype(BF16)
    return jnp.asarray(hi), jnp.asarray(lo)


def unit(m, n, sign):
    angle = (m % n).astype(F32) * F32(sign * 2.0 * math.pi / n)
    return jnp.cos(angle), jnp.sin(angle)


def send_matrices():
    row = np.arange(256)
    dd, pp, ks = row // 8, (row // 4) % 2, row % 4
    k2 = 4 * dd + ks
    col = np.arange(512)
    pin, riin, lane = col // 256, (col // 128) % 2, col % 128
    ang = -2.0 * np.pi * np.outer(k2, lane) / 128.0
    c, s = np.cos(ang), np.sin(ang)
    same = (pp[:, None] == pin[None, :])
    real = np.where(riin[None, :] == 0, c, -s) * same
    imag = np.where(riin[None, :] == 0, s, c) * same
    return real.astype(np.float32), imag.astype(np.float32)


def row_block(sign):
    idx = np.arange(128)
    q, r = idx // 32, idx % 32
    ang = sign * 2.0 * np.pi * np.outer(r, r) / 32.0
    same = q[:, None] == q[None, :]
    wr = np.cos(ang) * same
    wi = np.sin(ang) * same
    top = np.concatenate([wr, wi], axis=1)
    bottom = np.concatenate([-wi, wr], axis=1)
    return np.concatenate([top, bottom], axis=0).astype(np.float32)


def row_twiddle(sign):
    g = np.arange(32)[:, None]
    r = (np.arange(512) % 32)[None, :]
    ang = sign * 2.0 * np.pi * (g * r) / 1024.0
    return np.cos(ang).astype(np.float32), np.sin(ang).astype(np.float32)


def receive_matrix():
    row = np.arange(512)
    riin, dd, pp, ks = row // 256, (row // 8) % 32, (row // 4) % 2, row % 4
    k2 = 4 * dd + ks
    col = np.arange(512)
    pout, riout, lc = col // 256, (col // 128) % 2, col % 128
    ang = 2.0 * np.pi * np.outer(k2, lc) / 128.0
    c, s = np.cos(ang), np.sin(ang)
    same = pp[:, None] == pout[None, :]
    val = np.where(riin[:, None] == 0,
                   np.where(riout[None, :] == 0, c, s),
                   np.where(riout[None, :] == 0, -s, c))
    return (val * same / LENGTH).astype(np.float32)


def lane_twiddle(sign, width):
    ka = np.arange(32)[:, None]
    lc = (np.arange(width) % 128)[None, :]
    ang = sign * 2.0 * np.pi * (ka * lc) / 4096.0
    return np.cos(ang).astype(np.float32), np.sin(ang).astype(np.float32)


def cmul(ar, ai, br, bi):
    return ar * br - ai * bi, ar * bi + ai * br


def column_forward_kernel(blk_ref, hist_ref, t1c, t1s, t2c, t2s, lrh, lrl, lih, lil, pac, pas, pbc, pbs,
                          out_ref, xs_ref):
    tw = [cmul(t1c[k:k + 1, :], t1s[k:k + 1, :], t2c[:, k:k + 1], t2s[:, k:k + 1]) for k in range(32)]
    for p in range(2):
        xr, xi = [], []
        for t in range(32):
            if t < 8:
                xr.append(hist_ref[p, 0, :, t * 128:(t + 1) * 128])
                xi.append(hist_ref[p, 1, :, t * 128:(t + 1) * 128])
            else:
                xr.append(blk_ref[p, 0, :, (t - 8) * 128:(t - 7) * 128])
                xi.append(blk_ref[p, 1, :, (t - 8) * 128:(t - 7) * 128])
        ar, ai = fft_list(xr, xi, -1)
        for k in range(32):
            re, im = cmul(ar[k], ai[k], *tw[k])
            xs_ref[k * 32:(k + 1) * 32, p * 256:p * 256 + 128] = re
            xs_ref[k * 32:(k + 1) * 32, p * 256 + 128:p * 256 + 256] = im
    dims = (((1,), (1,)), ((), ()))
    for h in range(2):
        x = xs_ref[512 * h:512 * (h + 1), :]
        ore = dot3(x, lrh[...], lrl[...], dims, a_first=False)
        oim = dot3(x, lih[...], lil[...], dims, a_first=False)
        ac = pac[:, 512 * h:512 * (h + 1)]
        as_ = pas[:, 512 * h:512 * (h + 1)]
        for d in range(32):
            bc = pbc[d:d + 1, 512 * h:512 * (h + 1)]
            bs = pbs[d:d + 1, 512 * h:512 * (h + 1)]
            wc, ws = cmul(ac, as_, bc, bs)
            re, im = cmul(ore[8 * d:8 * d + 8], oim[8 * d:8 * d + 8], wc, ws)
            out_ref[8 * d:8 * d + 8, 1024 * h:1024 * h + 512] = re
            out_ref[8 * d:8 * d + 8, 1024 * h + 512:1024 * h + 1024] = im


def row_kernel(x_ref, twc_ref, tws_ref, bfh, bfl, bbh, bbl, chc_ref, chs_ref, pc_ref, ps_ref, out_ref, y_ref, w_ref):
    for h in range(2):
        row_half(h, x_ref, twc_ref, tws_ref, bfh, bfl, bbh, bbl, chc_ref, chs_ref, pc_ref, ps_ref, out_ref, y_ref, w_ref)


def row_half(h, x_ref, twc_ref, tws_ref, bfh, bfl, bbh, bbl, chc_ref, chs_ref, pc_ref, ps_ref, out_ref, y_ref, w_ref):
    base = 1024 * h
    lanes = slice(512 * h, 512 * (h + 1))
    er = [x_ref[8 * d:8 * d + 8, base:base + 512] for d in range(32)]
    ei = [x_ref[8 * d:8 * d + 8, base + 512:base + 1024] for d in range(32)]
    fr, fi = fft_list(er, ei, -1)
    for g in range(32):
        a, b = cmul(fr[g], fi[g], twc_ref[g:g + 1, :], tws_ref[g:g + 1, :])
        for p in range(2):
            for j in range(4):
                at = 512 * p + 128 * j + 4 * g
                y_ref[at:at + 4, 0:128] = a[4 * p:4 * p + 4, 128 * j:128 * (j + 1)]
                y_ref[at:at + 4, 128:256] = b[4 * p:4 * p + 4, 128 * j:128 * (j + 1)]
    z = dot3(y_ref[...], bfh[...], bfl[...])
    c = chc_ref[512 * h:512 * (h + 1), :]
    s = chs_ref[512 * h:512 * (h + 1), :]
    for p in range(2):
        rows = slice(512 * p, 512 * (p + 1))
        re, im = cmul(z[rows, 0:128], z[rows, 128:256], c, s)
        y_ref[rows, 0:128] = re
        y_ref[rows, 128:256] = im
    w_ref[...] = dot3(y_ref[...], bbh[...], bbl[...])
    gr, gi = [], []
    for g in range(32):
        pa, pb = [], []
        for j in range(4):
            lo, hi = 128 * j + 4 * g, 512 + 128 * j + 4 * g
            pa.append(jnp.concatenate([w_ref[lo:lo + 4, 0:128], w_ref[hi:hi + 4, 0:128]], axis=0))
            pb.append(jnp.concatenate([w_ref[lo:lo + 4, 128:256], w_ref[hi:hi + 4, 128:256]], axis=0))
        a, b = cmul(jnp.concatenate(pa, axis=1), jnp.concatenate(pb, axis=1), twc_ref[g:g + 1, :], -tws_ref[g:g + 1, :])
        gr.append(a)
        gi.append(b)
    ur, ui = fft_list(gr, gi, 1)
    for d in range(32):
        re, im = cmul(ur[d], ui[d], pc_ref[8 * d:8 * d + 8, lanes], ps_ref[8 * d:8 * d + 8, lanes])
        out_ref[8 * d:8 * d + 8, base:base + 512] = re
        out_ref[8 * d:8 * d + 8, base + 512:base + 1024] = im


def column_inverse_kernel(x_ref, mh_ref, ml_ref, twc_ref, tws_ref, out_ref, s_ref):
    lhs_re = jnp.concatenate([x_ref[:, 0:512].T, x_ref[:, 1024:1536].T], axis=0)
    lhs_im = jnp.concatenate([x_ref[:, 512:1024].T, x_ref[:, 1536:2048].T], axis=0)
    lhs = jnp.concatenate([lhs_re, lhs_im], axis=1)
    s_ref[...] = dot3(lhs, mh_ref[...], ml_ref[...])
    er, ei = [], []
    for k in range(32):
        rows = slice(32 * k, 32 * (k + 1))
        a = jnp.concatenate([s_ref[rows, 0:128], s_ref[rows, 256:384]], axis=1)
        b = jnp.concatenate([s_ref[rows, 128:256], s_ref[rows, 384:512]], axis=1)
        a, b = cmul(a, b, twc_ref[k:k + 1, :], tws_ref[k:k + 1, :])
        er.append(a)
        ei.append(b)
    tr, ti = fft_list(er, ei, 1)
    for t in range(8, 32):
        for p in range(2):
            out_ref[p, 0, :, (t - 8) * 128:(t - 7) * 128] = tr[t][:, 128 * p:128 * (p + 1)]
            out_ref[p, 1, :, (t - 8) * 128:(t - 7) * 128] = ti[t][:, 128 * p:128 * (p + 1)]


def call(kernel, out_shapes, scratch, *args):
    return pl.pallas_call(
        kernel,
        out_shape=[jax.ShapeDtypeStruct(s, F32) for s in out_shapes],
        scratch_shapes=[pltpu.VMEM(s, F32) for s in scratch],
        interpret=INTERPRET,
    )(*args)


def exchanged(block):
    rows, width = block.shape
    out = lax.all_to_all(block.reshape(32, rows // 32, width), "band", 0, 0, tiled=True)
    return out.reshape(rows, width)


def arranged(table):
    return table.reshape(32, 32, 4, 8, 4).transpose(3, 1, 2, 4, 0).reshape(1024, 128)


def per_device(voltages, chirp_phase):
    block = voltages[0, 0]
    band = lax.axis_index("band")
    history = passed_along(block[..., 3072 - HIST:], "seg", 1)

    i32 = jnp.int32
    lane = jnp.arange(1024, dtype=i32)[None, :]
    r_lane = 32 * band + lane % 32
    ka_lane = lane // 32
    t2c, t2s = unit(jnp.arange(32, dtype=i32)[None, :] * (32 * band + jnp.arange(32, dtype=i32)[:, None]), LENGTH, -1)
    q = jnp.arange(8, dtype=i32)[:, None]
    dd = jnp.arange(32, dtype=i32)[:, None]
    pac, pas = unit(32 * r_lane * (q % 4), LENGTH, -1)
    pbc, pbs = unit(128 * r_lane * dd, LENGTH, -1)
    kc_lane = 128 * band + ka_lane
    rl_lane = lane % 32
    rows = jnp.arange(256, dtype=i32)[:, None]

    back_c, back_s = unit((32 * (rows // 8) + lane % 32) * (kc_lane + 32 * (rows % 4)), LENGTH, 1)
    back_c, back_s, history = lax.optimization_barrier((back_c, back_s, history))

    t1c, t1s = lane_twiddle(-1, 128)
    lr, li = send_matrices()
    (send,) = call(column_forward_kernel, [(256, 2048)], [(1024, 512)],
                   block, history, jnp.asarray(t1c), jnp.asarray(t1s), t2c, t2s,
                   *halves(lr), *halves(li), pac, pas, pbc, pbs)
    received = exchanged(send)

    chirp_phase, send = lax.optimization_barrier((chirp_phase, send))
    phases = gathered(chirp_phase, "seg", 1)[0]
    ch_c, ch_s = arranged(jnp.cos(phases)), arranged(jnp.sin(phases))

    twc, tws = row_twiddle(-1)
    (sent,) = call(row_kernel, [(256, 2048)], [(1024, 256), (1024, 256)],
                   received, jnp.asarray(twc), jnp.asarray(tws), *halves(row_block(-1)),
                   *halves(row_block(1)), ch_c, ch_s, back_c, back_s)
    returned = exchanged(sent)

    cc, cs = lane_twiddle(1, 256)
    (out,) = call(column_inverse_kernel, [(2, 2, ROWS_DEV, 3072)], [(1024, 512)],
                  returned, *halves(receive_matrix()), jnp.asarray(cc), jnp.asarray(cs))
    return out[None, None]


def solution(mesh):
    in_specs = (P("seg", None, None, None, "band", None), P(None, "seg", "band"))
    out_specs = P("seg", None, None, None, "band", None)
    return jax.shard_map(
        per_device, mesh=mesh, in_specs=in_specs, out_specs=out_specs, check_vma=False
    )
```

```python
import math

import numpy as np
import jax
import jax.numpy as jnp
from jax import lax
from jax.experimental import pallas as pl
from jax.experimental.pallas import tpu as pltpu
from jax.sharding import PartitionSpec as P

INTERPRET = False
HIGHEST = lax.Precision.HIGHEST
F32 = jnp.float32
ROWS_DEV = 32
COLS = 4096
HIST = 1024
LENGTH = 1024 * 4096


def passed_along(block, axis, distance):
    devices = range(lax.axis_size(axis))
    route = [(i - distance, i) for i in devices if i - distance in devices]
    return lax.ppermute(block, axis, route)


def gathered(block, axis, dim):
    size = lax.axis_size(axis)
    pieces = [block]
    for shift in range(1, size):
        route = [((i + shift) % size, i) for i in range(size)]
        pieces.append(lax.ppermute(block, axis, route))
    ahead = jnp.stack(pieces, axis=0)
    ordered = jnp.roll(ahead, lax.axis_index(axis), axis=0)
    ordered = jnp.moveaxis(ordered, 0, dim)
    shape = list(block.shape)
    shape[dim] *= size
    return ordered.reshape(shape)


def fft_list(xr, xi, sign):
    n = len(xr)
    if n == 1:
        return list(xr), list(xi)
    er, ei = fft_list(xr[0::2], xi[0::2], sign)
    odd_r, odd_i = fft_list(xr[1::2], xi[1::2], sign)
    half = n // 2
    outr = [None] * n
    outi = [None] * n
    for k in range(half):
        a, b = odd_r[k], odd_i[k]
        if k == 0:
            tr, ti = a, b
        elif 4 * k == n:
            tr, ti = (-b, a) if sign > 0 else (b, -a)
        else:
            angle = sign * 2.0 * math.pi * k / n
            c, s = math.cos(angle), math.sin(angle)
            tr = a * c - b * s
            ti = a * s + b * c
        outr[k] = er[k] + tr
        outi[k] = ei[k] + ti
        outr[k + half] = er[k] - tr
        outi[k + half] = ei[k] - ti
    return outr, outi


BF16 = jnp.bfloat16


def split(x):
    hi = x.astype(BF16)
    return hi, (x - hi.astype(F32)).astype(BF16)


def dot3(a, b_hi, b_lo, dims=(((1,), (0,)), ((), ())), a_first=True):
    a_hi, a_lo = split(a)
    def one(x, y):
        if a_first:
            return lax.dot_general(x, y, dims, preferred_element_type=F32)
        return lax.dot_general(y, x, dims, preferred_element_type=F32)
    return one(a_hi, b_hi) + (one(a_lo, b_hi) + one(a_hi, b_lo))


def halves(m):
    hi = m.astype(BF16)
    lo = (m - hi.astype(np.float32)).astype(BF16)
    return jnp.asarray(hi), jnp.asarray(lo)


def unit(m, n, sign):
    angle = (m % n).astype(F32) * F32(sign * 2.0 * math.pi / n)
    return jnp.cos(angle), jnp.sin(angle)


def send_matrices():
    row = np.arange(256)
    dd, pp, ks = row // 8, (row // 4) % 2, row % 4
    k2 = 4 * dd + ks
    col = np.arange(512)
    pin, riin, lane = col // 256, (col // 128) % 2, col % 128
    ang = -2.0 * np.pi * np.outer(k2, lane) / 128.0
    c, s = np.cos(ang), np.sin(ang)
    same = (pp[:, None] == pin[None, :])
    real = np.where(riin[None, :] == 0, c, -s) * same
    imag = np.where(riin[None, :] == 0, s, c) * same
    return real.astype(np.float32), imag.astype(np.float32)


def row_block(sign):
    idx = np.arange(128)
    q, r = idx // 32, idx % 32
    ang = sign * 2.0 * np.pi * np.outer(r, r) / 32.0
    same = q[:, None] == q[None, :]
    wr = np.cos(ang) * same
    wi = np.sin(ang) * same
    top = np.concatenate([wr, wi], axis=1)
    bottom = np.concatenate([-wi, wr], axis=1)
    return np.concatenate([top, bottom], axis=0).astype(np.float32)


def row_twiddle(sign):
    g = np.arange(32)[:, None]
    r = (np.arange(512) % 32)[None, :]
    ang = sign * 2.0 * np.pi * (g * r) / 1024.0
    return np.cos(ang).astype(np.float32), np.sin(ang).astype(np.float32)


def receive_matrix():
    row = np.arange(512)
    riin, dd, pp, ks = row // 256, (row // 8) % 32, (row // 4) % 2, row % 4
    k2 = 4 * dd + ks
    col = np.arange(512)
    pout, riout, lc = col // 256, (col // 128) % 2, col % 128
    ang = 2.0 * np.pi * np.outer(k2, lc) / 128.0
    c, s = np.cos(ang), np.sin(ang)
    same = pp[:, None] == pout[None, :]
    val = np.where(riin[:, None] == 0,
                   np.where(riout[None, :] == 0, c, s),
                   np.where(riout[None, :] == 0, -s, c))
    return (val * same / LENGTH).astype(np.float32)


def lane_twiddle(sign, width):
    ka = np.arange(32)[:, None]
    lc = (np.arange(width) % 128)[None, :]
    ang = sign * 2.0 * np.pi * (ka * lc) / 4096.0
    return np.cos(ang).astype(np.float32), np.sin(ang).astype(np.float32)


def cmul(ar, ai, br, bi):
    return ar * br - ai * bi, ar * bi + ai * br


def column_forward_kernel(blk_ref, hist_ref, t1c, t1s, t2c, t2s, lh, ll, pac, pas, pbc, pbs,
                          out_ref, xs_ref):
    tw = [cmul(t1c[k:k + 1, :], t1s[k:k + 1, :], t2c[:, k:k + 1], t2s[:, k:k + 1]) for k in range(32)]
    for p in range(2):
        xr, xi = [], []
        for t in range(32):
            if t < 8:
                xr.append(hist_ref[p, 0, :, t * 128:(t + 1) * 128])
                xi.append(hist_ref[p, 1, :, t * 128:(t + 1) * 128])
            else:
                xr.append(blk_ref[p, 0, :, (t - 8) * 128:(t - 7) * 128])
                xi.append(blk_ref[p, 1, :, (t - 8) * 128:(t - 7) * 128])
        ar, ai = fft_list(xr, xi, -1)
        for k in range(32):
            re, im = cmul(ar[k], ai[k], *tw[k])
            xs_ref[k * 32:(k + 1) * 32, p * 256:p * 256 + 128] = re
            xs_ref[k * 32:(k + 1) * 32, p * 256 + 128:p * 256 + 256] = im
    dims = (((1,), (1,)), ((), ()))
    for h in range(2):
        x = xs_ref[512 * h:512 * (h + 1), :]
        both = dot3(x, lh[...], ll[...], dims, a_first=False)
        ore = both[0:256]
        oim = both[256:512]
        ac = pac[:, 512 * h:512 * (h + 1)]
        as_ = pas[:, 512 * h:512 * (h + 1)]
        for d in range(32):
            bc = pbc[d:d + 1, 512 * h:512 * (h + 1)]
            bs = pbs[d:d + 1, 512 * h:512 * (h + 1)]
            wc, ws = cmul(ac, as_, bc, bs)
            re, im = cmul(ore[8 * d:8 * d + 8], oim[8 * d:8 * d + 8], wc, ws)
            out_ref[8 * d:8 * d + 8, 1024 * h:1024 * h + 512] = re
            out_ref[8 * d:8 * d + 8, 1024 * h + 512:1024 * h + 1024] = im


def row_kernel(x_ref, twc_ref, tws_ref, bfh, bfl, bbh, bbl, chc_ref, chs_ref, pc_ref, ps_ref, out_ref, y_ref, w_ref):
    for h in range(2):
        row_half(h, x_ref, twc_ref, tws_ref, bfh, bfl, bbh, bbl, chc_ref, chs_ref, pc_ref, ps_ref, out_ref, y_ref, w_ref)


def row_half(h, x_ref, twc_ref, tws_ref, bfh, bfl, bbh, bbl, chc_ref, chs_ref, pc_ref, ps_ref, out_ref, y_ref, w_ref):
    base = 1024 * h
    lanes = slice(512 * h, 512 * (h + 1))
    er = [x_ref[8 * d:8 * d + 8, base:base + 512] for d in range(32)]
    ei = [x_ref[8 * d:8 * d + 8, base + 512:base + 1024] for d in range(32)]
    fr, fi = fft_list(er, ei, -1)
    for g in range(32):
        a, b = cmul(fr[g], fi[g], twc_ref[g:g + 1, :], tws_ref[g:g + 1, :])
        for p in range(2):
            for j in range(4):
                at = 512 * p + 128 * j + 4 * g
                y_ref[at:at + 4, 0:128] = a[4 * p:4 * p + 4, 128 * j:128 * (j + 1)]
                y_ref[at:at + 4, 128:256] = b[4 * p:4 * p + 4, 128 * j:128 * (j + 1)]
    z = dot3(y_ref[...], bfh[...], bfl[...])
    c = chc_ref[512 * h:512 * (h + 1), :]
    s = chs_ref[512 * h:512 * (h + 1), :]
    for p in range(2):
        rows = slice(512 * p, 512 * (p + 1))
        re, im = cmul(z[rows, 0:128], z[rows, 128:256], c, s)
        y_ref[rows, 0:128] = re
        y_ref[rows, 128:256] = im
    w_ref[...] = dot3(y_ref[...], bbh[...], bbl[...])
    gr, gi = [], []
    for g in range(32):
        pa, pb = [], []
        for j in range(4):
            lo, hi = 128 * j + 4 * g, 512 + 128 * j + 4 * g
            pa.append(jnp.concatenate([w_ref[lo:lo + 4, 0:128], w_ref[hi:hi + 4, 0:128]], axis=0))
            pb.append(jnp.concatenate([w_ref[lo:lo + 4, 128:256], w_ref[hi:hi + 4, 128:256]], axis=0))
        a, b = cmul(jnp.concatenate(pa, axis=1), jnp.concatenate(pb, axis=1), twc_ref[g:g + 1, :], -tws_ref[g:g + 1, :])
        gr.append(a)
        gi.append(b)
    ur, ui = fft_list(gr, gi, 1)
    for d in range(32):
        re, im = cmul(ur[d], ui[d], pc_ref[8 * d:8 * d + 8, lanes], ps_ref[8 * d:8 * d + 8, lanes])
        out_ref[8 * d:8 * d + 8, base:base + 512] = re
        out_ref[8 * d:8 * d + 8, base + 512:base + 1024] = im


def column_inverse_kernel(x_ref, mh_ref, ml_ref, twc_ref, tws_ref, out_ref, s_ref):
    lhs_re = jnp.concatenate([x_ref[:, 0:512].T, x_ref[:, 1024:1536].T], axis=0)
    lhs_im = jnp.concatenate([x_ref[:, 512:1024].T, x_ref[:, 1536:2048].T], axis=0)
    lhs = jnp.concatenate([lhs_re, lhs_im], axis=1)
    s_ref[...] = dot3(lhs, mh_ref[...], ml_ref[...])
    er, ei = [], []
    for k in range(32):
        rows = slice(32 * k, 32 * (k + 1))
        a = jnp.concatenate([s_ref[rows, 0:128], s_ref[rows, 256:384]], axis=1)
        b = jnp.concatenate([s_ref[rows, 128:256], s_ref[rows, 384:512]], axis=1)
        a, b = cmul(a, b, twc_ref[k:k + 1, :], tws_ref[k:k + 1, :])
        er.append(a)
        ei.append(b)
    tr, ti = fft_list(er, ei, 1)
    for t in range(8, 32):
        for p in range(2):
            out_ref[p, 0, :, (t - 8) * 128:(t - 7) * 128] = tr[t][:, 128 * p:128 * (p + 1)]
            out_ref[p, 1, :, (t - 8) * 128:(t - 7) * 128] = ti[t][:, 128 * p:128 * (p + 1)]


def call(kernel, out_shapes, scratch, *args):
    return pl.pallas_call(
        kernel,
        out_shape=[jax.ShapeDtypeStruct(s, F32) for s in out_shapes],
        scratch_shapes=[pltpu.VMEM(s, F32) for s in scratch],
        interpret=INTERPRET,
    )(*args)


def exchanged(block):
    rows, width = block.shape
    out = lax.all_to_all(block.reshape(32, rows // 32, width), "band", 0, 0, tiled=True)
    return out.reshape(rows, width)


def arranged(table):
    return table.reshape(32, 32, 4, 8, 4).transpose(3, 1, 2, 4, 0).reshape(1024, 128)


def per_device(voltages, chirp_phase):
    block = voltages[0, 0]
    band = lax.axis_index("band")
    history = passed_along(block[..., 3072 - HIST:], "seg", 1)

    i32 = jnp.int32
    lane = jnp.arange(1024, dtype=i32)[None, :]
    r_lane = 32 * band + lane % 32
    ka_lane = lane // 32
    t2c, t2s = unit(jnp.arange(32, dtype=i32)[None, :] * (32 * band + jnp.arange(32, dtype=i32)[:, None]), LENGTH, -1)
    q = jnp.arange(8, dtype=i32)[:, None]
    dd = jnp.arange(32, dtype=i32)[:, None]
    pac, pas = unit(32 * r_lane * (q % 4), LENGTH, -1)
    pbc, pbs = unit(128 * r_lane * dd, LENGTH, -1)
    kc_lane = 128 * band + ka_lane
    rl_lane = lane % 32
    rows = jnp.arange(256, dtype=i32)[:, None]

    back_c, back_s = unit((32 * (rows // 8) + lane % 32) * (kc_lane + 32 * (rows % 4)), LENGTH, 1)
    back_c, back_s, history = lax.optimization_barrier((back_c, back_s, history))

    t1c, t1s = lane_twiddle(-1, 128)
    lr, li = send_matrices()
    (send,) = call(column_forward_kernel, [(256, 2048)], [(1024, 512)],
                   block, history, jnp.asarray(t1c), jnp.asarray(t1s), t2c, t2s,
                   *halves(np.concatenate([lr, li], axis=0)), pac, pas, pbc, pbs)
    received = exchanged(send)

    chirp_phase, send = lax.optimization_barrier((chirp_phase, send))
    phases = gathered(chirp_phase, "seg", 1)[0]
    ch_c, ch_s = arranged(jnp.cos(phases)), arranged(jnp.sin(phases))

    twc, tws = row_twiddle(-1)
    (sent,) = call(row_kernel, [(256, 2048)], [(1024, 256), (1024, 256)],
                   received, jnp.asarray(twc), jnp.asarray(tws), *halves(row_block(-1)),
                   *halves(row_block(1)), ch_c, ch_s, back_c, back_s)
    returned = exchanged(sent)

    cc, cs = lane_twiddle(1, 256)
    (out,) = call(column_inverse_kernel, [(2, 2, ROWS_DEV, 3072)], [(1024, 512)],
                  returned, *halves(receive_matrix()), jnp.asarray(cc), jnp.asarray(cs))
    return out[None, None]


def solution(mesh):
    in_specs = (P("seg", None, None, None, "band", None), P(None, "seg", "band"))
    out_specs = P("seg", None, None, None, "band", None)
    return jax.shard_map(
        per_device, mesh=mesh, in_specs=in_specs, out_specs=out_specs, check_vma=False
    )
```

```python
import math

import numpy as np
import jax
import jax.numpy as jnp
from jax import lax
from jax.experimental import pallas as pl
from jax.experimental.pallas import tpu as pltpu
from jax.sharding import PartitionSpec as P

INTERPRET = False
HIGHEST = lax.Precision.HIGHEST
F32 = jnp.float32
ROWS_DEV = 32
COLS = 4096
HIST = 1024
LENGTH = 1024 * 4096


def passed_along(block, axis, distance):
    devices = range(lax.axis_size(axis))
    route = [(i - distance, i) for i in devices if i - distance in devices]
    return lax.ppermute(block, axis, route)


def gathered(block, axis, dim):
    size = lax.axis_size(axis)
    pieces = [block]
    for shift in range(1, size):
        route = [((i + shift) % size, i) for i in range(size)]
        pieces.append(lax.ppermute(block, axis, route))
    ahead = jnp.stack(pieces, axis=0)
    ordered = jnp.roll(ahead, lax.axis_index(axis), axis=0)
    ordered = jnp.moveaxis(ordered, 0, dim)
    shape = list(block.shape)
    shape[dim] *= size
    return ordered.reshape(shape)


def fft_list(xr, xi, sign):
    n = len(xr)
    if n == 1:
        return list(xr), list(xi)
    er, ei = fft_list(xr[0::2], xi[0::2], sign)
    odd_r, odd_i = fft_list(xr[1::2], xi[1::2], sign)
    half = n // 2
    outr = [None] * n
    outi = [None] * n
    for k in range(half):
        a, b = odd_r[k], odd_i[k]
        if k == 0:
            tr, ti = a, b
        elif 4 * k == n:
            tr, ti = (-b, a) if sign > 0 else (b, -a)
        else:
            angle = sign * 2.0 * math.pi * k / n
            c, s = math.cos(angle), math.sin(angle)
            tr = a * c - b * s
            ti = a * s + b * c
        outr[k] = er[k] + tr
        outi[k] = ei[k] + ti
        outr[k + half] = er[k] - tr
        outi[k + half] = ei[k] - ti
    return outr, outi


BF16 = jnp.bfloat16


def split(x):
    hi = x.astype(BF16)
    return hi, (x - hi.astype(F32)).astype(BF16)


def dot3(a, b_hi, b_lo, dims=(((1,), (0,)), ((), ())), a_first=True):
    a_hi, a_lo = split(a)
    def one(x, y):
        if a_first:
            return lax.dot_general(x, y, dims, preferred_element_type=F32)
        return lax.dot_general(y, x, dims, preferred_element_type=F32)
    return one(a_hi, b_hi) + (one(a_lo, b_hi) + one(a_hi, b_lo))


def halves(m):
    hi = m.astype(BF16)
    lo = (m - hi.astype(np.float32)).astype(BF16)
    return jnp.asarray(hi), jnp.asarray(lo)


def unit(m, n, sign):
    angle = (m % n).astype(F32) * F32(sign * 2.0 * math.pi / n)
    return jnp.cos(angle), jnp.sin(angle)


def send_matrices():
    row = np.arange(256)
    dd, pp, ks = row // 8, (row // 4) % 2, row % 4
    k2 = 4 * dd + ks
    col = np.arange(512)
    pin, riin, lane = col // 256, (col // 128) % 2, col % 128
    ang = -2.0 * np.pi * np.outer(k2, lane) / 128.0
    c, s = np.cos(ang), np.sin(ang)
    same = (pp[:, None] == pin[None, :])
    real = np.where(riin[None, :] == 0, c, -s) * same
    imag = np.where(riin[None, :] == 0, s, c) * same
    return real.astype(np.float32), imag.astype(np.float32)


def row_block(sign):
    idx = np.arange(128)
    q, r = idx // 32, idx % 32
    ang = sign * 2.0 * np.pi * np.outer(r, r) / 32.0
    same = q[:, None] == q[None, :]
    wr = np.cos(ang) * same
    wi = np.sin(ang) * same
    top = np.concatenate([wr, wi], axis=1)
    bottom = np.concatenate([-wi, wr], axis=1)
    return np.concatenate([top, bottom], axis=0).astype(np.float32)


def row_twiddle(sign):
    g = np.arange(32)[:, None]
    r = (np.arange(512) % 32)[None, :]
    ang = sign * 2.0 * np.pi * (g * r) / 1024.0
    return np.cos(ang).astype(np.float32), np.sin(ang).astype(np.float32)


def receive_matrix():
    row = np.arange(512)
    riin, dd, pp, ks = row // 256, (row // 8) % 32, (row // 4) % 2, row % 4
    k2 = 4 * dd + ks
    col = np.arange(512)
    pout, riout, lc = col // 256, (col // 128) % 2, col % 128
    ang = 2.0 * np.pi * np.outer(k2, lc) / 128.0
    c, s = np.cos(ang), np.sin(ang)
    same = pp[:, None] == pout[None, :]
    val = np.where(riin[:, None] == 0,
                   np.where(riout[None, :] == 0, c, s),
                   np.where(riout[None, :] == 0, -s, c))
    return (val * same / LENGTH).astype(np.float32)


def lane_twiddle(sign, width):
    ka = np.arange(32)[:, None]
    lc = (np.arange(width) % 128)[None, :]
    ang = sign * 2.0 * np.pi * (ka * lc) / 4096.0
    return np.cos(ang).astype(np.float32), np.sin(ang).astype(np.float32)


def cmul(ar, ai, br, bi):
    return ar * br - ai * bi, ar * bi + ai * br


def column_forward_kernel(blk_ref, hist_ref, t1c, t1s, t2c, t2s, lrh, lrl, lih, lil, pac, pas, pbc, pbs,
                          out_ref, xs_ref):
    tw = [cmul(t1c[k:k + 1, :], t1s[k:k + 1, :], t2c[:, k:k + 1], t2s[:, k:k + 1]) for k in range(32)]
    for p in range(2):
        xr, xi = [], []
        for t in range(32):
            if t < 8:
                xr.append(hist_ref[p, 0, :, t * 128:(t + 1) * 128])
                xi.append(hist_ref[p, 1, :, t * 128:(t + 1) * 128])
            else:
                xr.append(blk_ref[p, 0, :, (t - 8) * 128:(t - 7) * 128])
                xi.append(blk_ref[p, 1, :, (t - 8) * 128:(t - 7) * 128])
        ar, ai = fft_list(xr, xi, -1)
        for k in range(32):
            re, im = cmul(ar[k], ai[k], *tw[k])
            xs_ref[k * 32:(k + 1) * 32, p * 256:p * 256 + 128] = re
            xs_ref[k * 32:(k + 1) * 32, p * 256 + 128:p * 256 + 256] = im
    dims = (((1,), (1,)), ((), ()))
    for h in range(2):
        x = xs_ref[512 * h:512 * (h + 1), :]
        ore = dot3(x, lrh[...], lrl[...], dims, a_first=False)
        oim = dot3(x, lih[...], lil[...], dims, a_first=False)
        for d in range(32):
            wc = pac[8 * d:8 * d + 8, 512 * h:512 * (h + 1)]
            ws = pas[8 * d:8 * d + 8, 512 * h:512 * (h + 1)]
            re, im = cmul(ore[8 * d:8 * d + 8], oim[8 * d:8 * d + 8], wc, ws)
            out_ref[8 * d:8 * d + 8, 1024 * h:1024 * h + 512] = re
            out_ref[8 * d:8 * d + 8, 1024 * h + 512:1024 * h + 1024] = im


def row_kernel(x_ref, twc_ref, tws_ref, bfh, bfl, bbh, bbl, chc_ref, chs_ref, pc_ref, ps_ref, out_ref, y_ref, w_ref):
    for h in range(2):
        row_half(h, x_ref, twc_ref, tws_ref, bfh, bfl, bbh, bbl, chc_ref, chs_ref, pc_ref, ps_ref, out_ref, y_ref, w_ref)


def row_half(h, x_ref, twc_ref, tws_ref, bfh, bfl, bbh, bbl, chc_ref, chs_ref, pc_ref, ps_ref, out_ref, y_ref, w_ref):
    base = 1024 * h
    lanes = slice(512 * h, 512 * (h + 1))
    er = [x_ref[8 * d:8 * d + 8, base:base + 512] for d in range(32)]
    ei = [x_ref[8 * d:8 * d + 8, base + 512:base + 1024] for d in range(32)]
    fr, fi = fft_list(er, ei, -1)
    for g in range(32):
        a, b = cmul(fr[g], fi[g], twc_ref[g:g + 1, :], tws_ref[g:g + 1, :])
        for p in range(2):
            for j in range(4):
                at = 512 * p + 128 * j + 4 * g
                y_ref[at:at + 4, 0:128] = a[4 * p:4 * p + 4, 128 * j:128 * (j + 1)]
                y_ref[at:at + 4, 128:256] = b[4 * p:4 * p + 4, 128 * j:128 * (j + 1)]
    z = dot3(y_ref[...], bfh[...], bfl[...])
    c = chc_ref[512 * h:512 * (h + 1), :]
    s = chs_ref[512 * h:512 * (h + 1), :]
    for p in range(2):
        rows = slice(512 * p, 512 * (p + 1))
        re, im = cmul(z[rows, 0:128], z[rows, 128:256], c, s)
        y_ref[rows, 0:128] = re
        y_ref[rows, 128:256] = im
    w_ref[...] = dot3(y_ref[...], bbh[...], bbl[...])
    gr, gi = [], []
    for g in range(32):
        pa, pb = [], []
        for j in range(4):
            lo, hi = 128 * j + 4 * g, 512 + 128 * j + 4 * g
            pa.append(jnp.concatenate([w_ref[lo:lo + 4, 0:128], w_ref[hi:hi + 4, 0:128]], axis=0))
            pb.append(jnp.concatenate([w_ref[lo:lo + 4, 128:256], w_ref[hi:hi + 4, 128:256]], axis=0))
        a, b = cmul(jnp.concatenate(pa, axis=1), jnp.concatenate(pb, axis=1), twc_ref[g:g + 1, :], -tws_ref[g:g + 1, :])
        gr.append(a)
        gi.append(b)
    ur, ui = fft_list(gr, gi, 1)
    for d in range(32):
        re, im = cmul(ur[d], ui[d], pc_ref[8 * d:8 * d + 8, lanes], ps_ref[8 * d:8 * d + 8, lanes])
        out_ref[8 * d:8 * d + 8, base:base + 512] = re
        out_ref[8 * d:8 * d + 8, base + 512:base + 1024] = im


def column_inverse_kernel(x_ref, mh_ref, ml_ref, twc_ref, tws_ref, out_ref, s_ref):
    lhs_re = jnp.concatenate([x_ref[:, 0:512].T, x_ref[:, 1024:1536].T], axis=0)
    lhs_im = jnp.concatenate([x_ref[:, 512:1024].T, x_ref[:, 1536:2048].T], axis=0)
    lhs = jnp.concatenate([lhs_re, lhs_im], axis=1)
    s_ref[...] = dot3(lhs, mh_ref[...], ml_ref[...])
    er, ei = [], []
    for k in range(32):
        rows = slice(32 * k, 32 * (k + 1))
        a = jnp.concatenate([s_ref[rows, 0:128], s_ref[rows, 256:384]], axis=1)
        b = jnp.concatenate([s_ref[rows, 128:256], s_ref[rows, 384:512]], axis=1)
        a, b = cmul(a, b, twc_ref[k:k + 1, :], tws_ref[k:k + 1, :])
        er.append(a)
        ei.append(b)
    tr, ti = fft_list(er, ei, 1)
    for t in range(8, 32):
        for p in range(2):
            out_ref[p, 0, :, (t - 8) * 128:(t - 7) * 128] = tr[t][:, 128 * p:128 * (p + 1)]
            out_ref[p, 1, :, (t - 8) * 128:(t - 7) * 128] = ti[t][:, 128 * p:128 * (p + 1)]


def call(kernel, out_shapes, scratch, *args):
    return pl.pallas_call(
        kernel,
        out_shape=[jax.ShapeDtypeStruct(s, F32) for s in out_shapes],
        scratch_shapes=[pltpu.VMEM(s, F32) for s in scratch],
        interpret=INTERPRET,
    )(*args)


def exchanged(block):
    rows, width = block.shape
    out = lax.all_to_all(block.reshape(32, rows // 32, width), "band", 0, 0, tiled=True)
    return out.reshape(rows, width)


def arranged(table):
    return table.reshape(32, 32, 4, 8, 4).transpose(3, 1, 2, 4, 0).reshape(1024, 128)


def per_device(voltages, chirp_phase):
    block = voltages[0, 0]
    band = lax.axis_index("band")
    history = passed_along(block[..., 3072 - HIST:], "seg", 1)

    i32 = jnp.int32
    lane = jnp.arange(1024, dtype=i32)[None, :]
    r_lane = 32 * band + lane % 32
    ka_lane = lane // 32
    t2c, t2s = unit(jnp.arange(32, dtype=i32)[None, :] * (32 * band + jnp.arange(32, dtype=i32)[:, None]), LENGTH, -1)
    q = jnp.arange(8, dtype=i32)[:, None]
    dd = jnp.arange(32, dtype=i32)[:, None]
    pac, pas = unit(32 * r_lane * (q % 4), LENGTH, -1)
    pbc, pbs = unit(128 * r_lane * dd, LENGTH, -1)
    kc_lane = 128 * band + ka_lane
    rl_lane = lane % 32
    rows = jnp.arange(256, dtype=i32)[:, None]

    back_c, back_s = unit((32 * (rows // 8) + lane % 32) * (kc_lane + 32 * (rows % 4)), LENGTH, 1)
    back_c, back_s, history = lax.optimization_barrier((back_c, back_s, history))

    post_c, post_s = cmul(pac[None], pas[None], pbc[:, None], pbs[:, None])
    post_c, post_s = post_c.reshape(256, 1024), post_s.reshape(256, 1024)
    t1c, t1s = lane_twiddle(-1, 128)
    lr, li = send_matrices()
    (send,) = call(column_forward_kernel, [(256, 2048)], [(1024, 512)],
                   block, history, jnp.asarray(t1c), jnp.asarray(t1s), t2c, t2s,
                   *halves(lr), *halves(li), post_c, post_s, pbc, pbs)
    received = exchanged(send)

    chirp_phase, send = lax.optimization_barrier((chirp_phase, send))
    phases = gathered(chirp_phase, "seg", 1)[0]
    ch_c, ch_s = arranged(jnp.cos(phases)), arranged(jnp.sin(phases))

    twc, tws = row_twiddle(-1)
    (sent,) = call(row_kernel, [(256, 2048)], [(1024, 256), (1024, 256)],
                   received, jnp.asarray(twc), jnp.asarray(tws), *halves(row_block(-1)),
                   *halves(row_block(1)), ch_c, ch_s, back_c, back_s)
    returned = exchanged(sent)

    cc, cs = lane_twiddle(1, 256)
    (out,) = call(column_inverse_kernel, [(2, 2, ROWS_DEV, 3072)], [(1024, 512)],
                  returned, *halves(receive_matrix()), jnp.asarray(cc), jnp.asarray(cs))
    return out[None, None]


def solution(mesh):
    in_specs = (P("seg", None, None, None, "band", None), P(None, "seg", "band"))
    out_specs = P("seg", None, None, None, "band", None)
    return jax.shard_map(
        per_device, mesh=mesh, in_specs=in_specs, out_specs=out_specs, check_vma=False
    )
```
